128 devices in a mesh: req: 8 (over z, core), wide: 16 (over y, x).
Axes of the slice: x: 4, y: 4, z: 4, core: 2. Of those that a mesh axis runs over, the one named last changes fastest.
Arguments:
- hidden_in: bfloat16 [16384, 2048], P(('req', 'wide')), may hold values from -6 to 6
- queries: bfloat16 [16384, 3072], P(('req', 'wide')), may hold values from -104 to 104
- latent_weight: bfloat16 [2048, 576], replicated, may hold values from -0.125 to 0.125
- latent_gain: float32 [512], replicated, may hold values from 0.25 to 1.75
- key_up: bfloat16 [512, 2048], replicated, may hold values from -0.25 to 0.25
- value_up: bfloat16 [512, 2048], replicated, may hold values from -2 to 2
- out_weight: bfloat16 [2048, 2048], replicated, may hold values from -0.5 to 0.5
- ffn_gain: float32 [2048], replicated, may hold values from 0.25 to 1.75
- router_weight: bfloat16 [2048, 64], replicated, may hold values from -0.046875 to 0.046875
- gate_pieces: bfloat16 [128, 2048, 704], P(('req', 'wide')), may hold values from -0.125 to 0.125
- up_pieces: bfloat16 [128, 2048, 704], P(('req', 'wide')), may hold values from -0.125 to 0.125
- down_pieces: bfloat16 [128, 704, 2048], P(('req', 'wide')), may hold values from -0.625 to 0.625
- prefix_latent: bfloat16 [8, 128, 512], P('req'), may hold values from -6 to 6
- prefix_rope: bfloat16 [8, 128, 64], P('req'), may hold values from -6 to 6
- page_table: int32 [8], replicated, may hold values from 0 to 7, each once
- segment_ids: int32 [8, 2048], P('req', 'wide'), may hold values from 0 to 7, never falling along the last dimension, each value on 1 to 1024 neighbouring positions
- expert_ids: int32 [16384, 6], P(('req', 'wide')), may hold values from 0 to 63, all different within a row; in each aligned block of 128 rows (0 to 127, 128 to 255, ...) at most 14 rows name the same one
Outputs:
- hidden_out: bfloat16 [16384, 2048], P(('req', 'wide'))
- suffix_cache: bfloat16 [16384, 576], P(('req', 'wide'))
The draws below stay inside these ranges and needn't reach their ends.
Inputs may be any that keep to these rules, and one draw needn't show every extreme that they name: `segment_ids`: request numbers never fall along a row; each request holds 1 to 1024 tokens and one holds exactly 1024. `expert_ids`: A token names 6 different experts; among the 128 tokens of one device no expert is named more than 14 times, and that many is reached.
All inputs are finite; a program needn't handle non-finite values.
Results may differ from the reference program's by a relative error of at most 0.015.
Values may be sent and summed in bfloat16 or wider, within the bound.
No kernel may reach another device: no remote copies, remote signals or barrier semaphores. Data moves between devices by JAX's collectives and lax.ppermute only.
A program may use at most 192 MiB of HBM per device.

```python
import math
import jax
import jax.numpy as jnp
import numpy as np
from jax import lax

D = 2048
HEADS = 16
NOPE = 128
ROPE = 64
LAT = 512
EXPERTS = 64
FF = 1408
TOPK = 6
SPLIT = 2
PAGE = 128
ROWS_DEV = 128
REQS_GROUP = 8
HALF = 704
PREFIX_PAGES = 8
GROUP_ROWS = 2048
TOKENS = 16384
MOST_LEN = 1024
CAP = 14
N_REQ = 8
N_WIDE = 16


def draw_queries(key, part):
    first = jax.random.fold_in(key, 0)
    shape = (TOKENS, HEADS * (NOPE + ROPE))
    return jnp.clip(jax.random.normal(first, shape, jnp.float32), -5.0, 5.0).astype(jnp.bfloat16)


def block_scale(key, shape, cuts, least, largest):
    loudness, own = 1.0, jax.random.fold_in(key, 6)
    for axis_at, shards_of in cuts:
        steps = jnp.exp(jax.random.uniform(jax.random.fold_in(own, axis_at), (shards_of,), jnp.float32, least / len(cuts), largest / len(cuts)))
        loudness = loudness * jnp.repeat(steps, shape[axis_at] // shards_of).reshape([-1 if axis == axis_at else 1 for axis in range(len(shape))])
    return loudness


def length_profile(number_of, total, reach, slope):
    portions = [(1 << 20) // math.isqrt(grade ** slope) + 1 for grade in range(2, number_of + 1)]
    spare, counts = total - reach - (number_of - 1), [1] * (number_of - 1)
    while spare > 0:
        free = [i for i in range(number_of - 1) if counts[i] < reach]
        pool, remaining = sum([portions[i] for i in free]), spare
        for i in free:
            extra = min(reach - counts[i], max(1, remaining * portions[i] // pool), spare)
            counts[i] = counts[i] + extra
            spare = spare - extra
    return np.array([reach] + counts)


def ragged_sizes(rng, amount, total, most, lean):
    if amount == 2:
        one = jax.random.randint(rng, (), max(1, total - most), min(most, total - 1) + 1)
        return jnp.stack([one, total - one])
    tallies = jnp.asarray(length_profile(amount, total, most, lean), jnp.int32)
    twos = (amount - 1) // 2
    donor, receiver = tallies[1:1 + 2 * twos:2], tallies[2:2 + 2 * twos:2]
    room = jnp.minimum(donor - 1, most - receiver)
    shifted = jax.random.randint(jax.random.fold_in(rng, 1), (twos,), 0, 1 << 20) % (room + 1)
    tallies = tallies.at[1:1 + 2 * twos:2].set(donor - shifted).at[2:2 + 2 * twos:2].set(receiver + shifted)
    return tallies[jax.random.permutation(jax.random.fold_in(rng, 2), amount)]


def routed_block(rng, own, number, rows, number_of, top, bound, lean):
    ranking = jax.random.permutation(rng, number_of)
    packed, common = portions_of(number_of, rows * top, bound, lean, True), portions_of(number_of, rows * top, bound, lean, False)
    places = jnp.arange(number_of)

    def named(lengths, turn):
        used = int((lengths > 0).sum())
        fixed = max(1, used // 4)
        passed = fixed + (places - fixed + turn * (used - fixed)) % max(1, number_of - fixed)
        return jnp.zeros((number_of,), jnp.int32).at[ranking[jnp.where(places < fixed, places, passed)]].set(jnp.asarray(lengths, jnp.int32))

    lengths = jnp.where(number % 4 == 0, named(packed, number // 4), named(common, number - number // 4 - 1))
    mixed = jax.random.permutation(jax.random.fold_in(own, 3), number_of)
    donor, taker = mixed[0:number_of // 2 * 2:2], mixed[1:number_of // 2 * 2:2]
    slack = jnp.minimum(lengths[donor] - 1, bound - lengths[taker]) // 2
    slack = jnp.where((donor == ranking[0]) | (taker == ranking[0]) | (lengths[taker] == 0), 0, jnp.maximum(slack, 0))
    passed = jax.random.randint(jax.random.fold_in(own, 4), (number_of // 2,), 0, 1 << 20) % (slack + 1)
    lengths = lengths.at[donor].add(-passed).at[taker].add(passed)
    members = jnp.searchsorted(jnp.cumsum(lengths), jnp.arange(rows * top), side="right").astype(jnp.int32)
    grid = members.reshape(top, rows).T
    grid = grid[jax.random.permutation(jax.random.fold_in(own, 1), rows)]
    turn = jax.random.randint(jax.random.fold_in(own, 2), (rows, 1), 0, top)
    return jnp.take_along_axis(grid, (jnp.arange(top)[None, :] + turn) % top, axis=1)


def portions_of(number_of, total, most, slope, full):
    portions = [(1 << 20) // math.isqrt(standing ** slope) + 1 for standing in range(1, number_of + 1)]
    largest = most if full else min(most, max(-(-total // number_of), total * portions[0] // sum(portions)))
    least = 1 if total - largest >= number_of - 1 else 0
    given, surplus = [largest] + [least] * (number_of - 1), total - largest - least * (number_of - 1)
    while surplus > 0:
        movable = [i for i in range(1, number_of) if given[i] < largest] or [i for i in range(1, number_of) if given[i] < most]
        mass, budget = sum([portions[i] for i in movable]), surplus
        for i in movable:
            more = min(most - given[i], max(1, budget * portions[i] // mass), surplus)
            given[i] = given[i] + more
            surplus = surplus - more
    return np.array(given)


def centred(own_key, extent, width, reach, cuts=(), kind=jnp.bfloat16):
    factor_of = block_scale(own_key, extent, cuts, -0.22, 0.18) if cuts else 1.0
    drawn = jax.random.normal(own_key, extent, jnp.float32) * width * factor_of
    return jnp.minimum(jnp.maximum(drawn, -reach), reach).astype(kind)


def setup_inputs(seed: int = 0) -> dict:
    keys = jax.random.split(jax.random.key(seed), 18)
    hidden_in = centred(keys[0], (TOKENS, D), 1.0, 6.0, ((0, 128),))
    queries = draw_queries(jax.random.fold_in(keys[17], 71), 0)
    latent_weight = centred(keys[2], (D, LAT + ROPE), D ** -0.5, 0.125)
    latent_gain = jnp.clip(1.0 + 0.15 * jax.random.normal(keys[3], (LAT,), jnp.float32), 0.25, 1.75)
    key_up = centred(keys[4], (LAT, HEADS * NOPE), LAT ** -0.5, 0.25)
    value_up = centred(keys[5], (LAT, HEADS * NOPE), (max(LAT // 64, 1)) ** -0.5, 2.0)
    out_weight = centred(keys[6], (HEADS * NOPE, D), (max(HEADS * NOPE // 16, 1)) ** -0.5, 0.5)
    ffn_gain = jnp.clip(1.0 + 0.15 * jax.random.normal(keys[7], (D,), jnp.float32), 0.25, 1.75)
    router_weight = centred(keys[8], (D, EXPERTS), (8 * D) ** -0.5, 0.046875)
    gate_pieces = centred(keys[9], (EXPERTS * SPLIT, D, HALF), D ** -0.5, 0.125, ((0, 128),))
    up_pieces = centred(keys[10], (EXPERTS * SPLIT, D, HALF), D ** -0.5, 0.125, ((0, 128),))
    down_pieces = centred(keys[11], (EXPERTS * SPLIT, HALF, D), (max(FF // 16, 1)) ** -0.5, 0.625, ((0, 128),))
    prefix_latent = centred(keys[12], (PREFIX_PAGES, PAGE, LAT), 1.0, 6.0, ((0, 8),))
    prefix_rope = centred(keys[13], (PREFIX_PAGES, PAGE, ROPE), 1.0, 6.0, ((0, 8),))
    page_table = jax.random.permutation(keys[14], PREFIX_PAGES).astype(jnp.int32)
    segment_ids = jax.vmap(lambda own: jnp.searchsorted(jnp.cumsum(ragged_sizes(own, REQS_GROUP, GROUP_ROWS, MOST_LEN, 2)), jnp.arange(GROUP_ROWS), side="right"))(jax.random.split(keys[15], N_REQ)).reshape((N_REQ, GROUP_ROWS)).astype(jnp.int32)
    expert_ids_keys = jax.random.split(jax.random.fold_in(keys[16], 1), TOKENS // ROWS_DEV)
    expert_ids_turns = jax.random.permutation(jax.random.fold_in(keys[16], 3), TOKENS // ROWS_DEV)
    expert_ids = jax.vmap(lambda own, number: routed_block(jax.random.fold_in(keys[16], 2), own, number, ROWS_DEV, EXPERTS, TOPK, CAP, 1))(expert_ids_keys, expert_ids_turns).reshape((TOKENS, TOPK))
    return {"hidden_in": hidden_in, "queries": queries, "latent_weight": latent_weight, "latent_gain": latent_gain, "key_up": key_up, "value_up": value_up, "out_weight": out_weight, "ffn_gain": ffn_gain, "router_weight": router_weight, "gate_pieces": gate_pieces, "up_pieces": up_pieces, "down_pieces": down_pieces, "prefix_latent": prefix_latent, "prefix_rope": prefix_rope, "page_table": page_table, "segment_ids": segment_ids, "expert_ids": expert_ids}


EPS = 1e-06
NEG = -1e+30

def round_bf(values):
    return lax.optimization_barrier(values.astype(jnp.bfloat16)).astype(jnp.float32)

def rotary(values, positions):
    half = values.shape[-1] // 2
    freqs = 10000.0 ** (-2.0 * jnp.arange(half, dtype=jnp.float32) / values.shape[-1])
    angles = positions.astype(jnp.float32)[:, None] * freqs[None, :]
    shape = (positions.shape[0],) + (1,) * (values.ndim - 2) + (half,)
    cosine = jnp.cos(angles).reshape(shape)
    sine = jnp.sin(angles).reshape(shape)
    first = values[..., :half]
    second = values[..., half:]
    return jnp.concatenate([first * cosine - second * sine, second * cosine + first * sine], axis=-1)

def rms_scale(values, gain):
    return values * lax.rsqrt(lax.optimization_barrier(jnp.mean(values * values, axis=-1, keepdims=True)) + EPS) * gain

def offsets(segments):
    length = segments.shape[0]
    index = jnp.arange(length, dtype=jnp.int32)
    fresh = jnp.concatenate([jnp.ones((1,), dtype=bool), segments[1:] != segments[:-1]])
    starts = lax.cummax(jnp.where(fresh, index, 0), axis=0)
    return index - starts

def page_positions(page_table, slots):
    logical = lax.optimization_barrier(jnp.sum(jnp.where(page_table[None, :] == slots[:, None], jnp.arange(page_table.shape[0], dtype=jnp.int32)[None, :], 0), axis=1))
    return (logical[:, None] * PAGE + jnp.arange(PAGE, dtype=jnp.int32)[None, :]).reshape(-1)

def reference(hidden_in, queries, latent_weight, latent_gain, key_up, value_up, out_weight, ffn_gain, router_weight, gate_pieces, up_pieces, down_pieces, prefix_latent, prefix_rope, page_table, segment_ids, expert_ids):
    devices = N_REQ * N_WIDE
    prefix_len = PREFIX_PAGES * PAGE
    raw = jnp.dot(hidden_in, latent_weight, preferred_element_type=jnp.float32)
    latent = rms_scale(raw[:, :LAT], latent_gain).astype(jnp.bfloat16)
    key_rope = raw[:, LAT:].astype(jnp.bfloat16)
    suffix_cache = jnp.concatenate([latent, key_rope], axis=1)
    position = (prefix_len + jax.vmap(offsets)(segment_ids)).reshape(-1).astype(jnp.int32)
    suffix_rot = rotary(key_rope.astype(jnp.float32), position).astype(jnp.bfloat16)
    prefix_pos = page_positions(page_table, jnp.arange(PREFIX_PAGES, dtype=jnp.int32))
    prefix_rot = rotary(prefix_rope.reshape(-1, ROPE).astype(jnp.float32), prefix_pos).astype(jnp.bfloat16)
    prefix_lat = prefix_latent.reshape(-1, LAT)
    key_up3 = key_up.reshape(LAT, HEADS, NOPE).astype(jnp.float32)
    value_up3 = value_up.reshape(LAT, HEADS, NOPE).astype(jnp.float32)
    scale = 1.0 / math.sqrt(NOPE + ROPE)

    def attend(block):
        group = block // N_WIDE
        first = block * ROWS_DEV
        rows_q = lax.dynamic_slice_in_dim(queries, first, ROWS_DEV, 0).reshape(ROWS_DEV, HEADS, NOPE + ROPE)
        pos_q = lax.dynamic_slice_in_dim(position, first, ROWS_DEV, 0)
        q_lat = round_bf(jnp.einsum('thn,lhn->thl', rows_q[..., :NOPE].astype(jnp.float32), key_up3))
        q_rot = round_bf(rotary(rows_q[..., NOPE:].astype(jnp.float32), pos_q))
        group_start = group * GROUP_ROWS
        group_lat = lax.dynamic_slice_in_dim(latent, group_start, GROUP_ROWS, 0)
        group_rot = lax.dynamic_slice_in_dim(suffix_rot, group_start, GROUP_ROWS, 0)
        group_seg = lax.dynamic_index_in_dim(segment_ids, group, 0, keepdims=False)
        local = block % N_WIDE * ROWS_DEV
        seg_q = lax.dynamic_slice_in_dim(group_seg, local, ROWS_DEV, 0)
        index_q = local + jnp.arange(ROWS_DEV, dtype=jnp.int32)
        index_k = jnp.arange(GROUP_ROWS, dtype=jnp.int32)
        allowed = (seg_q[:, None] == group_seg[None, :]) & (index_k[None, :] <= index_q[:, None])
        allowed = jnp.concatenate([jnp.ones((ROWS_DEV, prefix_len), dtype=bool), allowed], axis=1)
        keys_lat = jnp.concatenate([prefix_lat, group_lat], axis=0).astype(jnp.float32)
        keys_rot = jnp.concatenate([prefix_rot, group_rot], axis=0).astype(jnp.float32)
        scores = (jnp.einsum('thl,kl->thk', q_lat, keys_lat) + jnp.einsum('the,ke->thk', q_rot, keys_rot)) * scale
        scores = jnp.where(allowed[:, None, :], scores, NEG)
        top = lax.optimization_barrier(jnp.max(scores, axis=-1, keepdims=True))
        weights = jnp.exp(scores - top)
        total = lax.optimization_barrier(jnp.sum(weights, axis=-1))
        mixed = round_bf(jnp.einsum('thk,kl->thl', round_bf(weights), keys_lat) / total[..., None])
        head_out = jnp.einsum('thl,lhn->thn', mixed, value_up3).astype(jnp.bfloat16).reshape(ROWS_DEV, HEADS * NOPE)
        rows_x = lax.dynamic_slice_in_dim(hidden_in, first, ROWS_DEV, 0)
        return rows_x.astype(jnp.float32) + jnp.dot(head_out, out_weight, preferred_element_type=jnp.float32)
    residual = lax.map(attend, jnp.arange(devices, dtype=jnp.int32)).reshape(-1, D)
    normed = rms_scale(residual, ffn_gain).astype(jnp.bfloat16)
    logits = jnp.dot(normed, router_weight, preferred_element_type=jnp.float32)
    chosen = jnp.take_along_axis(logits, expert_ids, axis=1)
    gates = jax.nn.softmax(chosen, axis=-1)
    pair_ids = expert_ids.reshape(devices, ROWS_DEV * TOPK)
    hits = (pair_ids[..., None] == jnp.arange(EXPERTS, dtype=jnp.int32)).astype(jnp.int32)
    slot = lax.optimization_barrier(jnp.sum((jnp.cumsum(hits, axis=1) - hits) * hits, axis=-1)).astype(jnp.int32)
    owner = jnp.broadcast_to(jnp.arange(devices, dtype=jnp.int32)[:, None], pair_ids.shape)
    token = owner * ROWS_DEV + jnp.arange(ROWS_DEV * TOPK, dtype=jnp.int32)[None, :] // TOPK
    table = jnp.full((EXPERTS, devices, CAP), TOKENS, dtype=jnp.int32).at[pair_ids, owner, slot].set(token)
    padded = jnp.concatenate([normed, jnp.zeros((1, D), jnp.bfloat16)], axis=0)

    def expert(index):
        rows_in = padded[table[index].reshape(-1)]
        summed = jnp.zeros((devices * CAP, D), jnp.float32)
        for half in range(SPLIT):
            piece = index * SPLIT + half
            gate = jnp.dot(rows_in, gate_pieces[piece], preferred_element_type=jnp.float32)
            upper = jnp.dot(rows_in, up_pieces[piece], preferred_element_type=jnp.float32)
            active = (jax.nn.silu(gate) * upper).astype(jnp.bfloat16)
            summed = summed + round_bf(jnp.dot(active, down_pieces[piece], preferred_element_type=jnp.float32))
        return summed
    combined = lax.map(expert, jnp.arange(EXPERTS, dtype=jnp.int32)).reshape(-1, D)
    flat_index = (pair_ids * (devices * CAP) + owner * CAP + slot).reshape(TOKENS, TOPK)
    routed = jnp.zeros((TOKENS, D), jnp.float32)
    for choice_k in range(TOPK):
        routed = routed + gates[:, choice_k:choice_k + 1] * combined[flat_index[:, choice_k]]
    hidden_out = (residual + routed).astype(jnp.bfloat16)
    return (hidden_out, suffix_cache)
```

```python
import functools
import math

import jax
import jax.numpy as jnp
from jax import lax
from jax.experimental import pallas as pl
from jax.experimental.pallas import tpu as pltpu
from jax.sharding import PartitionSpec as P

D = 2048
HEADS = 16
NOPE = 128
ROPE = 64
LAT = 512
EXPERTS = 64
TOPK = 6
SPLIT = 2
PAGE = 128
CAP = 14
MOST_LEN = 1024


EPS = 1e-06
NEG = -1e30


def rotary(values, positions):
    half = values.shape[-1] // 2
    freqs = 10000.0 ** (-2.0 * jnp.arange(half, dtype=jnp.float32) / values.shape[-1])
    angles = positions.astype(jnp.float32)[:, None] * freqs[None, :]
    shape = (positions.shape[0],) + (1,) * (values.ndim - 2) + (half,)
    cosine = jnp.cos(angles).reshape(shape)
    sine = jnp.sin(angles).reshape(shape)
    first = values[..., :half]
    second = values[..., half:]
    return jnp.concatenate(
        [first * cosine - second * sine, second * cosine + first * sine], axis=-1
    )


def rms_scale(values, gain):
    return values * lax.rsqrt(jnp.mean(values * values, axis=-1, keepdims=True) + EPS) * gain


def offsets(segments):
    length = segments.shape[0]
    index = jnp.arange(length, dtype=jnp.int32)
    fresh = jnp.concatenate([jnp.ones((1,), dtype=bool), segments[1:] != segments[:-1]])
    starts = lax.cummax(jnp.where(fresh, index, 0), axis=0)
    return index - starts


def page_positions(page_table, slots):
    logical = jnp.sum(
        jnp.where(
            page_table[None, :] == slots[:, None],
            jnp.arange(page_table.shape[0], dtype=jnp.int32)[None, :],
            0,
        ),
        axis=1,
    )
    return (logical[:, None] * PAGE + jnp.arange(PAGE, dtype=jnp.int32)[None, :]).reshape(-1)


def attend_kernel(base_ref, q_ref, kp_ref, ks_ref, lo_ref, hi_ref, out_ref, *, window, scale):
    base = pl.multiple_of(base_ref[0], 128)
    q = q_ref[...]
    kp = kp_ref[...]
    ks = ks_ref[pl.ds(base, window), :]
    dims = (((1,), (1,)), ((), ()))
    s_p = lax.dot_general(q, kp, dims, preferred_element_type=jnp.float32) * scale
    s_s = lax.dot_general(q, ks, dims, preferred_element_type=jnp.float32) * scale
    kidx = base + lax.broadcasted_iota(jnp.int32, (1, window), 1)
    allowed = (kidx >= lo_ref[...]) & (kidx <= hi_ref[...])
    s_s = jnp.where(allowed, s_s, NEG)
    top = jnp.maximum(jnp.max(s_p, axis=1, keepdims=True), jnp.max(s_s, axis=1, keepdims=True))
    w_p = jnp.exp(s_p - top)
    w_s = jnp.exp(s_s - top)
    total = jnp.sum(w_p, axis=1, keepdims=True) + jnp.sum(w_s, axis=1, keepdims=True)
    accum = jnp.dot(w_p.astype(jnp.bfloat16), kp, preferred_element_type=jnp.float32) + jnp.dot(
        w_s.astype(jnp.bfloat16), ks, preferred_element_type=jnp.float32
    )
    lat = out_ref.shape[1]
    out_ref[...] = (accum[:, :lat] / total).astype(out_ref.dtype)


def attend(base, q, kp, ks, lo, hi, window, block=256):
    rows, width = q.shape
    return pl.pallas_call(
        functools.partial(attend_kernel, window=window, scale=1.0 / math.sqrt(NOPE + ROPE)),
        grid_spec=pltpu.PrefetchScalarGridSpec(
            num_scalar_prefetch=1,
            grid=(rows // block,),
            in_specs=[
                pl.BlockSpec((block, width), lambda i, b: (i, 0)),
                pl.BlockSpec(kp.shape, lambda i, b: (0, 0)),
                pl.BlockSpec(ks.shape, lambda i, b: (0, 0)),
                pl.BlockSpec((block, 1), lambda i, b: (i, 0)),
                pl.BlockSpec((block, 1), lambda i, b: (i, 0)),
            ],
            out_specs=pl.BlockSpec((block, LAT), lambda i, b: (i, 0)),
        ),
        out_shape=jax.ShapeDtypeStruct((rows, LAT), jnp.bfloat16),
    )(base, q, kp, ks, lo, hi)


def expert_rows(received, gate_pieces, up_pieces, down_pieces):
    owned = gate_pieces.shape[0]
    grid = received.reshape(-1, owned, received.shape[1], received.shape[2])
    gate = jnp.einsum("spkd,pdf->spkf", grid, gate_pieces, preferred_element_type=jnp.float32)
    upper = jnp.einsum("spkd,pdf->spkf", grid, up_pieces, preferred_element_type=jnp.float32)
    active = (jax.nn.silu(gate) * upper).astype(jnp.bfloat16)
    output = jnp.einsum(
        "spkf,pfd->spkd", active, down_pieces, preferred_element_type=jnp.float32
    ).astype(jnp.bfloat16)
    return output.reshape(received.shape)


def on_device(
    hidden_in,
    queries,
    latent_weight,
    latent_gain,
    key_up,
    value_up,
    out_weight,
    ffn_gain,
    router_weight,
    gate_pieces,
    up_pieces,
    down_pieces,
    prefix_latent,
    prefix_rope,
    page_table,
    segment_ids,
    expert_ids,
):
    rows = hidden_in.shape[0]
    n_wide = lax.axis_size("wide")
    wide_at = lax.axis_index("wide")
    my_start = wide_at * rows
    prefix_len = prefix_latent.shape[0] * lax.axis_size("req") * PAGE
    slots = lax.axis_index("req") * prefix_latent.shape[0] + jnp.arange(
        prefix_latent.shape[0], dtype=jnp.int32
    )
    key_pos = page_positions(page_table, slots)
    own_rot = rotary(prefix_rope.reshape(-1, ROPE).astype(jnp.float32), key_pos).astype(jnp.bfloat16)
    own_keys = jnp.concatenate([prefix_latent.reshape(-1, LAT), own_rot], axis=1)
    page_keys = lax.all_gather(own_keys, "req", axis=0, tiled=True)
    group_seg = lax.all_gather(segment_ids, "wide", axis=1, tiled=True)[0]
    index_q = my_start + jnp.arange(rows, dtype=jnp.int32)
    offs = lax.dynamic_slice_in_dim(offsets(group_seg), my_start, rows, 0)
    position = prefix_len + offs
    raw = jnp.dot(hidden_in, latent_weight, preferred_element_type=jnp.float32)
    latent = rms_scale(raw[:, :LAT], latent_gain).astype(jnp.bfloat16)
    key_rope = raw[:, LAT:].astype(jnp.bfloat16)
    suffix_cache = jnp.concatenate([latent, key_rope], axis=1)
    suffix_rot = rotary(key_rope.astype(jnp.float32), position).astype(jnp.bfloat16)
    group_keys = lax.all_gather(
        jnp.concatenate([latent, suffix_rot], axis=1), "wide", axis=0, tiled=True
    )
    split_q = queries.reshape(rows, HEADS, NOPE + ROPE)
    q_lat = jnp.einsum(
        "thn,lhn->thl",
        split_q[..., :NOPE],
        key_up.reshape(LAT, HEADS, NOPE),
        preferred_element_type=jnp.float32,
    ).astype(jnp.bfloat16)
    q_rot = rotary(split_q[..., NOPE:].astype(jnp.float32), position).astype(jnp.bfloat16)
    q_all = jnp.concatenate([q_lat, q_rot], axis=2).reshape(rows * HEADS, LAT + ROPE)
    reach = -(-(MOST_LEN - 1) // rows) + 1
    blocks = min(n_wide, reach)
    base = (jnp.maximum(wide_at - (blocks - 1), 0) * rows).astype(jnp.int32).reshape(1)
    lo = jnp.repeat((index_q - offs)[:, None], HEADS, axis=0)
    hi = jnp.repeat(index_q[:, None], HEADS, axis=0)
    mixed = attend(base, q_all, page_keys, group_keys, lo, hi, blocks * rows).reshape(
        rows, HEADS, LAT
    )
    head_out = (
        jnp.einsum(
            "thl,lhn->thn",
            mixed,
            value_up.reshape(LAT, HEADS, NOPE),
            preferred_element_type=jnp.float32,
        )
        .astype(jnp.bfloat16)
        .reshape(rows, HEADS * NOPE)
    )
    residual = hidden_in.astype(jnp.float32) + jnp.dot(
        head_out, out_weight, preferred_element_type=jnp.float32
    )
    normed = rms_scale(residual, ffn_gain).astype(jnp.bfloat16)
    logits = jnp.dot(normed, router_weight, preferred_element_type=jnp.float32)
    hits = expert_ids[..., None] == jnp.arange(EXPERTS, dtype=jnp.int32)
    chosen = jnp.sum(jnp.where(hits, logits[:, None, :], 0.0), axis=-1)
    gates = jax.nn.softmax(chosen, axis=-1)
    flat_hits = hits.reshape(rows * TOPK, EXPERTS).astype(jnp.int32)
    slot = jnp.sum((jnp.cumsum(flat_hits, axis=0) - flat_hits) * flat_hits, axis=-1).reshape(
        rows, TOPK
    )
    column = jnp.arange(EXPERTS * SPLIT * CAP, dtype=jnp.int32)
    first = expert_ids * (SPLIT * CAP) + slot
    match = jnp.zeros((EXPERTS * SPLIT * CAP, rows, TOPK), dtype=bool)
    for half in range(SPLIT):
        match = match | ((first + half * CAP)[None, :, :] == column[:, None, None])
    selector = jnp.any(match, axis=-1).astype(jnp.bfloat16)
    outgoing = (
        jnp.dot(selector, normed, preferred_element_type=jnp.float32)
        .astype(jnp.bfloat16)
        .reshape(EXPERTS * SPLIT, CAP, D)
    )
    worked = expert_rows(
        lax.all_to_all(outgoing, ("req", "wide"), split_axis=0, concat_axis=0, tiled=True),
        gate_pieces,
        up_pieces,
        down_pieces,
    )
    returned = lax.all_to_all(worked, ("req", "wide"), split_axis=0, concat_axis=0, tiled=True)
    weight = jnp.sum(jnp.where(match.transpose(1, 0, 2), gates[:, None, :], 0.0), axis=-1)
    weight_hi = weight.astype(jnp.bfloat16)
    weight_lo = (weight - weight_hi.astype(jnp.float32)).astype(jnp.bfloat16)
    flat = returned.reshape(EXPERTS * SPLIT * CAP, D)
    routed = jnp.dot(weight_hi, flat, preferred_element_type=jnp.float32) + jnp.dot(
        weight_lo, flat, preferred_element_type=jnp.float32
    )
    return ((residual + routed).astype(jnp.bfloat16), suffix_cache)


def solution(mesh):
    return jax.shard_map(
        on_device,
        mesh=mesh,
        in_specs=(
            P(("req", "wide"), None),
            P(("req", "wide"), None),
            P(),
            P(),
            P(),
            P(),
            P(),
            P(),
            P(),
            P(("req", "wide"), None, None),
            P(("req", "wide"), None, None),
            P(("req", "wide"), None, None),
            P("req", None, None),
            P("req", None, None),
            P(),
            P("req", "wide"),
            P(("req", "wide"), None),
        ),
        out_specs=(P(("req", "wide"), None), P(("req", "wide"), None)),
        check_vma=False,
    )
```

```python
import functools
import math

import jax
import jax.numpy as jnp
from jax import lax
from jax.experimental import pallas as pl
from jax.experimental.pallas import tpu as pltpu
from jax.sharding import PartitionSpec as P

D = 2048
HEADS = 16
NOPE = 128
ROPE = 64
LAT = 512
EXPERTS = 64
TOPK = 6
SPLIT = 2
PAGE = 128
CAP = 14
MOST_LEN = 1024


EPS = 1e-06
NEG = -1e30


def rotary(values, positions):
    half = values.shape[-1] // 2
    freqs = 10000.0 ** (-2.0 * jnp.arange(half, dtype=jnp.float32) / values.shape[-1])
    angles = positions.astype(jnp.float32)[:, None] * freqs[None, :]
    shape = (positions.shape[0],) + (1,) * (values.ndim - 2) + (half,)
    cosine = jnp.cos(angles).reshape(shape)
    sine = jnp.sin(angles).reshape(shape)
    first = values[..., :half]
    second = values[..., half:]
    return jnp.concatenate(
        [first * cosine - second * sine, second * cosine + first * sine], axis=-1
    )


def rms_scale(values, gain):
    return values * lax.rsqrt(jnp.mean(values * values, axis=-1, keepdims=True) + EPS) * gain


def offsets(segments):
    length = segments.shape[0]
    index = jnp.arange(length, dtype=jnp.int32)
    fresh = jnp.concatenate([jnp.ones((1,), dtype=bool), segments[1:] != segments[:-1]])
    starts = lax.cummax(jnp.where(fresh, index, 0), axis=0)
    return index - starts


def page_positions(page_table, slots):
    logical = jnp.sum(
        jnp.where(
            page_table[None, :] == slots[:, None],
            jnp.arange(page_table.shape[0], dtype=jnp.int32)[None, :],
            0,
        ),
        axis=1,
    )
    return (logical[:, None] * PAGE + jnp.arange(PAGE, dtype=jnp.int32)[None, :]).reshape(-1)


def attend_kernel(base_ref, q_ref, kp_ref, ks_ref, lo_ref, hi_ref, out_ref, *, window, scale):
    base = base_ref[0]
    q = q_ref[...]
    kp = kp_ref[...]
    ks = ks_ref[...]
    dims = (((1,), (1,)), ((), ()))
    s_p = lax.dot_general(q, kp, dims, preferred_element_type=jnp.float32) * scale
    s_s = lax.dot_general(q, ks, dims, preferred_element_type=jnp.float32) * scale
    kidx = base + lax.broadcasted_iota(jnp.int32, (1, window), 1)
    allowed = (kidx >= lo_ref[...]) & (kidx <= hi_ref[...])
    s_s = jnp.where(allowed, s_s, NEG)
    top = jnp.maximum(jnp.max(s_p, axis=1, keepdims=True), jnp.max(s_s, axis=1, keepdims=True))
    w_p = jnp.exp(s_p - top)
    w_s = jnp.exp(s_s - top)
    total = jnp.sum(w_p, axis=1, keepdims=True) + jnp.sum(w_s, axis=1, keepdims=True)
    accum = jnp.dot(w_p.astype(jnp.bfloat16), kp, preferred_element_type=jnp.float32) + jnp.dot(
        w_s.astype(jnp.bfloat16), ks, preferred_element_type=jnp.float32
    )
    lat = out_ref.shape[1]
    out_ref[...] = (accum[:, :lat] / total).astype(out_ref.dtype)


def attend(base, q, kp, ks, lo, hi, window, block=256):
    rows, width = q.shape
    return pl.pallas_call(
        functools.partial(attend_kernel, window=window, scale=1.0 / math.sqrt(NOPE + ROPE)),
        grid_spec=pltpu.PrefetchScalarGridSpec(
            num_scalar_prefetch=1,
            grid=(rows // block,),
            in_specs=[
                pl.BlockSpec((block, width), lambda i, b: (i, 0)),
                pl.BlockSpec(kp.shape, lambda i, b: (0, 0)),
                pl.BlockSpec(ks.shape, lambda i, b: (0, 0)),
                pl.BlockSpec((block, 1), lambda i, b: (i, 0)),
                pl.BlockSpec((block, 1), lambda i, b: (i, 0)),
            ],
            out_specs=pl.BlockSpec((block, LAT), lambda i, b: (i, 0)),
        ),
        out_shape=jax.ShapeDtypeStruct((rows, LAT), jnp.bfloat16),
    )(base, q, kp, ks, lo, hi)


def expert_rows(received, gate_pieces, up_pieces, down_pieces):
    owned = gate_pieces.shape[0]
    grid = received.reshape(-1, owned, received.shape[1], received.shape[2])
    gate = jnp.einsum("spkd,pdf->spkf", grid, gate_pieces, preferred_element_type=jnp.float32)
    upper = jnp.einsum("spkd,pdf->spkf", grid, up_pieces, preferred_element_type=jnp.float32)
    active = (jax.nn.silu(gate) * upper).astype(jnp.bfloat16)
    output = jnp.einsum(
        "spkf,pfd->spkd", active, down_pieces, preferred_element_type=jnp.float32
    ).astype(jnp.bfloat16)
    return output.reshape(received.shape)


def on_device(
    hidden_in,
    queries,
    latent_weight,
    latent_gain,
    key_up,
    value_up,
    out_weight,
    ffn_gain,
    router_weight,
    gate_pieces,
    up_pieces,
    down_pieces,
    prefix_latent,
    prefix_rope,
    page_table,
    segment_ids,
    expert_ids,
):
    rows = hidden_in.shape[0]
    n_wide = lax.axis_size("wide")
    wide_at = lax.axis_index("wide")
    my_start = wide_at * rows
    prefix_len = prefix_latent.shape[0] * lax.axis_size("req") * PAGE
    slots = lax.axis_index("req") * prefix_latent.shape[0] + jnp.arange(
        prefix_latent.shape[0], dtype=jnp.int32
    )
    key_pos = page_positions(page_table, slots)
    own_rot = rotary(prefix_rope.reshape(-1, ROPE).astype(jnp.float32), key_pos).astype(jnp.bfloat16)
    own_keys = jnp.concatenate([prefix_latent.reshape(-1, LAT), own_rot], axis=1)
    n_req = lax.axis_size("req")
    page_keys = jnp.concatenate(
        [own_keys]
        + [
            lax.ppermute(own_keys, "req", [(r, (r + k) % n_req) for r in range(n_req)])
            for k in range(1, n_req)
        ],
        axis=0,
    )
    group_seg = lax.all_gather(segment_ids, "wide", axis=1, tiled=True)[0]
    index_q = my_start + jnp.arange(rows, dtype=jnp.int32)
    offs = lax.dynamic_slice_in_dim(offsets(group_seg), my_start, rows, 0)
    position = prefix_len + offs
    raw = jnp.dot(hidden_in, latent_weight, preferred_element_type=jnp.float32)
    latent = rms_scale(raw[:, :LAT], latent_gain).astype(jnp.bfloat16)
    key_rope = raw[:, LAT:].astype(jnp.bfloat16)
    suffix_cache = jnp.concatenate([latent, key_rope], axis=1)
    suffix_rot = rotary(key_rope.astype(jnp.float32), position).astype(jnp.bfloat16)
    own_suffix = jnp.concatenate([latent, suffix_rot], axis=1)
    split_q = queries.reshape(rows, HEADS, NOPE + ROPE)
    q_lat = jnp.einsum(
        "thn,lhn->thl",
        split_q[..., :NOPE],
        key_up.reshape(LAT, HEADS, NOPE),
        preferred_element_type=jnp.float32,
    ).astype(jnp.bfloat16)
    q_rot = rotary(split_q[..., NOPE:].astype(jnp.float32), position).astype(jnp.bfloat16)
    q_all = jnp.concatenate([q_lat, q_rot], axis=2).reshape(rows * HEADS, LAT + ROPE)
    reach = -(-(MOST_LEN - 1) // rows) + 1
    blocks = min(n_wide, reach)
    base = ((wide_at - (blocks - 1)) * rows).astype(jnp.int32).reshape(1)
    group_keys = jnp.concatenate(
        [
            lax.ppermute(own_suffix, "wide", [(w, w + k) for w in range(n_wide - k)])
            for k in range(blocks - 1, 0, -1)
        ]
        + [own_suffix],
        axis=0,
    )
    lo = jnp.repeat((index_q - offs)[:, None], HEADS, axis=0)
    hi = jnp.repeat(index_q[:, None], HEADS, axis=0)
    mixed = attend(base, q_all, page_keys, group_keys, lo, hi, blocks * rows).reshape(
        rows, HEADS, LAT
    )
    head_out = (
        jnp.einsum(
            "thl,lhn->thn",
            mixed,
            value_up.reshape(LAT, HEADS, NOPE),
            preferred_element_type=jnp.float32,
        )
        .astype(jnp.bfloat16)
        .reshape(rows, HEADS * NOPE)
    )
    residual = hidden_in.astype(jnp.float32) + jnp.dot(
        head_out, out_weight, preferred_element_type=jnp.float32
    )
    normed = rms_scale(residual, ffn_gain).astype(jnp.bfloat16)
    logits = jnp.dot(normed, router_weight, preferred_element_type=jnp.float32)
    hits = expert_ids[..., None] == jnp.arange(EXPERTS, dtype=jnp.int32)
    chosen = jnp.sum(jnp.where(hits, logits[:, None, :], 0.0), axis=-1)
    gates = jax.nn.softmax(chosen, axis=-1)
    flat_hits = hits.reshape(rows * TOPK, EXPERTS).astype(jnp.int32)
    slot = jnp.sum((jnp.cumsum(flat_hits, axis=0) - flat_hits) * flat_hits, axis=-1).reshape(
        rows, TOPK
    )
    column = jnp.arange(EXPERTS * SPLIT * CAP, dtype=jnp.int32)
    first = expert_ids * (SPLIT * CAP) + slot
    match = jnp.zeros((EXPERTS * SPLIT * CAP, rows, TOPK), dtype=bool)
    for half in range(SPLIT):
        match = match | ((first + half * CAP)[None, :, :] == column[:, None, None])
    selector = jnp.any(match, axis=-1).astype(jnp.bfloat16)
    outgoing = (
        jnp.dot(selector, normed, preferred_element_type=jnp.float32)
        .astype(jnp.bfloat16)
        .reshape(EXPERTS * SPLIT, CAP, D)
    )
    worked = expert_rows(
        lax.all_to_all(outgoing, ("req", "wide"), split_axis=0, concat_axis=0, tiled=True),
        gate_pieces,
        up_pieces,
        down_pieces,
    )
    returned = lax.all_to_all(worked, ("req", "wide"), split_axis=0, concat_axis=0, tiled=True)
    weight = jnp.sum(jnp.where(match.transpose(1, 0, 2), gates[:, None, :], 0.0), axis=-1)
    weight_hi = weight.astype(jnp.bfloat16)
    weight_lo = (weight - weight_hi.astype(jnp.float32)).astype(jnp.bfloat16)
    flat = returned.reshape(EXPERTS * SPLIT * CAP, D)
    routed = jnp.dot(weight_hi, flat, preferred_element_type=jnp.float32) + jnp.dot(
        weight_lo, flat, preferred_element_type=jnp.float32
    )
    return ((residual + routed).astype(jnp.bfloat16), suffix_cache)


def solution(mesh):
    return jax.shard_map(
        on_device,
        mesh=mesh,
        in_specs=(
            P(("req", "wide"), None),
            P(("req", "wide"), None),
            P(),
            P(),
            P(),
            P(),
            P(),
            P(),
            P(),
            P(("req", "wide"), None, None),
            P(("req", "wide"), None, None),
            P(("req", "wide"), None, None),
            P("req", None, None),
            P("req", None, None),
            P(),
            P("req", "wide"),
            P(("req", "wide"), None),
        ),
        out_specs=(P(("req", "wide"), None), P(("req", "wide"), None)),
        check_vma=False,
    )
```

```python
import functools
import math

import jax
import jax.numpy as jnp
from jax import lax
from jax.experimental import pallas as pl
from jax.experimental.pallas import tpu as pltpu
from jax.sharding import PartitionSpec as P

D = 2048
HEADS = 16
NOPE = 128
ROPE = 64
LAT = 512
EXPERTS = 64
TOPK = 6
SPLIT = 2
PAGE = 128
CAP = 14
MOST_LEN = 1024


EPS = 1e-06
NEG = -1e30


def rotary(values, positions):
    half = values.shape[-1] // 2
    freqs = 10000.0 ** (-2.0 * jnp.arange(half, dtype=jnp.float32) / values.shape[-1])
    angles = positions.astype(jnp.float32)[:, None] * freqs[None, :]
    shape = (positions.shape[0],) + (1,) * (values.ndim - 2) + (half,)
    cosine = jnp.cos(angles).reshape(shape)
    sine = jnp.sin(angles).reshape(shape)
    first = values[..., :half]
    second = values[..., half:]
    return jnp.concatenate(
        [first * cosine - second * sine, second * cosine + first * sine], axis=-1
    )


def rms_scale(values, gain):
    return values * lax.rsqrt(jnp.mean(values * values, axis=-1, keepdims=True) + EPS) * gain


def offsets(segments):
    length = segments.shape[0]
    index = jnp.arange(length, dtype=jnp.int32)
    fresh = jnp.concatenate([jnp.ones((1,), dtype=bool), segments[1:] != segments[:-1]])
    starts = lax.cummax(jnp.where(fresh, index, 0), axis=0)
    return index - starts


def page_positions(page_table, slots):
    logical = jnp.sum(
        jnp.where(
            page_table[None, :] == slots[:, None],
            jnp.arange(page_table.shape[0], dtype=jnp.int32)[None, :],
            0,
        ),
        axis=1,
    )
    return (logical[:, None] * PAGE + jnp.arange(PAGE, dtype=jnp.int32)[None, :]).reshape(-1)


def attend_kernel(
    base_ref, ql_ref, qr_ref, kp_ref, kl_ref, kr_ref, lo_ref, hi_ref, out_ref, *, window, scale
):
    base = pl.multiple_of(base_ref[0], 128)
    lat = out_ref.shape[1]
    q = jnp.concatenate([ql_ref[...], qr_ref[...]], axis=1)
    kp = kp_ref[...]
    k_lat = kl_ref[pl.ds(base, window), :lat]
    k_rot = kr_ref[pl.ds(base, window), :]
    dims = (((1,), (1,)), ((), ()))
    s_p = lax.dot_general(q, kp, dims, preferred_element_type=jnp.float32) * scale
    s_s = (
        lax.dot_general(ql_ref[...], k_lat, dims, preferred_element_type=jnp.float32)
        + lax.dot_general(qr_ref[...], k_rot, dims, preferred_element_type=jnp.float32)
    ) * scale
    kidx = base + lax.broadcasted_iota(jnp.int32, (1, window), 1)
    allowed = (kidx >= lo_ref[...]) & (kidx <= hi_ref[...])
    s_s = jnp.where(allowed, s_s, NEG)
    top = jnp.maximum(jnp.max(s_p, axis=1, keepdims=True), jnp.max(s_s, axis=1, keepdims=True))
    w_p = jnp.exp(s_p - top)
    w_s = jnp.exp(s_s - top)
    total = jnp.sum(w_p, axis=1, keepdims=True) + jnp.sum(w_s, axis=1, keepdims=True)
    accum = jnp.dot(w_p.astype(jnp.bfloat16), kp, preferred_element_type=jnp.float32)[:, :lat] + jnp.dot(
        w_s.astype(jnp.bfloat16), k_lat, preferred_element_type=jnp.float32
    )
    out_ref[...] = (accum / total).astype(out_ref.dtype)


def attend(base, q_lat, q_rot, kp, k_lat, k_rot, lo, hi, window, block=256):
    rows = q_lat.shape[0]
    return pl.pallas_call(
        functools.partial(attend_kernel, window=window, scale=1.0 / math.sqrt(NOPE + ROPE)),
        grid_spec=pltpu.PrefetchScalarGridSpec(
            num_scalar_prefetch=1,
            grid=(rows // block,),
            in_specs=[
                pl.BlockSpec((block, LAT), lambda i, b: (i, 0)),
                pl.BlockSpec((block, ROPE), lambda i, b: (i, 0)),
                pl.BlockSpec(kp.shape, lambda i, b: (0, 0)),
                pl.BlockSpec(k_lat.shape, lambda i, b: (0, 0)),
                pl.BlockSpec(k_rot.shape, lambda i, b: (0, 0)),
                pl.BlockSpec((block, 1), lambda i, b: (i, 0)),
                pl.BlockSpec((block, 1), lambda i, b: (i, 0)),
            ],
            out_specs=pl.BlockSpec((block, LAT), lambda i, b: (i, 0)),
        ),
        out_shape=jax.ShapeDtypeStruct((rows, LAT), jnp.bfloat16),
    )(base, q_lat, q_rot, kp, k_lat, k_rot, lo, hi)


def expert_rows(received, gate_pieces, up_pieces, down_pieces):
    owned = gate_pieces.shape[0]
    grid = received.reshape(-1, owned, received.shape[1], received.shape[2])
    gate = jnp.einsum("spkd,pdf->spkf", grid, gate_pieces, preferred_element_type=jnp.float32)
    upper = jnp.einsum("spkd,pdf->spkf", grid, up_pieces, preferred_element_type=jnp.float32)
    active = (jax.nn.silu(gate) * upper).astype(jnp.bfloat16)
    output = jnp.einsum(
        "spkf,pfd->spkd", active, down_pieces, preferred_element_type=jnp.float32
    ).astype(jnp.bfloat16)
    return output.reshape(received.shape)


def on_device(
    hidden_in,
    queries,
    latent_weight,
    latent_gain,
    key_up,
    value_up,
    out_weight,
    ffn_gain,
    router_weight,
    gate_pieces,
    up_pieces,
    down_pieces,
    prefix_latent,
    prefix_rope,
    page_table,
    segment_ids,
    expert_ids,
):
    rows = hidden_in.shape[0]
    n_wide = lax.axis_size("wide")
    wide_at = lax.axis_index("wide")
    my_start = wide_at * rows
    prefix_len = prefix_latent.shape[0] * lax.axis_size("req") * PAGE
    slots = lax.axis_index("req") * prefix_latent.shape[0] + jnp.arange(
        prefix_latent.shape[0], dtype=jnp.int32
    )
    key_pos = page_positions(page_table, slots)
    own_rot = rotary(prefix_rope.reshape(-1, ROPE).astype(jnp.float32), key_pos).astype(jnp.bfloat16)
    own_keys = jnp.concatenate([prefix_latent.reshape(-1, LAT), own_rot], axis=1)
    page_keys = lax.all_gather(own_keys, "req", axis=0, tiled=True)
    raw = jnp.dot(hidden_in, latent_weight, preferred_element_type=jnp.float32)
    latent = rms_scale(raw[:, :LAT], latent_gain).astype(jnp.bfloat16)
    key_rope = raw[:, LAT:].astype(jnp.bfloat16)
    suffix_cache = jnp.concatenate([latent, key_rope], axis=1)
    tag = jnp.broadcast_to(segment_ids.reshape(rows, 1).astype(jnp.bfloat16), (rows, ROPE))
    group = lax.all_gather(
        jnp.concatenate([suffix_cache, tag], axis=1), "wide", axis=0, tiled=True
    )
    group_seg = group[:, LAT + ROPE].astype(jnp.int32)
    group_pos = prefix_len + offsets(group_seg)
    group_rot = rotary(group[:, LAT : LAT + ROPE].astype(jnp.float32), group_pos).astype(
        jnp.bfloat16
    )
    index_q = my_start + jnp.arange(rows, dtype=jnp.int32)
    position = lax.dynamic_slice_in_dim(group_pos, my_start, rows, 0)
    split_q = queries.reshape(rows, HEADS, NOPE + ROPE)
    q_lat = jnp.einsum(
        "thn,lhn->thl",
        split_q[..., :NOPE],
        key_up.reshape(LAT, HEADS, NOPE),
        preferred_element_type=jnp.float32,
    ).astype(jnp.bfloat16)
    q_rot = rotary(split_q[..., NOPE:].astype(jnp.float32), position).astype(jnp.bfloat16)
    reach = -(-(MOST_LEN - 1) // rows) + 1
    blocks = min(n_wide, reach)
    base = (jnp.maximum(wide_at - (blocks - 1), 0) * rows).astype(jnp.int32).reshape(1)
    lo = jnp.repeat((index_q - (position - prefix_len))[:, None], HEADS, axis=0)
    hi = jnp.repeat(index_q[:, None], HEADS, axis=0)
    mixed = attend(
        base,
        q_lat.reshape(rows * HEADS, LAT),
        q_rot.reshape(rows * HEADS, ROPE),
        page_keys,
        group,
        group_rot,
        lo,
        hi,
        blocks * rows,
    ).reshape(
        rows, HEADS, LAT
    )
    head_out = (
        jnp.einsum(
            "thl,lhn->thn",
            mixed,
            value_up.reshape(LAT, HEADS, NOPE),
            preferred_element_type=jnp.float32,
        )
        .astype(jnp.bfloat16)
        .reshape(rows, HEADS * NOPE)
    )
    residual = hidden_in.astype(jnp.float32) + jnp.dot(
        head_out, out_weight, preferred_element_type=jnp.float32
    )
    normed = rms_scale(residual, ffn_gain).astype(jnp.bfloat16)
    logits = jnp.dot(normed, router_weight, preferred_element_type=jnp.float32)
    hits = expert_ids[..., None] == jnp.arange(EXPERTS, dtype=jnp.int32)
    chosen = jnp.sum(jnp.where(hits, logits[:, None, :], 0.0), axis=-1)
    gates = jax.nn.softmax(chosen, axis=-1)
    flat_hits = hits.reshape(rows * TOPK, EXPERTS).astype(jnp.int32)
    slot = jnp.sum((jnp.cumsum(flat_hits, axis=0) - flat_hits) * flat_hits, axis=-1).reshape(
        rows, TOPK
    )
    column = jnp.arange(EXPERTS * SPLIT * CAP, dtype=jnp.int32)
    first = expert_ids * (SPLIT * CAP) + slot
    match = jnp.zeros((EXPERTS * SPLIT * CAP, rows, TOPK), dtype=bool)
    for half in range(SPLIT):
        match = match | ((first + half * CAP)[None, :, :] == column[:, None, None])
    selector = jnp.any(match, axis=-1).astype(jnp.bfloat16)
    outgoing = (
        jnp.dot(selector, normed, preferred_element_type=jnp.float32)
        .astype(jnp.bfloat16)
        .reshape(EXPERTS * SPLIT, CAP, D)
    )
    worked = expert_rows(
        lax.all_to_all(outgoing, ("req", "wide"), split_axis=0, concat_axis=0, tiled=True),
        gate_pieces,
        up_pieces,
        down_pieces,
    )
    returned = lax.all_to_all(worked, ("req", "wide"), split_axis=0, concat_axis=0, tiled=True)
    weight = jnp.sum(jnp.where(match.transpose(1, 0, 2), gates[:, None, :], 0.0), axis=-1)
    weight_hi = weight.astype(jnp.bfloat16)
    weight_lo = (weight - weight_hi.astype(jnp.float32)).astype(jnp.bfloat16)
    flat = returned.reshape(EXPERTS * SPLIT * CAP, D)
    routed = jnp.dot(weight_hi, flat, preferred_element_type=jnp.float32) + jnp.dot(
        weight_lo, flat, preferred_element_type=jnp.float32
    )
    return ((residual + routed).astype(jnp.bfloat16), suffix_cache)


def solution(mesh):
    return jax.shard_map(
        on_device,
        mesh=mesh,
        in_specs=(
            P(("req", "wide"), None),
            P(("req", "wide"), None),
            P(),
            P(),
            P(),
            P(),
            P(),
            P(),
            P(),
            P(("req", "wide"), None, None),
            P(("req", "wide"), None, None),
            P(("req", "wide"), None, None),
            P("req", None, None),
            P("req", None, None),
            P(),
            P("req", "wide"),
            P(("req", "wide"), None),
        ),
        out_specs=(P(("req", "wide"), None), P(("req", "wide"), None)),
        check_vma=False,
    )
```

```python
import functools
import math

import jax
import jax.numpy as jnp
from jax import lax
from jax.experimental import pallas as pl
from jax.experimental.pallas import tpu as pltpu
from jax.sharding import PartitionSpec as P

D = 2048
HEADS = 16
NOPE = 128
ROPE = 64
LAT = 512
EXPERTS = 64
TOPK = 6
SPLIT = 2
PAGE = 128
CAP = 14
MOST_LEN = 1024


EPS = 1e-06
NEG = -1e30


def rotary(values, positions):
    half = values.shape[-1] // 2
    freqs = 10000.0 ** (-2.0 * jnp.arange(half, dtype=jnp.float32) / values.shape[-1])
    angles = positions.astype(jnp.float32)[:, None] * freqs[None, :]
    shape = (positions.shape[0],) + (1,) * (values.ndim - 2) + (half,)
    cosine = jnp.cos(angles).reshape(shape)
    sine = jnp.sin(angles).reshape(shape)
    first = values[..., :half]
    second = values[..., half:]
    return jnp.concatenate(
        [first * cosine - second * sine, second * cosine + first * sine], axis=-1
    )


def rms_scale(values, gain):
    return values * lax.rsqrt(jnp.mean(values * values, axis=-1, keepdims=True) + EPS) * gain


def offsets(segments):
    length = segments.shape[0]
    index = jnp.arange(length, dtype=jnp.int32)
    fresh = jnp.concatenate([jnp.ones((1,), dtype=bool), segments[1:] != segments[:-1]])
    starts = lax.cummax(jnp.where(fresh, index, 0), axis=0)
    return index - starts


def page_positions(page_table, slots):
    logical = jnp.sum(
        jnp.where(
            page_table[None, :] == slots[:, None],
            jnp.arange(page_table.shape[0], dtype=jnp.int32)[None, :],
            0,
        ),
        axis=1,
    )
    return (logical[:, None] * PAGE + jnp.arange(PAGE, dtype=jnp.int32)[None, :]).reshape(-1)


def attend_kernel(
    base_ref, ql_ref, qr_ref, kp_ref, kl_ref, kr_ref, lo_ref, hi_ref, out_ref, *, window, scale
):
    base = pl.multiple_of(base_ref[0], 128)
    lat = out_ref.shape[1]
    q = jnp.concatenate([ql_ref[...], qr_ref[...]], axis=1)
    kp = kp_ref[...]
    k_lat = kl_ref[pl.ds(base, window), :lat]
    k_rot = kr_ref[pl.ds(base, window), :]
    dims = (((1,), (1,)), ((), ()))
    s_p = lax.dot_general(q, kp, dims, preferred_element_type=jnp.float32) * scale
    s_s = (
        lax.dot_general(ql_ref[...], k_lat, dims, preferred_element_type=jnp.float32)
        + lax.dot_general(qr_ref[...], k_rot, dims, preferred_element_type=jnp.float32)
    ) * scale
    kidx = base + lax.broadcasted_iota(jnp.int32, (1, window), 1)
    allowed = (kidx >= lo_ref[...]) & (kidx <= hi_ref[...])
    s_s = jnp.where(allowed, s_s, NEG)
    top = jnp.maximum(jnp.max(s_p, axis=1, keepdims=True), jnp.max(s_s, axis=1, keepdims=True))
    w_p = jnp.exp(s_p - top)
    w_s = jnp.exp(s_s - top)
    total = jnp.sum(w_p, axis=1, keepdims=True) + jnp.sum(w_s, axis=1, keepdims=True)
    accum = jnp.dot(w_p.astype(jnp.bfloat16), kp, preferred_element_type=jnp.float32)[:, :lat] + jnp.dot(
        w_s.astype(jnp.bfloat16), k_lat, preferred_element_type=jnp.float32
    )
    out_ref[...] = (accum / total).astype(out_ref.dtype)


def attend(base, q_lat, q_rot, kp, k_lat, k_rot, lo, hi, window, block=256):
    rows = q_lat.shape[0]
    return pl.pallas_call(
        functools.partial(attend_kernel, window=window, scale=1.0 / math.sqrt(NOPE + ROPE)),
        grid_spec=pltpu.PrefetchScalarGridSpec(
            num_scalar_prefetch=1,
            grid=(rows // block,),
            in_specs=[
                pl.BlockSpec((block, LAT), lambda i, b: (i, 0)),
                pl.BlockSpec((block, ROPE), lambda i, b: (i, 0)),
                pl.BlockSpec(kp.shape, lambda i, b: (0, 0)),
                pl.BlockSpec(k_lat.shape, lambda i, b: (0, 0)),
                pl.BlockSpec(k_rot.shape, lambda i, b: (0, 0)),
                pl.BlockSpec((block, 1), lambda i, b: (i, 0)),
                pl.BlockSpec((block, 1), lambda i, b: (i, 0)),
            ],
            out_specs=pl.BlockSpec((block, LAT), lambda i, b: (i, 0)),
        ),
        out_shape=jax.ShapeDtypeStruct((rows, LAT), jnp.bfloat16),
    )(base, q_lat, q_rot, kp, k_lat, k_rot, lo, hi)


def expert_rows(received, gate_pieces, up_pieces, down_pieces):
    owned = gate_pieces.shape[0]
    grid = received.reshape(-1, owned, received.shape[1], received.shape[2])
    gate = jnp.einsum("spkd,pdf->spkf", grid, gate_pieces, preferred_element_type=jnp.float32)
    upper = jnp.einsum("spkd,pdf->spkf", grid, up_pieces, preferred_element_type=jnp.float32)
    active = (jax.nn.silu(gate) * upper).astype(jnp.bfloat16)
    output = jnp.einsum(
        "spkf,pfd->spkd", active, down_pieces, preferred_element_type=jnp.float32
    ).astype(jnp.bfloat16)
    return output.reshape(received.shape)


def on_device(
    hidden_in,
    queries,
    latent_weight,
    latent_gain,
    key_up,
    value_up,
    out_weight,
    ffn_gain,
    router_weight,
    gate_pieces,
    up_pieces,
    down_pieces,
    prefix_latent,
    prefix_rope,
    page_table,
    segment_ids,
    expert_ids,
):
    rows = hidden_in.shape[0]
    n_wide = lax.axis_size("wide")
    wide_at = lax.axis_index("wide")
    my_start = wide_at * rows
    prefix_len = prefix_latent.shape[0] * lax.axis_size("req") * PAGE
    slots = lax.axis_index("req") * prefix_latent.shape[0] + jnp.arange(
        prefix_latent.shape[0], dtype=jnp.int32
    )
    key_pos = page_positions(page_table, slots)
    own_rot = rotary(prefix_rope.reshape(-1, ROPE).astype(jnp.float32), key_pos).astype(jnp.bfloat16)
    own_keys = jnp.concatenate([prefix_latent.reshape(-1, LAT), own_rot], axis=1)
    page_keys = lax.all_gather(own_keys, "req", axis=0, tiled=True)
    raw = jnp.dot(hidden_in, latent_weight, preferred_element_type=jnp.float32)
    latent = rms_scale(raw[:, :LAT], latent_gain).astype(jnp.bfloat16)
    key_rope = raw[:, LAT:].astype(jnp.bfloat16)
    suffix_cache = jnp.concatenate([latent, key_rope], axis=1)
    tag = jnp.broadcast_to(segment_ids.reshape(rows, 1).astype(jnp.bfloat16), (rows, ROPE))
    group = lax.all_gather(
        jnp.concatenate([suffix_cache, tag], axis=1), "wide", axis=0, tiled=True
    )
    group_seg = group[:, LAT + ROPE].astype(jnp.int32)
    group_pos = prefix_len + offsets(group_seg)
    group_rot = rotary(group[:, LAT : LAT + ROPE].astype(jnp.float32), group_pos).astype(
        jnp.bfloat16
    )
    index_q = my_start + jnp.arange(rows, dtype=jnp.int32)
    position = lax.dynamic_slice_in_dim(group_pos, my_start, rows, 0)
    split_q = queries.reshape(rows, HEADS, NOPE + ROPE)
    q_lat = jnp.einsum(
        "thn,lhn->thl",
        split_q[..., :NOPE],
        key_up.reshape(LAT, HEADS, NOPE),
        preferred_element_type=jnp.float32,
    ).astype(jnp.bfloat16)
    q_rot = rotary(split_q[..., NOPE:].astype(jnp.float32), position).astype(jnp.bfloat16)
    reach = -(-(MOST_LEN - 1) // rows) + 1
    blocks = min(n_wide, reach)
    base = (jnp.maximum(wide_at - (blocks - 1), 0) * rows).astype(jnp.int32).reshape(1)
    lo = jnp.repeat((index_q - (position - prefix_len))[:, None], HEADS, axis=0)
    hi = jnp.repeat(index_q[:, None], HEADS, axis=0)
    mixed = attend(
        base,
        q_lat.reshape(rows * HEADS, LAT),
        q_rot.reshape(rows * HEADS, ROPE),
        page_keys,
        group,
        group_rot,
        lo,
        hi,
        blocks * rows,
    ).reshape(
        rows, HEADS, LAT
    )
    head_out = (
        jnp.einsum(
            "thl,lhn->thn",
            mixed,
            value_up.reshape(LAT, HEADS, NOPE),
            preferred_element_type=jnp.float32,
        )
        .astype(jnp.bfloat16)
        .reshape(rows, HEADS * NOPE)
    )
    residual = hidden_in.astype(jnp.float32) + jnp.dot(
        head_out, out_weight, preferred_element_type=jnp.float32
    )
    normed = rms_scale(residual, ffn_gain).astype(jnp.bfloat16)
    logits = jnp.dot(normed, router_weight, preferred_element_type=jnp.float32)
    hits = expert_ids[..., None] == jnp.arange(EXPERTS, dtype=jnp.int32)
    chosen = jnp.sum(jnp.where(hits, logits[:, None, :], 0.0), axis=-1)
    gates = jax.nn.softmax(chosen, axis=-1)
    flat_hits = hits.reshape(rows * TOPK, EXPERTS).astype(jnp.int32)
    slot = jnp.sum((jnp.cumsum(flat_hits, axis=0) - flat_hits) * flat_hits, axis=-1).reshape(
        rows, TOPK
    )
    column = jnp.arange(EXPERTS * SPLIT * CAP, dtype=jnp.int32)
    first = expert_ids * (SPLIT * CAP) + slot
    match = jnp.zeros((EXPERTS * SPLIT * CAP, rows, TOPK), dtype=bool)
    for half in range(SPLIT):
        match = match | ((first + half * CAP)[None, :, :] == column[:, None, None])
    selector = jnp.any(match, axis=-1).astype(jnp.bfloat16)
    outgoing = (
        jnp.dot(selector, normed, preferred_element_type=jnp.float32)
        .astype(jnp.bfloat16)
        .reshape(EXPERTS * SPLIT, CAP, D)
    )
    worked = expert_rows(
        lax.all_to_all(outgoing, ("req", "wide"), split_axis=0, concat_axis=0, tiled=True),
        gate_pieces,
        up_pieces,
        down_pieces,
    )
    returned = lax.all_to_all(worked, ("req", "wide"), split_axis=0, concat_axis=0, tiled=True)
    weight = jnp.sum(jnp.where(match.transpose(1, 0, 2), gates[:, None, :], 0.0), axis=-1)
    weight_hi = weight.astype(jnp.bfloat16)
    weight_lo = (weight - weight_hi.astype(jnp.float32)).astype(jnp.bfloat16)
    shape3 = (rows, EXPERTS * SPLIT, CAP)
    routed = jnp.einsum(
        "tps,psd->td", weight_hi.reshape(shape3), returned, preferred_element_type=jnp.float32
    ) + jnp.einsum(
        "tps,psd->td", weight_lo.reshape(shape3), returned, preferred_element_type=jnp.float32
    )
    return ((residual + routed).astype(jnp.bfloat16), suffix_cache)


def solution(mesh):
    return jax.shard_map(
        on_device,
        mesh=mesh,
        in_specs=(
            P(("req", "wide"), None),
            P(("req", "wide"), None),
            P(),
            P(),
            P(),
            P(),
            P(),
            P(),
            P(),
            P(("req", "wide"), None, None),
            P(("req", "wide"), None, None),
            P(("req", "wide"), None, None),
            P("req", None, None),
            P("req", None, None),
            P(),
            P("req", "wide"),
            P(("req", "wide"), None),
        ),
        out_specs=(P(("req", "wide"), None), P(("req", "wide"), None)),
        check_vma=False,
    )
```

```python
import functools
import math

import jax
import jax.numpy as jnp
from jax import lax
from jax.experimental import pallas as pl
from jax.experimental.pallas import tpu as pltpu
from jax.sharding import PartitionSpec as P

D = 2048
HEADS = 16
NOPE = 128
ROPE = 64
LAT = 512
EXPERTS = 64
TOPK = 6
SPLIT = 2
PAGE = 128
CAP = 14
MOST_LEN = 1024


EPS = 1e-06
NEG = -1e30


def rotary(values, positions):
    half = values.shape[-1] // 2
    freqs = 10000.0 ** (-2.0 * jnp.arange(half, dtype=jnp.float32) / values.shape[-1])
    angles = positions.astype(jnp.float32)[:, None] * freqs[None, :]
    shape = (positions.shape[0],) + (1,) * (values.ndim - 2) + (half,)
    cosine = jnp.cos(angles).reshape(shape)
    sine = jnp.sin(angles).reshape(shape)
    first = values[..., :half]
    second = values[..., half:]
    return jnp.concatenate(
        [first * cosine - second * sine, second * cosine + first * sine], axis=-1
    )


def rms_scale(values, gain):
    return values * lax.rsqrt(jnp.mean(values * values, axis=-1, keepdims=True) + EPS) * gain


def offsets(segments):
    length = segments.shape[0]
    index = jnp.arange(length, dtype=jnp.int32)
    fresh = jnp.concatenate([jnp.ones((1,), dtype=bool), segments[1:] != segments[:-1]])
    starts = lax.cummax(jnp.where(fresh, index, 0), axis=0)
    return index - starts


def page_positions(page_table, slots):
    logical = jnp.sum(
        jnp.where(
            page_table[None, :] == slots[:, None],
            jnp.arange(page_table.shape[0], dtype=jnp.int32)[None, :],
            0,
        ),
        axis=1,
    )
    return (logical[:, None] * PAGE + jnp.arange(PAGE, dtype=jnp.int32)[None, :]).reshape(-1)


def attend_kernel(
    base_ref, ql_ref, qr_ref, kp_ref, kl_ref, kr_ref, lo_ref, hi_ref, out_ref, *, window, scale
):
    base = pl.multiple_of(base_ref[0], 128)
    lat = out_ref.shape[1]
    q = jnp.concatenate([ql_ref[...], qr_ref[...]], axis=1)
    kp = kp_ref[...]
    k_lat = kl_ref[pl.ds(base, window), :lat]
    k_rot = kr_ref[pl.ds(base, window), :]
    dims = (((1,), (1,)), ((), ()))
    s_p = lax.dot_general(q, kp, dims, preferred_element_type=jnp.float32) * scale
    s_s = (
        lax.dot_general(ql_ref[...], k_lat, dims, preferred_element_type=jnp.float32)
        + lax.dot_general(qr_ref[...], k_rot, dims, preferred_element_type=jnp.float32)
    ) * scale
    kidx = base + lax.broadcasted_iota(jnp.int32, (1, window), 1)
    allowed = (kidx >= lo_ref[...]) & (kidx <= hi_ref[...])
    s_s = jnp.where(allowed, s_s, NEG)
    top = jnp.maximum(jnp.max(s_p, axis=1, keepdims=True), jnp.max(s_s, axis=1, keepdims=True))
    w_p = jnp.exp(s_p - top)
    w_s = jnp.exp(s_s - top)
    total = jnp.sum(w_p, axis=1, keepdims=True) + jnp.sum(w_s, axis=1, keepdims=True)
    accum = jnp.dot(w_p.astype(jnp.bfloat16), kp, preferred_element_type=jnp.float32)[:, :lat] + jnp.dot(
        w_s.astype(jnp.bfloat16), k_lat, preferred_element_type=jnp.float32
    )
    out_ref[...] = (accum / total).astype(out_ref.dtype)


def attend(base, q_lat, q_rot, kp, k_lat, k_rot, lo, hi, window, block=256):
    rows = q_lat.shape[0]
    return pl.pallas_call(
        functools.partial(attend_kernel, window=window, scale=1.0 / math.sqrt(NOPE + ROPE)),
        grid_spec=pltpu.PrefetchScalarGridSpec(
            num_scalar_prefetch=1,
            grid=(rows // block,),
            in_specs=[
                pl.BlockSpec((block, LAT), lambda i, b: (i, 0)),
                pl.BlockSpec((block, ROPE), lambda i, b: (i, 0)),
                pl.BlockSpec(kp.shape, lambda i, b: (0, 0)),
                pl.BlockSpec(k_lat.shape, lambda i, b: (0, 0)),
                pl.BlockSpec(k_rot.shape, lambda i, b: (0, 0)),
                pl.BlockSpec((block, 1), lambda i, b: (i, 0)),
                pl.BlockSpec((block, 1), lambda i, b: (i, 0)),
            ],
            out_specs=pl.BlockSpec((block, LAT), lambda i, b: (i, 0)),
        ),
        out_shape=jax.ShapeDtypeStruct((rows, LAT), jnp.bfloat16),
    )(base, q_lat, q_rot, kp, k_lat, k_rot, lo, hi)


def expert_rows(received, gate_pieces, up_pieces, down_pieces):
    owned = gate_pieces.shape[0]
    grid = received.reshape(-1, owned, received.shape[1], received.shape[2])
    gate = jnp.einsum("spkd,pdf->spkf", grid, gate_pieces, preferred_element_type=jnp.float32)
    upper = jnp.einsum("spkd,pdf->spkf", grid, up_pieces, preferred_element_type=jnp.float32)
    active = (jax.nn.silu(gate) * upper).astype(jnp.bfloat16)
    output = jnp.einsum(
        "spkf,pfd->spkd", active, down_pieces, preferred_element_type=jnp.float32
    ).astype(jnp.bfloat16)
    return output.reshape(received.shape)


def on_device(
    hidden_in,
    queries,
    latent_weight,
    latent_gain,
    key_up,
    value_up,
    out_weight,
    ffn_gain,
    router_weight,
    gate_pieces,
    up_pieces,
    down_pieces,
    prefix_latent,
    prefix_rope,
    page_table,
    segment_ids,
    expert_ids,
):
    rows = hidden_in.shape[0]
    n_wide = lax.axis_size("wide")
    wide_at = lax.axis_index("wide")
    my_start = wide_at * rows
    prefix_len = prefix_latent.shape[0] * lax.axis_size("req") * PAGE
    slots = lax.axis_index("req") * prefix_latent.shape[0] + jnp.arange(
        prefix_latent.shape[0], dtype=jnp.int32
    )
    key_pos = page_positions(page_table, slots)
    own_rot = rotary(prefix_rope.reshape(-1, ROPE).astype(jnp.float32), key_pos).astype(jnp.bfloat16)
    own_keys = jnp.concatenate([prefix_latent.reshape(-1, LAT), own_rot], axis=1)
    page_keys = lax.all_gather(own_keys, "req", axis=0, tiled=True)
    raw = jnp.dot(hidden_in, latent_weight, preferred_element_type=jnp.float32)
    latent = rms_scale(raw[:, :LAT], latent_gain).astype(jnp.bfloat16)
    key_rope = raw[:, LAT:].astype(jnp.bfloat16)
    suffix_cache = jnp.concatenate([latent, key_rope], axis=1)
    tag = jnp.broadcast_to(segment_ids.reshape(rows, 1).astype(jnp.bfloat16), (rows, ROPE))
    group = lax.all_gather(
        jnp.concatenate([suffix_cache, tag], axis=1), "wide", axis=0, tiled=True
    )
    group_seg = group[:, LAT + ROPE].astype(jnp.int32)
    group_pos = prefix_len + offsets(group_seg)
    group_rot = rotary(group[:, LAT : LAT + ROPE].astype(jnp.float32), group_pos).astype(
        jnp.bfloat16
    )
    index_q = my_start + jnp.arange(rows, dtype=jnp.int32)
    position = lax.dynamic_slice_in_dim(group_pos, my_start, rows, 0)
    split_q = queries.reshape(rows, HEADS, NOPE + ROPE)
    q_lat = jnp.einsum(
        "thn,lhn->thl",
        split_q[..., :NOPE],
        key_up.reshape(LAT, HEADS, NOPE),
        preferred_element_type=jnp.float32,
    ).astype(jnp.bfloat16)
    q_rot = rotary(split_q[..., NOPE:].astype(jnp.float32), position).astype(jnp.bfloat16)
    reach = -(-(MOST_LEN - 1) // rows) + 1
    blocks = min(n_wide, reach)
    base = (jnp.maximum(wide_at - (blocks - 1), 0) * rows).astype(jnp.int32).reshape(1)
    lo = jnp.repeat((index_q - (position - prefix_len))[:, None], HEADS, axis=0)
    hi = jnp.repeat(index_q[:, None], HEADS, axis=0)
    mixed = attend(
        base,
        q_lat.reshape(rows * HEADS, LAT),
        q_rot.reshape(rows * HEADS, ROPE),
        page_keys,
        group,
        group_rot,
        lo,
        hi,
        blocks * rows,
    ).reshape(
        rows, HEADS, LAT
    )
    head_out = (
        jnp.einsum(
            "thl,lhn->thn",
            mixed,
            value_up.reshape(LAT, HEADS, NOPE),
            preferred_element_type=jnp.float32,
        )
        .astype(jnp.bfloat16)
        .reshape(rows, HEADS * NOPE)
    )
    residual = hidden_in.astype(jnp.float32) + jnp.dot(
        head_out, out_weight, preferred_element_type=jnp.float32
    )
    normed = rms_scale(residual, ffn_gain).astype(jnp.bfloat16)
    logits = jnp.dot(normed, router_weight, preferred_element_type=jnp.float32)
    hits = expert_ids[..., None] == jnp.arange(EXPERTS, dtype=jnp.int32)
    chosen = jnp.sum(jnp.where(hits, logits[:, None, :], 0.0), axis=-1)
    gates = jax.nn.softmax(chosen, axis=-1)
    flat_hits = hits.reshape(rows * TOPK, EXPERTS).astype(jnp.int32)
    slot = jnp.sum((jnp.cumsum(flat_hits, axis=0) - flat_hits) * flat_hits, axis=-1).reshape(
        rows, TOPK
    )
    column = jnp.arange(EXPERTS * SPLIT * CAP, dtype=jnp.int32)
    first = expert_ids * (SPLIT * CAP) + slot
    match = jnp.zeros((EXPERTS * SPLIT * CAP, rows, TOPK), dtype=bool)
    for half in range(SPLIT):
        match = match | ((first + half * CAP)[None, :, :] == column[:, None, None])
    selector = jnp.any(match, axis=-1).astype(jnp.bfloat16)
    outgoing = (
        jnp.dot(selector, normed, preferred_element_type=jnp.float32)
        .astype(jnp.bfloat16)
        .reshape(EXPERTS * SPLIT, CAP, D)
    )
    cut = CAP // 2
    parts = []
    for lo_slot, hi_slot in ((0, cut), (cut, CAP)):
        sent = lax.all_to_all(
            outgoing[:, lo_slot:hi_slot], ("req", "wide"), split_axis=0, concat_axis=0, tiled=True
        )
        worked = expert_rows(sent, gate_pieces, up_pieces, down_pieces)
        parts.append(
            lax.all_to_all(worked, ("req", "wide"), split_axis=0, concat_axis=0, tiled=True)
        )
    returned = jnp.concatenate(parts, axis=1)
    weight = jnp.sum(jnp.where(match.transpose(1, 0, 2), gates[:, None, :], 0.0), axis=-1)
    weight_hi = weight.astype(jnp.bfloat16)
    weight_lo = (weight - weight_hi.astype(jnp.float32)).astype(jnp.bfloat16)
    flat = returned.reshape(EXPERTS * SPLIT * CAP, D)
    routed = jnp.dot(weight_hi, flat, preferred_element_type=jnp.float32) + jnp.dot(
        weight_lo, flat, preferred_element_type=jnp.float32
    )
    return ((residual + routed).astype(jnp.bfloat16), suffix_cache)


def solution(mesh):
    return jax.shard_map(
        on_device,
        mesh=mesh,
        in_specs=(
            P(("req", "wide"), None),
            P(("req", "wide"), None),
            P(),
            P(),
            P(),
            P(),
            P(),
            P(),
            P(),
            P(("req", "wide"), None, None),
            P(("req", "wide"), None, None),
            P(("req", "wide"), None, None),
            P("req", None, None),
            P("req", None, None),
            P(),
            P("req", "wide"),
            P(("req", "wide"), None),
        ),
        out_specs=(P(("req", "wide"), None), P(("req", "wide"), None)),
        check_vma=False,
    )
```

```python
import functools
import math

import jax
import jax.numpy as jnp
from jax import lax
from jax.experimental import pallas as pl
from jax.experimental.pallas import tpu as pltpu
from jax.sharding import PartitionSpec as P

D = 2048
HEADS = 16
NOPE = 128
ROPE = 64
LAT = 512
EXPERTS = 64
TOPK = 6
SPLIT = 2
PAGE = 128
CAP = 14
MOST_LEN = 1024


EPS = 1e-06
NEG = -1e30


def rotary(values, positions):
    half = values.shape[-1] // 2
    freqs = 10000.0 ** (-2.0 * jnp.arange(half, dtype=jnp.float32) / values.shape[-1])
    angles = positions.astype(jnp.float32)[:, None] * freqs[None, :]
    shape = (positions.shape[0],) + (1,) * (values.ndim - 2) + (half,)
    cosine = jnp.cos(angles).reshape(shape)
    sine = jnp.sin(angles).reshape(shape)
    first = values[..., :half]
    second = values[..., half:]
    return jnp.concatenate(
        [first * cosine - second * sine, second * cosine + first * sine], axis=-1
    )


def rms_scale(values, gain):
    return values * lax.rsqrt(jnp.mean(values * values, axis=-1, keepdims=True) + EPS) * gain


def offsets(segments):
    length = segments.shape[0]
    index = jnp.arange(length, dtype=jnp.int32)
    fresh = jnp.concatenate([jnp.ones((1,), dtype=bool), segments[1:] != segments[:-1]])
    starts = lax.cummax(jnp.where(fresh, index, 0), axis=0)
    return index - starts


def page_positions(page_table, slots):
    logical = jnp.sum(
        jnp.where(
            page_table[None, :] == slots[:, None],
            jnp.arange(page_table.shape[0], dtype=jnp.int32)[None, :],
            0,
        ),
        axis=1,
    )
    return (logical[:, None] * PAGE + jnp.arange(PAGE, dtype=jnp.int32)[None, :]).reshape(-1)


def attend_kernel(
    base_ref, ql_ref, qr_ref, kp_ref, kl_ref, kr_ref, lo_ref, hi_ref, out_ref, *, window, scale
):
    base = pl.multiple_of(base_ref[0], 128)
    lat = out_ref.shape[1]
    q = jnp.concatenate([ql_ref[...], qr_ref[...]], axis=1)
    kp = kp_ref[...]
    k_lat = kl_ref[pl.ds(base, window), :lat]
    k_rot = kr_ref[pl.ds(base, window), :]
    dims = (((1,), (1,)), ((), ()))
    s_p = lax.dot_general(q, kp, dims, preferred_element_type=jnp.float32) * scale
    s_s = (
        lax.dot_general(ql_ref[...], k_lat, dims, preferred_element_type=jnp.float32)
        + lax.dot_general(qr_ref[...], k_rot, dims, preferred_element_type=jnp.float32)
    ) * scale
    kidx = base + lax.broadcasted_iota(jnp.int32, (1, window), 1)
    allowed = (kidx >= lo_ref[...]) & (kidx <= hi_ref[...])
    s_s = jnp.where(allowed, s_s, NEG)
    top = jnp.maximum(jnp.max(s_p, axis=1, keepdims=True), jnp.max(s_s, axis=1, keepdims=True))
    w_p = jnp.exp(s_p - top)
    w_s = jnp.exp(s_s - top)
    total = jnp.sum(w_p, axis=1, keepdims=True) + jnp.sum(w_s, axis=1, keepdims=True)
    accum = jnp.dot(w_p.astype(jnp.bfloat16), kp, preferred_element_type=jnp.float32)[:, :lat] + jnp.dot(
        w_s.astype(jnp.bfloat16), k_lat, preferred_element_type=jnp.float32
    )
    out_ref[...] = (accum / total).astype(out_ref.dtype)


def attend(base, q_lat, q_rot, kp, k_lat, k_rot, lo, hi, window, block=256):
    rows = q_lat.shape[0]
    return pl.pallas_call(
        functools.partial(attend_kernel, window=window, scale=1.0 / math.sqrt(NOPE + ROPE)),
        grid_spec=pltpu.PrefetchScalarGridSpec(
            num_scalar_prefetch=1,
            grid=(rows // block,),
            in_specs=[
                pl.BlockSpec((block, LAT), lambda i, b: (i, 0)),
                pl.BlockSpec((block, ROPE), lambda i, b: (i, 0)),
                pl.BlockSpec(kp.shape, lambda i, b: (0, 0)),
                pl.BlockSpec(k_lat.shape, lambda i, b: (0, 0)),
                pl.BlockSpec(k_rot.shape, lambda i, b: (0, 0)),
                pl.BlockSpec((block, 1), lambda i, b: (i, 0)),
                pl.BlockSpec((block, 1), lambda i, b: (i, 0)),
            ],
            out_specs=pl.BlockSpec((block, LAT), lambda i, b: (i, 0)),
        ),
        out_shape=jax.ShapeDtypeStruct((rows, LAT), jnp.bfloat16),
    )(base, q_lat, q_rot, kp, k_lat, k_rot, lo, hi)


def expert_rows(received, gate_pieces, up_pieces, down_pieces):
    owned = gate_pieces.shape[0]
    grid = received.reshape(-1, owned, received.shape[1], received.shape[2])
    gate = jnp.einsum("spkd,pdf->spkf", grid, gate_pieces, preferred_element_type=jnp.float32)
    upper = jnp.einsum("spkd,pdf->spkf", grid, up_pieces, preferred_element_type=jnp.float32)
    active = (jax.nn.silu(gate) * upper).astype(jnp.bfloat16)
    output = jnp.einsum(
        "spkf,pfd->spkd", active, down_pieces, preferred_element_type=jnp.float32
    ).astype(jnp.bfloat16)
    return output.reshape(received.shape)


def on_device(
    hidden_in,
    queries,
    latent_weight,
    latent_gain,
    key_up,
    value_up,
    out_weight,
    ffn_gain,
    router_weight,
    gate_pieces,
    up_pieces,
    down_pieces,
    prefix_latent,
    prefix_rope,
    page_table,
    segment_ids,
    expert_ids,
):
    rows = hidden_in.shape[0]
    n_wide = lax.axis_size("wide")
    wide_at = lax.axis_index("wide")
    my_start = wide_at * rows
    prefix_len = prefix_latent.shape[0] * lax.axis_size("req") * PAGE
    slots = lax.axis_index("req") * prefix_latent.shape[0] + jnp.arange(
        prefix_latent.shape[0], dtype=jnp.int32
    )
    key_pos = page_positions(page_table, slots)
    own_rot = rotary(prefix_rope.reshape(-1, ROPE).astype(jnp.float32), key_pos).astype(jnp.bfloat16)
    own_keys = jnp.concatenate([prefix_latent.reshape(-1, LAT), own_rot], axis=1)
    page_keys = lax.all_gather(own_keys, "req", axis=0, tiled=True)
    raw = jnp.dot(hidden_in, latent_weight, preferred_element_type=jnp.float32)
    latent = rms_scale(raw[:, :LAT], latent_gain).astype(jnp.bfloat16)
    key_rope = raw[:, LAT:].astype(jnp.bfloat16)
    suffix_cache = jnp.concatenate([latent, key_rope], axis=1)
    tag = jnp.broadcast_to(segment_ids.reshape(rows, 1).astype(jnp.bfloat16), (rows, ROPE))
    group = lax.all_gather(
        jnp.concatenate([suffix_cache, tag], axis=1), "wide", axis=0, tiled=True
    )
    group_seg = group[:, LAT + ROPE].astype(jnp.int32)
    group_pos = prefix_len + offsets(group_seg)
    group_rot = rotary(group[:, LAT : LAT + ROPE].astype(jnp.float32), group_pos).astype(
        jnp.bfloat16
    )
    index_q = my_start + jnp.arange(rows, dtype=jnp.int32)
    position = lax.dynamic_slice_in_dim(group_pos, my_start, rows, 0)
    split_q = queries.reshape(rows, HEADS, NOPE + ROPE)
    q_lat = jnp.einsum(
        "thn,lhn->thl",
        split_q[..., :NOPE],
        key_up.reshape(LAT, HEADS, NOPE),
        preferred_element_type=jnp.float32,
    ).astype(jnp.bfloat16)
    q_rot = rotary(split_q[..., NOPE:].astype(jnp.float32), position).astype(jnp.bfloat16)
    reach = -(-(MOST_LEN - 1) // rows) + 1
    blocks = min(n_wide, reach)
    base = (jnp.maximum(wide_at - (blocks - 1), 0) * rows).astype(jnp.int32).reshape(1)
    lo = jnp.repeat((index_q - (position - prefix_len))[:, None], HEADS, axis=0)
    hi = jnp.repeat(index_q[:, None], HEADS, axis=0)
    mixed = attend(
        base,
        q_lat.reshape(rows * HEADS, LAT),
        q_rot.reshape(rows * HEADS, ROPE),
        page_keys,
        group,
        group_rot,
        lo,
        hi,
        blocks * rows,
    ).reshape(
        rows, HEADS, LAT
    )
    head_out = (
        jnp.einsum(
            "thl,lhn->thn",
            mixed,
            value_up.reshape(LAT, HEADS, NOPE),
            preferred_element_type=jnp.float32,
        )
        .astype(jnp.bfloat16)
        .reshape(rows, HEADS * NOPE)
    )
    residual = hidden_in.astype(jnp.float32) + jnp.dot(
        head_out, out_weight, preferred_element_type=jnp.float32
    )
    normed = rms_scale(residual, ffn_gain).astype(jnp.bfloat16)
    logits = jnp.dot(normed, router_weight, preferred_element_type=jnp.float32)
    hits = expert_ids[..., None] == jnp.arange(EXPERTS, dtype=jnp.int32)
    chosen = jnp.sum(jnp.where(hits, logits[:, None, :], 0.0), axis=-1)
    gates = jax.nn.softmax(chosen, axis=-1)
    flat_hits = hits.reshape(rows * TOPK, EXPERTS).astype(jnp.int32)
    slot = jnp.sum((jnp.cumsum(flat_hits, axis=0) - flat_hits) * flat_hits, axis=-1).reshape(
        rows, TOPK
    )
    column = jnp.arange(EXPERTS * SPLIT * CAP, dtype=jnp.int32)
    first = expert_ids * (SPLIT * CAP) + slot
    match = jnp.zeros((EXPERTS * SPLIT * CAP, rows, TOPK), dtype=bool)
    for half in range(SPLIT):
        match = match | ((first + half * CAP)[None, :, :] == column[:, None, None])
    selector = jnp.any(match, axis=-1).astype(jnp.bfloat16)
    outgoing = (
        jnp.dot(selector, normed, preferred_element_type=jnp.float32)
        .astype(jnp.bfloat16)
        .reshape(EXPERTS * SPLIT, CAP, D)
    )
    cut = CAP // 2
    parts = []
    for lo_slot, hi_slot in ((0, cut), (cut, CAP)):
        sent = lax.all_to_all(
            outgoing[:, lo_slot:hi_slot], ("req", "wide"), split_axis=0, concat_axis=0, tiled=True
        )
        worked = expert_rows(sent, gate_pieces, up_pieces, down_pieces)
        parts.append(
            lax.all_to_all(worked, ("req", "wide"), split_axis=0, concat_axis=0, tiled=True)
        )
    weight = jnp.sum(jnp.where(match.transpose(1, 0, 2), gates[:, None, :], 0.0), axis=-1)
    weight_hi = weight.astype(jnp.bfloat16)
    weight_lo = (weight - weight_hi.astype(jnp.float32)).astype(jnp.bfloat16)
    routed = jnp.zeros((rows, D), jnp.float32)
    bounds = ((0, cut), (cut, CAP))
    for (lo_slot, hi_slot), part in zip(bounds, parts):
        flat = part.reshape(-1, D)
        for piece_weight in (weight_hi, weight_lo):
            chunk = piece_weight.reshape(rows, EXPERTS * SPLIT, CAP)[:, :, lo_slot:hi_slot]
            routed = routed + jnp.dot(
                chunk.reshape(rows, -1), flat, preferred_element_type=jnp.float32
            )
    return ((residual + routed).astype(jnp.bfloat16), suffix_cache)


def solution(mesh):
    return jax.shard_map(
        on_device,
        mesh=mesh,
        in_specs=(
            P(("req", "wide"), None),
            P(("req", "wide"), None),
            P(),
            P(),
            P(),
            P(),
            P(),
            P(),
            P(),
            P(("req", "wide"), None, None),
            P(("req", "wide"), None, None),
            P(("req", "wide"), None, None),
            P("req", None, None),
            P("req", None, None),
            P(),
            P("req", "wide"),
            P(("req", "wide"), None),
        ),
        out_specs=(P(("req", "wide"), None), P(("req", "wide"), None)),
        check_vma=False,
    )
```

```python
import functools
import math

import jax
import jax.numpy as jnp
from jax import lax
from jax.experimental import pallas as pl
from jax.experimental.pallas import tpu as pltpu
from jax.sharding import PartitionSpec as P

D = 2048
HEADS = 16
NOPE = 128
ROPE = 64
LAT = 512
EXPERTS = 64
TOPK = 6
SPLIT = 2
PAGE = 128
CAP = 14
MOST_LEN = 1024


EPS = 1e-06
NEG = -1e30


def rotary(values, positions):
    half = values.shape[-1] // 2
    freqs = 10000.0 ** (-2.0 * jnp.arange(half, dtype=jnp.float32) / values.shape[-1])
    angles = positions.astype(jnp.float32)[:, None] * freqs[None, :]
    shape = (positions.shape[0],) + (1,) * (values.ndim - 2) + (half,)
    cosine = jnp.cos(angles).reshape(shape)
    sine = jnp.sin(angles).reshape(shape)
    first = values[..., :half]
    second = values[..., half:]
    return jnp.concatenate(
        [first * cosine - second * sine, second * cosine + first * sine], axis=-1
    )


def rms_scale(values, gain):
    return values * lax.rsqrt(jnp.mean(values * values, axis=-1, keepdims=True) + EPS) * gain


def offsets(segments):
    length = segments.shape[0]
    index = jnp.arange(length, dtype=jnp.int32)
    fresh = jnp.concatenate([jnp.ones((1,), dtype=bool), segments[1:] != segments[:-1]])
    starts = lax.cummax(jnp.where(fresh, index, 0), axis=0)
    return index - starts


def page_positions(page_table, slots):
    logical = jnp.sum(
        jnp.where(
            page_table[None, :] == slots[:, None],
            jnp.arange(page_table.shape[0], dtype=jnp.int32)[None, :],
            0,
        ),
        axis=1,
    )
    return (logical[:, None] * PAGE + jnp.arange(PAGE, dtype=jnp.int32)[None, :]).reshape(-1)


def attend_kernel(
    base_ref, ql_ref, qr_ref, kp_ref, kl_ref, kr_ref, lo_ref, hi_ref, out_ref, *, window, scale
):
    base = pl.multiple_of(base_ref[0], 128)
    lat = out_ref.shape[1]
    q = jnp.concatenate([ql_ref[...], qr_ref[...]], axis=1)
    kp = kp_ref[...]
    k_lat = kl_ref[pl.ds(base, window), :lat]
    k_rot = kr_ref[pl.ds(base, window), :]
    dims = (((1,), (1,)), ((), ()))
    s_p = lax.dot_general(q, kp, dims, preferred_element_type=jnp.float32) * scale
    s_s = (
        lax.dot_general(ql_ref[...], k_lat, dims, preferred_element_type=jnp.float32)
        + lax.dot_general(qr_ref[...], k_rot, dims, preferred_element_type=jnp.float32)
    ) * scale
    copies = ql_ref.shape[0] // lo_ref.shape[0]
    lo = jnp.concatenate([lo_ref[...]] * copies, axis=0)
    hi = jnp.concatenate([hi_ref[...]] * copies, axis=0)
    kidx = base + lax.broadcasted_iota(jnp.int32, (1, window), 1)
    allowed = (kidx >= lo) & (kidx <= hi)
    s_s = jnp.where(allowed, s_s, NEG)
    top = jnp.maximum(jnp.max(s_p, axis=1, keepdims=True), jnp.max(s_s, axis=1, keepdims=True))
    w_p = jnp.exp(s_p - top)
    w_s = jnp.exp(s_s - top)
    total = jnp.sum(w_p, axis=1, keepdims=True) + jnp.sum(w_s, axis=1, keepdims=True)
    accum = jnp.dot(w_p.astype(jnp.bfloat16), kp, preferred_element_type=jnp.float32)[:, :lat] + jnp.dot(
        w_s.astype(jnp.bfloat16), k_lat, preferred_element_type=jnp.float32
    )
    out_ref[...] = (accum / total).astype(out_ref.dtype)


def attend(base, q_lat, q_rot, kp, k_lat, k_rot, lo, hi, window, block=256):
    rows = q_lat.shape[0]
    return pl.pallas_call(
        functools.partial(attend_kernel, window=window, scale=1.0 / math.sqrt(NOPE + ROPE)),
        grid_spec=pltpu.PrefetchScalarGridSpec(
            num_scalar_prefetch=1,
            grid=(rows // block,),
            in_specs=[
                pl.BlockSpec((block, LAT), lambda i, b: (i, 0)),
                pl.BlockSpec((block, ROPE), lambda i, b: (i, 0)),
                pl.BlockSpec(kp.shape, lambda i, b: (0, 0)),
                pl.BlockSpec(k_lat.shape, lambda i, b: (0, 0)),
                pl.BlockSpec(k_rot.shape, lambda i, b: (0, 0)),
                pl.BlockSpec(lo.shape, lambda i, b: (0, 0)),
                pl.BlockSpec(hi.shape, lambda i, b: (0, 0)),
            ],
            out_specs=pl.BlockSpec((block, LAT), lambda i, b: (i, 0)),
        ),
        out_shape=jax.ShapeDtypeStruct((rows, LAT), jnp.bfloat16),
    )(base, q_lat, q_rot, kp, k_lat, k_rot, lo, hi)


def expert_rows(received, gate_pieces, up_pieces, down_pieces):
    owned = gate_pieces.shape[0]
    grid = received.reshape(-1, owned, received.shape[1], received.shape[2])
    gate = jnp.einsum("spkd,pdf->spkf", grid, gate_pieces, preferred_element_type=jnp.float32)
    upper = jnp.einsum("spkd,pdf->spkf", grid, up_pieces, preferred_element_type=jnp.float32)
    active = (jax.nn.silu(gate) * upper).astype(jnp.bfloat16)
    output = jnp.einsum(
        "spkf,pfd->spkd", active, down_pieces, preferred_element_type=jnp.float32
    ).astype(jnp.bfloat16)
    return output.reshape(received.shape)


def on_device(
    hidden_in,
    queries,
    latent_weight,
    latent_gain,
    key_up,
    value_up,
    out_weight,
    ffn_gain,
    router_weight,
    gate_pieces,
    up_pieces,
    down_pieces,
    prefix_latent,
    prefix_rope,
    page_table,
    segment_ids,
    expert_ids,
):
    rows = hidden_in.shape[0]
    n_wide = lax.axis_size("wide")
    wide_at = lax.axis_index("wide")
    my_start = wide_at * rows
    prefix_len = prefix_latent.shape[0] * lax.axis_size("req") * PAGE
    slots = lax.axis_index("req") * prefix_latent.shape[0] + jnp.arange(
        prefix_latent.shape[0], dtype=jnp.int32
    )
    key_pos = page_positions(page_table, slots)
    own_rot = rotary(prefix_rope.reshape(-1, ROPE).astype(jnp.float32), key_pos).astype(jnp.bfloat16)
    own_keys = jnp.concatenate([prefix_latent.reshape(-1, LAT), own_rot], axis=1)
    page_keys = lax.all_gather(own_keys, "req", axis=0, tiled=True)
    raw = jnp.dot(hidden_in, latent_weight, preferred_element_type=jnp.float32)
    latent = rms_scale(raw[:, :LAT], latent_gain).astype(jnp.bfloat16)
    key_rope = raw[:, LAT:].astype(jnp.bfloat16)
    suffix_cache = jnp.concatenate([latent, key_rope], axis=1)
    tag = jnp.broadcast_to(segment_ids.reshape(rows, 1).astype(jnp.bfloat16), (rows, ROPE))
    group = lax.all_gather(
        jnp.concatenate([suffix_cache, tag], axis=1), "wide", axis=0, tiled=True
    )
    group_seg = group[:, LAT + ROPE].astype(jnp.int32)
    group_pos = prefix_len + offsets(group_seg)
    group_rot = rotary(group[:, LAT : LAT + ROPE].astype(jnp.float32), group_pos).astype(
        jnp.bfloat16
    )
    index_q = my_start + jnp.arange(rows, dtype=jnp.int32)
    position = lax.dynamic_slice_in_dim(group_pos, my_start, rows, 0)
    split_q = queries.reshape(rows, HEADS, NOPE + ROPE)
    q_lat = jnp.einsum(
        "thn,lhn->htl",
        split_q[..., :NOPE],
        key_up.reshape(LAT, HEADS, NOPE),
        preferred_element_type=jnp.float32,
    ).astype(jnp.bfloat16)
    q_rot = (
        rotary(split_q[..., NOPE:].astype(jnp.float32), position)
        .astype(jnp.bfloat16)
        .transpose(1, 0, 2)
    )
    reach = -(-(MOST_LEN - 1) // rows) + 1
    blocks = min(n_wide, reach)
    base = (jnp.maximum(wide_at - (blocks - 1), 0) * rows).astype(jnp.int32).reshape(1)
    lo = (index_q - (position - prefix_len))[:, None]
    hi = index_q[:, None]
    mixed = attend(
        base,
        q_lat.reshape(rows * HEADS, LAT),
        q_rot.reshape(rows * HEADS, ROPE),
        page_keys,
        group,
        group_rot,
        lo,
        hi,
        blocks * rows,
    ).reshape(
        HEADS, rows, LAT
    )
    head_out = (
        jnp.einsum(
            "htl,lhn->thn",
            mixed,
            value_up.reshape(LAT, HEADS, NOPE),
            preferred_element_type=jnp.float32,
        )
        .astype(jnp.bfloat16)
        .reshape(rows, HEADS * NOPE)
    )
    residual = hidden_in.astype(jnp.float32) + jnp.dot(
        head_out, out_weight, preferred_element_type=jnp.float32
    )
    normed = rms_scale(residual, ffn_gain).astype(jnp.bfloat16)
    logits = jnp.dot(normed, router_weight, preferred_element_type=jnp.float32)
    hits = expert_ids[..., None] == jnp.arange(EXPERTS, dtype=jnp.int32)
    chosen = jnp.sum(jnp.where(hits, logits[:, None, :], 0.0), axis=-1)
    gates = jax.nn.softmax(chosen, axis=-1)
    flat_hits = hits.reshape(rows * TOPK, EXPERTS).astype(jnp.int32)
    slot = jnp.sum((jnp.cumsum(flat_hits, axis=0) - flat_hits) * flat_hits, axis=-1).reshape(
        rows, TOPK
    )
    column = jnp.arange(EXPERTS * SPLIT * CAP, dtype=jnp.int32)
    first = expert_ids * (SPLIT * CAP) + slot
    match = jnp.zeros((EXPERTS * SPLIT * CAP, rows, TOPK), dtype=bool)
    for half in range(SPLIT):
        match = match | ((first + half * CAP)[None, :, :] == column[:, None, None])
    selector = jnp.any(match, axis=-1).astype(jnp.bfloat16)
    outgoing = (
        jnp.dot(selector, normed, preferred_element_type=jnp.float32)
        .astype(jnp.bfloat16)
        .reshape(EXPERTS * SPLIT, CAP, D)
    )
    cut = CAP // 2
    parts = []
    for lo_slot, hi_slot in ((0, cut), (cut, CAP)):
        sent = lax.all_to_all(
            outgoing[:, lo_slot:hi_slot], ("req", "wide"), split_axis=0, concat_axis=0, tiled=True
        )
        worked = expert_rows(sent, gate_pieces, up_pieces, down_pieces)
        parts.append(
            lax.all_to_all(worked, ("req", "wide"), split_axis=0, concat_axis=0, tiled=True)
        )
    weight = jnp.sum(jnp.where(match.transpose(1, 0, 2), gates[:, None, :], 0.0), axis=-1)
    weight_hi = weight.astype(jnp.bfloat16)
    weight_lo = (weight - weight_hi.astype(jnp.float32)).astype(jnp.bfloat16)
    routed = jnp.zeros((rows, D), jnp.float32)
    bounds = ((0, cut), (cut, CAP))
    stacked = jnp.concatenate([weight_hi, weight_lo], axis=0).reshape(
        2 * rows, EXPERTS * SPLIT, CAP
    )
    for (lo_slot, hi_slot), part in zip(bounds, parts):
        both = jnp.dot(
            stacked[:, :, lo_slot:hi_slot].reshape(2 * rows, -1),
            part.reshape(-1, D),
            preferred_element_type=jnp.float32,
        )
        routed = routed + (both[:rows] + both[rows:])
    return ((residual + routed).astype(jnp.bfloat16), suffix_cache)


def solution(mesh):
    return jax.shard_map(
        on_device,
        mesh=mesh,
        in_specs=(
            P(("req", "wide"), None),
            P(("req", "wide"), None),
            P(),
            P(),
            P(),
            P(),
            P(),
            P(),
            P(),
            P(("req", "wide"), None, None),
            P(("req", "wide"), None, None),
            P(("req", "wide"), None, None),
            P("req", None, None),
            P("req", None, None),
            P(),
            P("req", "wide"),
            P(("req", "wide"), None),
        ),
        out_specs=(P(("req", "wide"), None), P(("req", "wide"), None)),
        check_vma=False,
    )
```

```python
import functools
import math

import jax
import jax.numpy as jnp
from jax import lax
from jax.experimental import pallas as pl
from jax.experimental.pallas import tpu as pltpu
from jax.sharding import PartitionSpec as P

D = 2048
HEADS = 16
NOPE = 128
ROPE = 64
LAT = 512
EXPERTS = 64
TOPK = 6
SPLIT = 2
PAGE = 128
CAP = 14
MOST_LEN = 1024


EPS = 1e-06
NEG = -1e30


def rotary(values, positions):
    half = values.shape[-1] // 2
    freqs = 10000.0 ** (-2.0 * jnp.arange(half, dtype=jnp.float32) / values.shape[-1])
    angles = positions.astype(jnp.float32)[:, None] * freqs[None, :]
    shape = (positions.shape[0],) + (1,) * (values.ndim - 2) + (half,)
    cosine = jnp.cos(angles).reshape(shape)
    sine = jnp.sin(angles).reshape(shape)
    first = values[..., :half]
    second = values[..., half:]
    return jnp.concatenate(
        [first * cosine - second * sine, second * cosine + first * sine], axis=-1
    )


def rms_scale(values, gain):
    return values * lax.rsqrt(jnp.mean(values * values, axis=-1, keepdims=True) + EPS) * gain


def offsets(segments):
    length = segments.shape[0]
    index = jnp.arange(length, dtype=jnp.int32)
    fresh = jnp.concatenate([jnp.ones((1,), dtype=bool), segments[1:] != segments[:-1]])
    starts = lax.cummax(jnp.where(fresh, index, 0), axis=0)
    return index - starts


def page_positions(page_table, slots):
    logical = jnp.sum(
        jnp.where(
            page_table[None, :] == slots[:, None],
            jnp.arange(page_table.shape[0], dtype=jnp.int32)[None, :],
            0,
        ),
        axis=1,
    )
    return (logical[:, None] * PAGE + jnp.arange(PAGE, dtype=jnp.int32)[None, :]).reshape(-1)


def attend_kernel(
    base_ref, ql_ref, qr_ref, kp_ref, kl_ref, kr_ref, lo_ref, hi_ref, out_ref, *, window, scale
):
    base = pl.multiple_of(base_ref[0], 128)
    lat = out_ref.shape[1]
    q = jnp.concatenate([ql_ref[...], qr_ref[...]], axis=1)
    kp = kp_ref[...]
    k_lat = kl_ref[pl.ds(base, window), :lat]
    k_rot = kr_ref[pl.ds(base, window), :]
    dims = (((1,), (1,)), ((), ()))
    s_p = lax.dot_general(q, kp, dims, preferred_element_type=jnp.float32) * scale
    s_s = (
        lax.dot_general(ql_ref[...], k_lat, dims, preferred_element_type=jnp.float32)
        + lax.dot_general(qr_ref[...], k_rot, dims, preferred_element_type=jnp.float32)
    ) * scale
    copies = ql_ref.shape[0] // lo_ref.shape[0]
    lo = jnp.concatenate([lo_ref[...]] * copies, axis=0)
    hi = jnp.concatenate([hi_ref[...]] * copies, axis=0)
    kidx = base + lax.broadcasted_iota(jnp.int32, (1, window), 1)
    allowed = (kidx >= lo) & (kidx <= hi)
    s_s = jnp.where(allowed, s_s, NEG)
    top = jnp.maximum(jnp.max(s_p, axis=1, keepdims=True), jnp.max(s_s, axis=1, keepdims=True))
    w_p = jnp.exp(s_p - top)
    w_s = jnp.exp(s_s - top)
    total = jnp.sum(w_p, axis=1, keepdims=True) + jnp.sum(w_s, axis=1, keepdims=True)
    accum = jnp.dot(w_p.astype(jnp.bfloat16), kp, preferred_element_type=jnp.float32)[:, :lat] + jnp.dot(
        w_s.astype(jnp.bfloat16), k_lat, preferred_element_type=jnp.float32
    )
    out_ref[...] = (accum / total).astype(out_ref.dtype)


def attend(base, q_lat, q_rot, kp, k_lat, k_rot, lo, hi, window, block=256):
    rows = q_lat.shape[0]
    return pl.pallas_call(
        functools.partial(attend_kernel, window=window, scale=1.0 / math.sqrt(NOPE + ROPE)),
        grid_spec=pltpu.PrefetchScalarGridSpec(
            num_scalar_prefetch=1,
            grid=(rows // block,),
            in_specs=[
                pl.BlockSpec((block, LAT), lambda i, b: (i, 0)),
                pl.BlockSpec((block, ROPE), lambda i, b: (i, 0)),
                pl.BlockSpec(kp.shape, lambda i, b: (0, 0)),
                pl.BlockSpec(k_lat.shape, lambda i, b: (0, 0)),
                pl.BlockSpec(k_rot.shape, lambda i, b: (0, 0)),
                pl.BlockSpec(lo.shape, lambda i, b: (0, 0)),
                pl.BlockSpec(hi.shape, lambda i, b: (0, 0)),
            ],
            out_specs=pl.BlockSpec((block, LAT), lambda i, b: (i, 0)),
        ),
        out_shape=jax.ShapeDtypeStruct((rows, LAT), jnp.bfloat16),
    )(base, q_lat, q_rot, kp, k_lat, k_rot, lo, hi)


def expert_rows(received, gate_pieces, up_pieces, down_pieces):
    owned = gate_pieces.shape[0]
    grid = received.reshape(-1, owned, received.shape[1], received.shape[2])
    gate = jnp.einsum("spkd,pdf->spkf", grid, gate_pieces, preferred_element_type=jnp.float32)
    upper = jnp.einsum("spkd,pdf->spkf", grid, up_pieces, preferred_element_type=jnp.float32)
    active = (jax.nn.silu(gate) * upper).astype(jnp.bfloat16)
    output = jnp.einsum(
        "spkf,pfd->spkd", active, down_pieces, preferred_element_type=jnp.float32
    ).astype(jnp.bfloat16)
    return output.reshape(received.shape)


def on_device(
    hidden_in,
    queries,
    latent_weight,
    latent_gain,
    key_up,
    value_up,
    out_weight,
    ffn_gain,
    router_weight,
    gate_pieces,
    up_pieces,
    down_pieces,
    prefix_latent,
    prefix_rope,
    page_table,
    segment_ids,
    expert_ids,
):
    rows = hidden_in.shape[0]
    n_wide = lax.axis_size("wide")
    wide_at = lax.axis_index("wide")
    my_start = wide_at * rows
    prefix_len = prefix_latent.shape[0] * lax.axis_size("req") * PAGE
    slots = lax.axis_index("req") * prefix_latent.shape[0] + jnp.arange(
        prefix_latent.shape[0], dtype=jnp.int32
    )
    key_pos = page_positions(page_table, slots)
    own_rot = rotary(prefix_rope.reshape(-1, ROPE).astype(jnp.float32), key_pos).astype(jnp.bfloat16)
    own_keys = jnp.concatenate([prefix_latent.reshape(-1, LAT), own_rot], axis=1)
    page_keys = lax.all_gather(own_keys, "req", axis=0, tiled=True)
    raw = jnp.dot(hidden_in, latent_weight, preferred_element_type=jnp.float32)
    latent = rms_scale(raw[:, :LAT], latent_gain).astype(jnp.bfloat16)
    key_rope = raw[:, LAT:].astype(jnp.bfloat16)
    suffix_cache = jnp.concatenate([latent, key_rope], axis=1)
    tag = jnp.broadcast_to(segment_ids.reshape(rows, 1).astype(jnp.bfloat16), (rows, ROPE))
    group = lax.all_gather(
        jnp.concatenate([suffix_cache, tag], axis=1), "wide", axis=0, tiled=True
    )
    group_seg = group[:, LAT + ROPE].astype(jnp.int32)
    group_pos = prefix_len + offsets(group_seg)
    group_rot = rotary(group[:, LAT : LAT + ROPE].astype(jnp.float32), group_pos).astype(
        jnp.bfloat16
    )
    index_q = my_start + jnp.arange(rows, dtype=jnp.int32)
    position = lax.dynamic_slice_in_dim(group_pos, my_start, rows, 0)
    split_q = queries.reshape(rows, HEADS, NOPE + ROPE)
    q_lat = jnp.einsum(
        "thn,lhn->htl",
        split_q[..., :NOPE],
        key_up.reshape(LAT, HEADS, NOPE),
        preferred_element_type=jnp.float32,
    ).astype(jnp.bfloat16)
    q_rot = (
        rotary(split_q[..., NOPE:].astype(jnp.float32), position)
        .astype(jnp.bfloat16)
        .transpose(1, 0, 2)
    )
    reach = -(-(MOST_LEN - 1) // rows) + 1
    blocks = min(n_wide, reach)
    base = (jnp.maximum(wide_at - (blocks - 1), 0) * rows).astype(jnp.int32).reshape(1)
    lo = (index_q - (position - prefix_len))[:, None]
    hi = index_q[:, None]
    mixed = attend(
        base,
        q_lat.reshape(rows * HEADS, LAT),
        q_rot.reshape(rows * HEADS, ROPE),
        page_keys,
        group,
        group_rot,
        lo,
        hi,
        blocks * rows,
    ).reshape(
        HEADS, rows, LAT
    )
    head_out = (
        jnp.einsum(
            "htl,lhn->thn",
            mixed,
            value_up.reshape(LAT, HEADS, NOPE),
            preferred_element_type=jnp.float32,
        )
        .astype(jnp.bfloat16)
        .reshape(rows, HEADS * NOPE)
    )
    residual = hidden_in.astype(jnp.float32) + jnp.dot(
        head_out, out_weight, preferred_element_type=jnp.float32
    )
    normed = rms_scale(residual, ffn_gain).astype(jnp.bfloat16)
    logits = jnp.dot(normed, router_weight, preferred_element_type=jnp.float32)
    hits = expert_ids[..., None] == jnp.arange(EXPERTS, dtype=jnp.int32)
    chosen = jnp.sum(jnp.where(hits, logits[:, None, :], 0.0), axis=-1)
    gates = jax.nn.softmax(chosen, axis=-1)
    flat_hits = hits.reshape(rows * TOPK, EXPERTS).astype(jnp.int32)
    slot = jnp.sum((jnp.cumsum(flat_hits, axis=0) - flat_hits) * flat_hits, axis=-1).reshape(
        rows, TOPK
    )
    column = jnp.arange(EXPERTS * SPLIT * CAP, dtype=jnp.int32)
    first = expert_ids * (SPLIT * CAP) + slot
    match = jnp.zeros((EXPERTS * SPLIT * CAP, rows, TOPK), dtype=bool)
    for half in range(SPLIT):
        match = match | ((first + half * CAP)[None, :, :] == column[:, None, None])
    selector = jnp.any(match, axis=-1).astype(jnp.bfloat16).reshape(EXPERTS * SPLIT, CAP, rows)
    cut = CAP // 2
    parts = []
    for lo_slot, hi_slot in ((0, cut), (cut, CAP)):
        outgoing = (
            jnp.dot(
                selector[:, lo_slot:hi_slot].reshape(-1, rows),
                normed,
                preferred_element_type=jnp.float32,
            )
            .astype(jnp.bfloat16)
            .reshape(EXPERTS * SPLIT, hi_slot - lo_slot, D)
        )
        sent = lax.all_to_all(outgoing, ("req", "wide"), split_axis=0, concat_axis=0, tiled=True)
        worked = expert_rows(sent, gate_pieces, up_pieces, down_pieces)
        parts.append(
            lax.all_to_all(worked, ("req", "wide"), split_axis=0, concat_axis=0, tiled=True)
        )
    weight = jnp.sum(jnp.where(match.transpose(1, 0, 2), gates[:, None, :], 0.0), axis=-1)
    weight_hi = weight.astype(jnp.bfloat16)
    weight_lo = (weight - weight_hi.astype(jnp.float32)).astype(jnp.bfloat16)
    routed = jnp.zeros((rows, D), jnp.float32)
    bounds = ((0, cut), (cut, CAP))
    stacked = jnp.concatenate([weight_hi, weight_lo], axis=0).reshape(
        2 * rows, EXPERTS * SPLIT, CAP
    )
    for (lo_slot, hi_slot), part in zip(bounds, parts):
        both = jnp.dot(
            stacked[:, :, lo_slot:hi_slot].reshape(2 * rows, -1),
            part.reshape(-1, D),
            preferred_element_type=jnp.float32,
        )
        routed = routed + (both[:rows] + both[rows:])
    return ((residual + routed).astype(jnp.bfloat16), suffix_cache)


def solution(mesh):
    return jax.shard_map(
        on_device,
        mesh=mesh,
        in_specs=(
            P(("req", "wide"), None),
            P(("req", "wide"), None),
            P(),
            P(),
            P(),
            P(),
            P(),
            P(),
            P(),
            P(("req", "wide"), None, None),
            P(("req", "wide"), None, None),
            P(("req", "wide"), None, None),
            P("req", None, None),
            P("req", None, None),
            P(),
            P("req", "wide"),
            P(("req", "wide"), None),
        ),
        out_specs=(P(("req", "wide"), None), P(("req", "wide"), None)),
        check_vma=False,
    )
```

```python
import functools
import math

import jax
import jax.numpy as jnp
from jax import lax
from jax.experimental import pallas as pl
from jax.experimental.pallas import tpu as pltpu
from jax.sharding import PartitionSpec as P

D = 2048
HEADS = 16
NOPE = 128
ROPE = 64
LAT = 512
EXPERTS = 64
TOPK = 6
SPLIT = 2
PAGE = 128
CAP = 14
MOST_LEN = 1024


EPS = 1e-06
NEG = -1e30


def rotary(values, positions):
    half = values.shape[-1] // 2
    freqs = 10000.0 ** (-2.0 * jnp.arange(half, dtype=jnp.float32) / values.shape[-1])
    angles = positions.astype(jnp.float32)[:, None] * freqs[None, :]
    shape = (positions.shape[0],) + (1,) * (values.ndim - 2) + (half,)
    cosine = jnp.cos(angles).reshape(shape)
    sine = jnp.sin(angles).reshape(shape)
    first = values[..., :half]
    second = values[..., half:]
    return jnp.concatenate(
        [first * cosine - second * sine, second * cosine + first * sine], axis=-1
    )


def rms_scale(values, gain):
    return values * lax.rsqrt(jnp.mean(values * values, axis=-1, keepdims=True) + EPS) * gain


def offsets(segments):
    length = segments.shape[0]
    index = jnp.arange(length, dtype=jnp.int32)
    fresh = jnp.concatenate([jnp.ones((1,), dtype=bool), segments[1:] != segments[:-1]])
    starts = lax.cummax(jnp.where(fresh, index, 0), axis=0)
    return index - starts


def page_positions(page_table, slots):
    logical = jnp.sum(
        jnp.where(
            page_table[None, :] == slots[:, None],
            jnp.arange(page_table.shape[0], dtype=jnp.int32)[None, :],
            0,
        ),
        axis=1,
    )
    return (logical[:, None] * PAGE + jnp.arange(PAGE, dtype=jnp.int32)[None, :]).reshape(-1)


def attend_kernel(
    base_ref, ql_ref, qr_ref, kp_ref, kl_ref, kr_ref, lo_ref, hi_ref, out_ref, *, window, scale
):
    base = pl.multiple_of(base_ref[0], 128)
    lat = out_ref.shape[1]
    q = jnp.concatenate([ql_ref[...], qr_ref[...]], axis=1)
    kp = kp_ref[...]
    k_lat = kl_ref[pl.ds(base, window), :lat]
    k_rot = kr_ref[...]
    dims = (((1,), (1,)), ((), ()))
    s_p = lax.dot_general(q, kp, dims, preferred_element_type=jnp.float32) * scale
    s_s = (
        lax.dot_general(ql_ref[...], k_lat, dims, preferred_element_type=jnp.float32)
        + lax.dot_general(qr_ref[...], k_rot, dims, preferred_element_type=jnp.float32)
    ) * scale
    copies = ql_ref.shape[0] // lo_ref.shape[0]
    lo = jnp.concatenate([lo_ref[...]] * copies, axis=0)
    hi = jnp.concatenate([hi_ref[...]] * copies, axis=0)
    kidx = base + lax.broadcasted_iota(jnp.int32, (1, window), 1)
    allowed = (kidx >= lo) & (kidx <= hi)
    s_s = jnp.where(allowed, s_s, NEG)
    top = jnp.maximum(jnp.max(s_p, axis=1, keepdims=True), jnp.max(s_s, axis=1, keepdims=True))
    w_p = jnp.exp(s_p - top)
    w_s = jnp.exp(s_s - top)
    total = jnp.sum(w_p, axis=1, keepdims=True) + jnp.sum(w_s, axis=1, keepdims=True)
    accum = jnp.dot(w_p.astype(jnp.bfloat16), kp, preferred_element_type=jnp.float32)[:, :lat] + jnp.dot(
        w_s.astype(jnp.bfloat16), k_lat, preferred_element_type=jnp.float32
    )
    out_ref[...] = (accum / total).astype(out_ref.dtype)


def attend(base, q_lat, q_rot, kp, k_lat, k_rot, lo, hi, window, block=256):
    rows = q_lat.shape[0]
    return pl.pallas_call(
        functools.partial(attend_kernel, window=window, scale=1.0 / math.sqrt(NOPE + ROPE)),
        grid_spec=pltpu.PrefetchScalarGridSpec(
            num_scalar_prefetch=1,
            grid=(rows // block,),
            in_specs=[
                pl.BlockSpec((block, LAT), lambda i, b: (i, 0)),
                pl.BlockSpec((block, ROPE), lambda i, b: (i, 0)),
                pl.BlockSpec(kp.shape, lambda i, b: (0, 0)),
                pl.BlockSpec(k_lat.shape, lambda i, b: (0, 0)),
                pl.BlockSpec(k_rot.shape, lambda i, b: (0, 0)),
                pl.BlockSpec(lo.shape, lambda i, b: (0, 0)),
                pl.BlockSpec(hi.shape, lambda i, b: (0, 0)),
            ],
            out_specs=pl.BlockSpec((block, LAT), lambda i, b: (i, 0)),
        ),
        out_shape=jax.ShapeDtypeStruct((rows, LAT), jnp.bfloat16),
    )(base, q_lat, q_rot, kp, k_lat, k_rot, lo, hi)


def expert_rows(received, gate_pieces, up_pieces, down_pieces):
    owned = gate_pieces.shape[0]
    grid = received.reshape(-1, owned, received.shape[1], received.shape[2])
    gate = jnp.einsum("spkd,pdf->spkf", grid, gate_pieces, preferred_element_type=jnp.float32)
    upper = jnp.einsum("spkd,pdf->spkf", grid, up_pieces, preferred_element_type=jnp.float32)
    active = (jax.nn.silu(gate) * upper).astype(jnp.bfloat16)
    output = jnp.einsum(
        "spkf,pfd->spkd", active, down_pieces, preferred_element_type=jnp.float32
    ).astype(jnp.bfloat16)
    return output.reshape(received.shape)


def on_device(
    hidden_in,
    queries,
    latent_weight,
    latent_gain,
    key_up,
    value_up,
    out_weight,
    ffn_gain,
    router_weight,
    gate_pieces,
    up_pieces,
    down_pieces,
    prefix_latent,
    prefix_rope,
    page_table,
    segment_ids,
    expert_ids,
):
    rows = hidden_in.shape[0]
    n_wide = lax.axis_size("wide")
    wide_at = lax.axis_index("wide")
    my_start = wide_at * rows
    prefix_len = prefix_latent.shape[0] * lax.axis_size("req") * PAGE
    slots = lax.axis_index("req") * prefix_latent.shape[0] + jnp.arange(
        prefix_latent.shape[0], dtype=jnp.int32
    )
    key_pos = page_positions(page_table, slots)
    own_rot = rotary(prefix_rope.reshape(-1, ROPE).astype(jnp.float32), key_pos).astype(jnp.bfloat16)
    own_keys = jnp.concatenate([prefix_latent.reshape(-1, LAT), own_rot], axis=1)
    page_keys = lax.all_gather(own_keys, "req", axis=0, tiled=True)
    raw = jnp.dot(hidden_in, latent_weight, preferred_element_type=jnp.float32)
    latent = rms_scale(raw[:, :LAT], latent_gain).astype(jnp.bfloat16)
    key_rope = raw[:, LAT:].astype(jnp.bfloat16)
    suffix_cache = jnp.concatenate([latent, key_rope], axis=1)
    tag = jnp.broadcast_to(segment_ids.reshape(rows, 1).astype(jnp.bfloat16), (rows, ROPE))
    group = lax.all_gather(
        jnp.concatenate([suffix_cache, tag], axis=1), "wide", axis=0, tiled=True
    )
    split_q = queries.reshape(rows, HEADS, NOPE + ROPE)
    q_lat = jnp.einsum(
        "thn,lhn->htl",
        split_q[..., :NOPE],
        key_up.reshape(LAT, HEADS, NOPE),
        preferred_element_type=jnp.float32,
    ).astype(jnp.bfloat16)
    hits = expert_ids[..., None] == jnp.arange(EXPERTS, dtype=jnp.int32)
    flat_hits = hits.reshape(rows * TOPK, EXPERTS).astype(jnp.int32)
    slot = jnp.sum((jnp.cumsum(flat_hits, axis=0) - flat_hits) * flat_hits, axis=-1).reshape(
        rows, TOPK
    )
    column = jnp.arange(EXPERTS * SPLIT * CAP, dtype=jnp.int32)
    first = expert_ids * (SPLIT * CAP) + slot
    match = jnp.zeros((EXPERTS * SPLIT * CAP, rows, TOPK), dtype=bool)
    for half in range(SPLIT):
        match = match | ((first + half * CAP)[None, :, :] == column[:, None, None])
    selector = jnp.any(match, axis=-1).astype(jnp.bfloat16).reshape(EXPERTS * SPLIT, CAP, rows)
    group, q_lat, selector = lax.optimization_barrier((group, q_lat, selector))
    group_seg = group[:, LAT + ROPE].astype(jnp.int32)
    group_pos = prefix_len + offsets(group_seg)
    index_q = my_start + jnp.arange(rows, dtype=jnp.int32)
    position = lax.dynamic_slice_in_dim(group_pos, my_start, rows, 0)
    q_rot = (
        rotary(split_q[..., NOPE:].astype(jnp.float32), position)
        .astype(jnp.bfloat16)
        .transpose(1, 0, 2)
    )
    reach = -(-(MOST_LEN - 1) // rows) + 1
    blocks = min(n_wide, reach)
    base = (jnp.maximum(wide_at - (blocks - 1), 0) * rows).astype(jnp.int32).reshape(1)
    window_rope = lax.dynamic_slice_in_dim(group[:, LAT : LAT + ROPE], base[0], blocks * rows, 0)
    window_pos = lax.dynamic_slice_in_dim(group_pos, base[0], blocks * rows, 0)
    group_rot = rotary(window_rope.astype(jnp.float32), window_pos).astype(jnp.bfloat16)
    lo = (index_q - (position - prefix_len))[:, None]
    hi = index_q[:, None]
    mixed = attend(
        base,
        q_lat.reshape(rows * HEADS, LAT),
        q_rot.reshape(rows * HEADS, ROPE),
        page_keys,
        group,
        group_rot,
        lo,
        hi,
        blocks * rows,
    ).reshape(
        HEADS, rows, LAT
    )
    head_out = (
        jnp.einsum(
            "htl,lhn->thn",
            mixed,
            value_up.reshape(LAT, HEADS, NOPE),
            preferred_element_type=jnp.float32,
        )
        .astype(jnp.bfloat16)
        .reshape(rows, HEADS * NOPE)
    )
    residual = hidden_in.astype(jnp.float32) + jnp.dot(
        head_out, out_weight, preferred_element_type=jnp.float32
    )
    normed = rms_scale(residual, ffn_gain).astype(jnp.bfloat16)
    logits = jnp.dot(normed, router_weight, preferred_element_type=jnp.float32)
    chosen = jnp.sum(jnp.where(hits, logits[:, None, :], 0.0), axis=-1)
    gates = jax.nn.softmax(chosen, axis=-1)
    cut = CAP // 2
    parts = []
    for lo_slot, hi_slot in ((0, cut), (cut, CAP)):
        outgoing = (
            jnp.dot(
                selector[:, lo_slot:hi_slot].reshape(-1, rows),
                normed,
                preferred_element_type=jnp.float32,
            )
            .astype(jnp.bfloat16)
            .reshape(EXPERTS * SPLIT, hi_slot - lo_slot, D)
        )
        sent = lax.all_to_all(outgoing, ("req", "wide"), split_axis=0, concat_axis=0, tiled=True)
        worked = expert_rows(sent, gate_pieces, up_pieces, down_pieces)
        parts.append(
            lax.all_to_all(worked, ("req", "wide"), split_axis=0, concat_axis=0, tiled=True)
        )
    weight = jnp.sum(jnp.where(match.transpose(1, 0, 2), gates[:, None, :], 0.0), axis=-1)
    weight_hi = weight.astype(jnp.bfloat16)
    weight_lo = (weight - weight_hi.astype(jnp.float32)).astype(jnp.bfloat16)
    routed = jnp.zeros((rows, D), jnp.float32)
    bounds = ((0, cut), (cut, CAP))
    stacked = jnp.concatenate([weight_hi, weight_lo], axis=0).reshape(
        2 * rows, EXPERTS * SPLIT, CAP
    )
    for (lo_slot, hi_slot), part in zip(bounds, parts):
        both = jnp.dot(
            stacked[:, :, lo_slot:hi_slot].reshape(2 * rows, -1),
            part.reshape(-1, D),
            preferred_element_type=jnp.float32,
        )
        routed = routed + (both[:rows] + both[rows:])
    return ((residual + routed).astype(jnp.bfloat16), suffix_cache)


def solution(mesh):
    return jax.shard_map(
        on_device,
        mesh=mesh,
        in_specs=(
            P(("req", "wide"), None),
            P(("req", "wide"), None),
            P(),
            P(),
            P(),
            P(),
            P(),
            P(),
            P(),
            P(("req", "wide"), None, None),
            P(("req", "wide"), None, None),
            P(("req", "wide"), None, None),
            P("req", None, None),
            P("req", None, None),
            P(),
            P("req", "wide"),
            P(("req", "wide"), None),
        ),
        out_specs=(P(("req", "wide"), None), P(("req", "wide"), None)),
        check_vma=False,
    )
```

```python
import functools
import math

import jax
import jax.numpy as jnp
from jax import lax
from jax.experimental import pallas as pl
from jax.experimental.pallas import tpu as pltpu
from jax.sharding import PartitionSpec as P

D = 2048
HEADS = 16
NOPE = 128
ROPE = 64
LAT = 512
EXPERTS = 64
TOPK = 6
SPLIT = 2
PAGE = 128
CAP = 14
MOST_LEN = 1024


EPS = 1e-06
NEG = -1e30


def rotary(values, positions):
    half = values.shape[-1] // 2
    freqs = 10000.0 ** (-2.0 * jnp.arange(half, dtype=jnp.float32) / values.shape[-1])
    angles = positions.astype(jnp.float32)[:, None] * freqs[None, :]
    shape = (positions.shape[0],) + (1,) * (values.ndim - 2) + (half,)
    cosine = jnp.cos(angles).reshape(shape)
    sine = jnp.sin(angles).reshape(shape)
    first = values[..., :half]
    second = values[..., half:]
    return jnp.concatenate(
        [first * cosine - second * sine, second * cosine + first * sine], axis=-1
    )


def rms_scale(values, gain):
    return values * lax.rsqrt(jnp.mean(values * values, axis=-1, keepdims=True) + EPS) * gain


def offsets(segments):
    length = segments.shape[0]
    index = jnp.arange(length, dtype=jnp.int32)
    fresh = jnp.concatenate([jnp.ones((1,), dtype=bool), segments[1:] != segments[:-1]])
    starts = lax.cummax(jnp.where(fresh, index, 0), axis=0)
    return index - starts


def page_positions(page_table, slots):
    logical = jnp.sum(
        jnp.where(
            page_table[None, :] == slots[:, None],
            jnp.arange(page_table.shape[0], dtype=jnp.int32)[None, :],
            0,
        ),
        axis=1,
    )
    return (logical[:, None] * PAGE + jnp.arange(PAGE, dtype=jnp.int32)[None, :]).reshape(-1)


def attend_kernel(
    base_ref, ql_ref, qr_ref, kp_ref, kl_ref, kr_ref, lo_ref, hi_ref, out_ref, *, window, scale
):
    base = pl.multiple_of(base_ref[0], 128)
    lat = out_ref.shape[1]
    q = jnp.concatenate([ql_ref[...], qr_ref[...]], axis=1)
    kp = kp_ref[...]
    k_lat = kl_ref[pl.ds(base, window), :lat]
    k_rot = kr_ref[...]
    dims = (((1,), (1,)), ((), ()))
    s_p = lax.dot_general(q, kp, dims, preferred_element_type=jnp.float32) * scale
    s_s = (
        lax.dot_general(ql_ref[...], k_lat, dims, preferred_element_type=jnp.float32)
        + lax.dot_general(qr_ref[...], k_rot, dims, preferred_element_type=jnp.float32)
    ) * scale
    copies = ql_ref.shape[0] // lo_ref.shape[0]
    lo = jnp.concatenate([lo_ref[...]] * copies, axis=0)
    hi = jnp.concatenate([hi_ref[...]] * copies, axis=0)
    kidx = base + lax.broadcasted_iota(jnp.int32, (1, window), 1)
    allowed = (kidx >= lo) & (kidx <= hi)
    s_s = jnp.where(allowed, s_s, NEG)
    top = jnp.maximum(jnp.max(s_p, axis=1, keepdims=True), jnp.max(s_s, axis=1, keepdims=True))
    w_p = jnp.exp(s_p - top)
    w_s = jnp.exp(s_s - top)
    total = jnp.sum(w_p, axis=1, keepdims=True) + jnp.sum(w_s, axis=1, keepdims=True)
    accum = jnp.dot(w_p.astype(jnp.bfloat16), kp, preferred_element_type=jnp.float32)[:, :lat] + jnp.dot(
        w_s.astype(jnp.bfloat16), k_lat, preferred_element_type=jnp.float32
    )
    out_ref[...] = (accum / total).astype(out_ref.dtype)


def attend(base, q_lat, q_rot, kp, k_lat, k_rot, lo, hi, window, block=256):
    rows = q_lat.shape[0]
    return pl.pallas_call(
        functools.partial(attend_kernel, window=window, scale=1.0 / math.sqrt(NOPE + ROPE)),
        grid_spec=pltpu.PrefetchScalarGridSpec(
            num_scalar_prefetch=1,
            grid=(rows // block,),
            in_specs=[
                pl.BlockSpec((block, LAT), lambda i, b: (i, 0)),
                pl.BlockSpec((block, ROPE), lambda i, b: (i, 0)),
                pl.BlockSpec(kp.shape, lambda i, b: (0, 0)),
                pl.BlockSpec(k_lat.shape, lambda i, b: (0, 0)),
                pl.BlockSpec(k_rot.shape, lambda i, b: (0, 0)),
                pl.BlockSpec(lo.shape, lambda i, b: (0, 0)),
                pl.BlockSpec(hi.shape, lambda i, b: (0, 0)),
            ],
            out_specs=pl.BlockSpec((block, LAT), lambda i, b: (i, 0)),
        ),
        out_shape=jax.ShapeDtypeStruct((rows, LAT), jnp.bfloat16),
    )(base, q_lat, q_rot, kp, k_lat, k_rot, lo, hi)


def expert_rows(received, gate_pieces, up_pieces, down_pieces):
    owned = gate_pieces.shape[0]
    grid = received.reshape(-1, owned, received.shape[1], received.shape[2])
    gate = jnp.einsum("spkd,pdf->spkf", grid, gate_pieces, preferred_element_type=jnp.float32)
    upper = jnp.einsum("spkd,pdf->spkf", grid, up_pieces, preferred_element_type=jnp.float32)
    active = (jax.nn.silu(gate) * upper).astype(jnp.bfloat16)
    output = jnp.einsum(
        "spkf,pfd->spkd", active, down_pieces, preferred_element_type=jnp.float32
    ).astype(jnp.bfloat16)
    return output.reshape(received.shape)


def on_device(
    hidden_in,
    queries,
    latent_weight,
    latent_gain,
    key_up,
    value_up,
    out_weight,
    ffn_gain,
    router_weight,
    gate_pieces,
    up_pieces,
    down_pieces,
    prefix_latent,
    prefix_rope,
    page_table,
    segment_ids,
    expert_ids,
):
    rows = hidden_in.shape[0]
    n_wide = lax.axis_size("wide")
    wide_at = lax.axis_index("wide")
    my_start = wide_at * rows
    prefix_len = prefix_latent.shape[0] * lax.axis_size("req") * PAGE
    slots = lax.axis_index("req") * prefix_latent.shape[0] + jnp.arange(
        prefix_latent.shape[0], dtype=jnp.int32
    )
    key_pos = page_positions(page_table, slots)
    own_rot = rotary(prefix_rope.reshape(-1, ROPE).astype(jnp.float32), key_pos).astype(jnp.bfloat16)
    own_keys = jnp.concatenate([prefix_latent.reshape(-1, LAT), own_rot], axis=1)
    page_keys = lax.all_gather(own_keys, "req", axis=0, tiled=True)
    raw = jnp.dot(hidden_in, latent_weight, preferred_element_type=jnp.float32)
    latent = rms_scale(raw[:, :LAT], latent_gain).astype(jnp.bfloat16)
    key_rope = raw[:, LAT:].astype(jnp.bfloat16)
    suffix_cache = jnp.concatenate([latent, key_rope], axis=1)
    tag = jnp.broadcast_to(segment_ids.reshape(rows, 1).astype(jnp.bfloat16), (rows, ROPE))
    group = lax.all_gather(
        jnp.concatenate([suffix_cache, tag], axis=1), "wide", axis=0, tiled=True
    )
    split_q = queries.reshape(rows, HEADS, NOPE + ROPE)
    q_lat = jnp.einsum(
        "thn,lhn->htl",
        split_q[..., :NOPE],
        key_up.reshape(LAT, HEADS, NOPE),
        preferred_element_type=jnp.float32,
    ).astype(jnp.bfloat16)
    hits = expert_ids[..., None] == jnp.arange(EXPERTS, dtype=jnp.int32)
    flat_hits = hits.reshape(rows * TOPK, EXPERTS).astype(jnp.int32)
    slot = jnp.sum((jnp.cumsum(flat_hits, axis=0) - flat_hits) * flat_hits, axis=-1).reshape(
        rows, TOPK
    )
    column = jnp.arange(EXPERTS * SPLIT * CAP, dtype=jnp.int32)
    first = expert_ids * (SPLIT * CAP) + slot
    match = jnp.zeros((EXPERTS * SPLIT * CAP, rows, TOPK), dtype=bool)
    for half in range(SPLIT):
        match = match | ((first + half * CAP)[None, :, :] == column[:, None, None])
    selector = jnp.any(match, axis=-1).astype(jnp.bfloat16).reshape(EXPERTS * SPLIT, CAP, rows)
    cut = CAP // 2
    bounds = ((0, cut), (cut, CAP))
    picks = tuple(selector[:, a:b].reshape(-1, rows) for a, b in bounds)
    value_heads = value_up.reshape(LAT, HEADS, NOPE).transpose(1, 0, 2)
    group, q_lat, picks, value_heads = lax.optimization_barrier((group, q_lat, picks, value_heads))
    group_seg = group[:, LAT + ROPE].astype(jnp.int32)
    group_pos = prefix_len + offsets(group_seg)
    index_q = my_start + jnp.arange(rows, dtype=jnp.int32)
    position = lax.dynamic_slice_in_dim(group_pos, my_start, rows, 0)
    q_rot = (
        rotary(split_q[..., NOPE:].astype(jnp.float32), position)
        .astype(jnp.bfloat16)
        .transpose(1, 0, 2)
    )
    reach = -(-(MOST_LEN - 1) // rows) + 1
    blocks = min(n_wide, reach)
    base = (jnp.maximum(wide_at - (blocks - 1), 0) * rows).astype(jnp.int32).reshape(1)
    window_rope = lax.dynamic_slice_in_dim(group[:, LAT : LAT + ROPE], base[0], blocks * rows, 0)
    window_pos = lax.dynamic_slice_in_dim(group_pos, base[0], blocks * rows, 0)
    group_rot = rotary(window_rope.astype(jnp.float32), window_pos).astype(jnp.bfloat16)
    lo = (index_q - (position - prefix_len))[:, None]
    hi = index_q[:, None]
    mixed = attend(
        base,
        q_lat.reshape(rows * HEADS, LAT),
        q_rot.reshape(rows * HEADS, ROPE),
        page_keys,
        group,
        group_rot,
        lo,
        hi,
        blocks * rows,
    ).reshape(
        HEADS, rows, LAT
    )
    head_out = (
        jnp.einsum(
            "htl,hln->thn",
            mixed,
            value_heads,
            preferred_element_type=jnp.float32,
        )
        .astype(jnp.bfloat16)
        .reshape(rows, HEADS * NOPE)
    )
    residual = hidden_in.astype(jnp.float32) + jnp.dot(
        head_out, out_weight, preferred_element_type=jnp.float32
    )
    normed = rms_scale(residual, ffn_gain).astype(jnp.bfloat16)
    logits = jnp.dot(normed, router_weight, preferred_element_type=jnp.float32)
    chosen = jnp.sum(jnp.where(hits, logits[:, None, :], 0.0), axis=-1)
    gates = jax.nn.softmax(chosen, axis=-1)
    parts = []
    for (lo_slot, hi_slot), pick in zip(bounds, picks):
        outgoing = (
            jnp.dot(
                pick,
                normed,
                preferred_element_type=jnp.float32,
            )
            .astype(jnp.bfloat16)
            .reshape(EXPERTS * SPLIT, hi_slot - lo_slot, D)
        )
        sent = lax.all_to_all(outgoing, ("req", "wide"), split_axis=0, concat_axis=0, tiled=True)
        worked = expert_rows(sent, gate_pieces, up_pieces, down_pieces)
        parts.append(
            lax.all_to_all(worked, ("req", "wide"), split_axis=0, concat_axis=0, tiled=True)
        )
    weight = jnp.sum(jnp.where(match.transpose(1, 0, 2), gates[:, None, :], 0.0), axis=-1)
    weight_hi = weight.astype(jnp.bfloat16)
    weight_lo = (weight - weight_hi.astype(jnp.float32)).astype(jnp.bfloat16)
    routed = jnp.zeros((rows, D), jnp.float32)
    stacked = jnp.concatenate([weight_hi, weight_lo], axis=0).reshape(
        2 * rows, EXPERTS * SPLIT, CAP
    )
    for (lo_slot, hi_slot), part in zip(bounds, parts):
        both = jnp.dot(
            stacked[:, :, lo_slot:hi_slot].reshape(2 * rows, -1),
            part.reshape(-1, D),
            preferred_element_type=jnp.float32,
        )
        routed = routed + (both[:rows] + both[rows:])
    return ((residual + routed).astype(jnp.bfloat16), suffix_cache)


def solution(mesh):
    return jax.shard_map(
        on_device,
        mesh=mesh,
        in_specs=(
            P(("req", "wide"), None),
            P(("req", "wide"), None),
            P(),
            P(),
            P(),
            P(),
            P(),
            P(),
            P(),
            P(("req", "wide"), None, None),
            P(("req", "wide"), None, None),
            P(("req", "wide"), None, None),
            P("req", None, None),
            P("req", None, None),
            P(),
            P("req", "wide"),
            P(("req", "wide"), None),
        ),
        out_specs=(P(("req", "wide"), None), P(("req", "wide"), None)),
        check_vma=False,
    )
```

```python
import functools
import math

import jax
import jax.numpy as jnp
from jax import lax
from jax.experimental import pallas as pl
from jax.experimental.pallas import tpu as pltpu
from jax.sharding import PartitionSpec as P

D = 2048
HEADS = 16
NOPE = 128
ROPE = 64
LAT = 512
EXPERTS = 64
TOPK = 6
SPLIT = 2
PAGE = 128
CAP = 14
MOST_LEN = 1024


EPS = 1e-06
NEG = -1e30


def rotary(values, positions):
    half = values.shape[-1] // 2
    freqs = 10000.0 ** (-2.0 * jnp.arange(half, dtype=jnp.float32) / values.shape[-1])
    angles = positions.astype(jnp.float32)[:, None] * freqs[None, :]
    shape = (positions.shape[0],) + (1,) * (values.ndim - 2) + (half,)
    cosine = jnp.cos(angles).reshape(shape)
    sine = jnp.sin(angles).reshape(shape)
    first = values[..., :half]
    second = values[..., half:]
    return jnp.concatenate(
        [first * cosine - second * sine, second * cosine + first * sine], axis=-1
    )


def rms_scale(values, gain):
    return values * lax.rsqrt(jnp.mean(values * values, axis=-1, keepdims=True) + EPS) * gain


def offsets(segments):
    length = segments.shape[0]
    index = jnp.arange(length, dtype=jnp.int32)
    fresh = jnp.concatenate([jnp.ones((1,), dtype=bool), segments[1:] != segments[:-1]])
    starts = lax.cummax(jnp.where(fresh, index, 0), axis=0)
    return index - starts


def page_positions(page_table, slots):
    logical = jnp.sum(
        jnp.where(
            page_table[None, :] == slots[:, None],
            jnp.arange(page_table.shape[0], dtype=jnp.int32)[None, :],
            0,
        ),
        axis=1,
    )
    return (logical[:, None] * PAGE + jnp.arange(PAGE, dtype=jnp.int32)[None, :]).reshape(-1)


def attend_kernel(
    base_ref, ql_ref, qr_ref, kp_ref, kl_ref, kr_ref, lo_ref, hi_ref, out_ref, *, window, scale
):
    base = pl.multiple_of(base_ref[0], 128)
    lat = out_ref.shape[1]
    q = jnp.concatenate([ql_ref[...], qr_ref[...]], axis=1)
    kp = kp_ref[...]
    k_lat = kl_ref[pl.ds(base, window), :lat]
    k_rot = kr_ref[...]
    dims = (((1,), (1,)), ((), ()))
    s_p = lax.dot_general(q, kp, dims, preferred_element_type=jnp.float32) * scale
    s_s = (
        lax.dot_general(ql_ref[...], k_lat, dims, preferred_element_type=jnp.float32)
        + lax.dot_general(qr_ref[...], k_rot, dims, preferred_element_type=jnp.float32)
    ) * scale
    copies = ql_ref.shape[0] // lo_ref.shape[0]
    lo = jnp.concatenate([lo_ref[...]] * copies, axis=0)
    hi = jnp.concatenate([hi_ref[...]] * copies, axis=0)
    kidx = base + lax.broadcasted_iota(jnp.int32, (1, window), 1)
    allowed = (kidx >= lo) & (kidx <= hi)
    s_s = jnp.where(allowed, s_s, NEG)
    top = jnp.maximum(jnp.max(s_p, axis=1, keepdims=True), jnp.max(s_s, axis=1, keepdims=True))
    w_p = jnp.exp(s_p - top)
    w_s = jnp.exp(s_s - top)
    total = jnp.sum(w_p, axis=1, keepdims=True) + jnp.sum(w_s, axis=1, keepdims=True)
    accum = jnp.dot(w_p.astype(jnp.bfloat16), kp, preferred_element_type=jnp.float32)[:, :lat] + jnp.dot(
        w_s.astype(jnp.bfloat16), k_lat, preferred_element_type=jnp.float32
    )
    out_ref[...] = (accum / total).astype(out_ref.dtype)


def attend(base, q_lat, q_rot, kp, k_lat, k_rot, lo, hi, window, block=512):
    rows = q_lat.shape[0]
    return pl.pallas_call(
        functools.partial(attend_kernel, window=window, scale=1.0 / math.sqrt(NOPE + ROPE)),
        grid_spec=pltpu.PrefetchScalarGridSpec(
            num_scalar_prefetch=1,
            grid=(rows // block,),
            in_specs=[
                pl.BlockSpec((block, LAT), lambda i, b: (i, 0)),
                pl.BlockSpec((block, ROPE), lambda i, b: (i, 0)),
                pl.BlockSpec(kp.shape, lambda i, b: (0, 0)),
                pl.BlockSpec(k_lat.shape, lambda i, b: (0, 0)),
                pl.BlockSpec(k_rot.shape, lambda i, b: (0, 0)),
                pl.BlockSpec(lo.shape, lambda i, b: (0, 0)),
                pl.BlockSpec(hi.shape, lambda i, b: (0, 0)),
            ],
            out_specs=pl.BlockSpec((block, LAT), lambda i, b: (i, 0)),
        ),
        out_shape=jax.ShapeDtypeStruct((rows, LAT), jnp.bfloat16),
    )(base, q_lat, q_rot, kp, k_lat, k_rot, lo, hi)


def expert_rows(received, gate_pieces, up_pieces, down_pieces):
    owned = gate_pieces.shape[0]
    grid = received.reshape(-1, owned, received.shape[1], received.shape[2])
    gate = jnp.einsum("spkd,pdf->spkf", grid, gate_pieces, preferred_element_type=jnp.float32)
    upper = jnp.einsum("spkd,pdf->spkf", grid, up_pieces, preferred_element_type=jnp.float32)
    active = (jax.nn.silu(gate) * upper).astype(jnp.bfloat16)
    output = jnp.einsum(
        "spkf,pfd->spkd", active, down_pieces, preferred_element_type=jnp.float32
    ).astype(jnp.bfloat16)
    return output.reshape(received.shape)


def on_device(
    hidden_in,
    queries,
    latent_weight,
    latent_gain,
    key_up,
    value_up,
    out_weight,
    ffn_gain,
    router_weight,
    gate_pieces,
    up_pieces,
    down_pieces,
    prefix_latent,
    prefix_rope,
    page_table,
    segment_ids,
    expert_ids,
):
    rows = hidden_in.shape[0]
    n_wide = lax.axis_size("wide")
    wide_at = lax.axis_index("wide")
    my_start = wide_at * rows
    prefix_len = prefix_latent.shape[0] * lax.axis_size("req") * PAGE
    slots = lax.axis_index("req") * prefix_latent.shape[0] + jnp.arange(
        prefix_latent.shape[0], dtype=jnp.int32
    )
    key_pos = page_positions(page_table, slots)
    own_rot = rotary(prefix_rope.reshape(-1, ROPE).astype(jnp.float32), key_pos).astype(jnp.bfloat16)
    own_keys = jnp.concatenate([prefix_latent.reshape(-1, LAT), own_rot], axis=1)
    page_keys = lax.all_gather(own_keys, "req", axis=0, tiled=True)
    raw = jnp.dot(hidden_in, latent_weight, preferred_element_type=jnp.float32)
    latent = rms_scale(raw[:, :LAT], latent_gain).astype(jnp.bfloat16)
    key_rope = raw[:, LAT:].astype(jnp.bfloat16)
    suffix_cache = jnp.concatenate([latent, key_rope], axis=1)
    tag = jnp.broadcast_to(segment_ids.reshape(rows, 1).astype(jnp.bfloat16), (rows, ROPE))
    group = lax.all_gather(
        jnp.concatenate([suffix_cache, tag], axis=1), "wide", axis=0, tiled=True
    )
    split_q = queries.reshape(rows, HEADS, NOPE + ROPE)
    q_lat = jnp.einsum(
        "thn,lhn->htl",
        split_q[..., :NOPE],
        key_up.reshape(LAT, HEADS, NOPE),
        preferred_element_type=jnp.float32,
    ).astype(jnp.bfloat16)
    hits = expert_ids[..., None] == jnp.arange(EXPERTS, dtype=jnp.int32)
    flat_hits = hits.reshape(rows * TOPK, EXPERTS).astype(jnp.int32)
    slot = jnp.sum((jnp.cumsum(flat_hits, axis=0) - flat_hits) * flat_hits, axis=-1).reshape(
        rows, TOPK
    )
    column = jnp.arange(EXPERTS * SPLIT * CAP, dtype=jnp.int32)
    first = expert_ids * (SPLIT * CAP) + slot
    match = jnp.zeros((EXPERTS * SPLIT * CAP, rows, TOPK), dtype=bool)
    for half in range(SPLIT):
        match = match | ((first + half * CAP)[None, :, :] == column[:, None, None])
    selector = jnp.any(match, axis=-1).astype(jnp.bfloat16).reshape(EXPERTS * SPLIT, CAP, rows)
    group, q_lat, selector = lax.optimization_barrier((group, q_lat, selector))
    group_seg = group[:, LAT + ROPE].astype(jnp.int32)
    group_pos = prefix_len + offsets(group_seg)
    index_q = my_start + jnp.arange(rows, dtype=jnp.int32)
    position = lax.dynamic_slice_in_dim(group_pos, my_start, rows, 0)
    q_rot = (
        rotary(split_q[..., NOPE:].astype(jnp.float32), position)
        .astype(jnp.bfloat16)
        .transpose(1, 0, 2)
    )
    reach = -(-(MOST_LEN - 1) // rows) + 1
    blocks = min(n_wide, reach)
    base = (jnp.maximum(wide_at - (blocks - 1), 0) * rows).astype(jnp.int32).reshape(1)
    window_rope = lax.dynamic_slice_in_dim(group[:, LAT : LAT + ROPE], base[0], blocks * rows, 0)
    window_pos = lax.dynamic_slice_in_dim(group_pos, base[0], blocks * rows, 0)
    group_rot = rotary(window_rope.astype(jnp.float32), window_pos).astype(jnp.bfloat16)
    lo = (index_q - (position - prefix_len))[:, None]
    hi = index_q[:, None]
    mixed = attend(
        base,
        q_lat.reshape(rows * HEADS, LAT),
        q_rot.reshape(rows * HEADS, ROPE),
        page_keys,
        group,
        group_rot,
        lo,
        hi,
        blocks * rows,
    ).reshape(
        HEADS, rows, LAT
    )
    head_out = (
        jnp.einsum(
            "htl,lhn->thn",
            mixed,
            value_up.reshape(LAT, HEADS, NOPE),
            preferred_element_type=jnp.float32,
        )
        .astype(jnp.bfloat16)
        .reshape(rows, HEADS * NOPE)
    )
    residual = hidden_in.astype(jnp.float32) + jnp.dot(
        head_out, out_weight, preferred_element_type=jnp.float32
    )
    normed = rms_scale(residual, ffn_gain).astype(jnp.bfloat16)
    logits = jnp.dot(normed, router_weight, preferred_element_type=jnp.float32)
    chosen = jnp.sum(jnp.where(hits, logits[:, None, :], 0.0), axis=-1)
    gates = jax.nn.softmax(chosen, axis=-1)
    cut = CAP // 2
    parts = []
    for lo_slot, hi_slot in ((0, cut), (cut, CAP)):
        outgoing = (
            jnp.dot(
                selector[:, lo_slot:hi_slot].reshape(-1, rows),
                normed,
                preferred_element_type=jnp.float32,
            )
            .astype(jnp.bfloat16)
            .reshape(EXPERTS * SPLIT, hi_slot - lo_slot, D)
        )
        sent = lax.all_to_all(outgoing, ("req", "wide"), split_axis=0, concat_axis=0, tiled=True)
        worked = expert_rows(sent, gate_pieces, up_pieces, down_pieces)
        parts.append(
            lax.all_to_all(worked, ("req", "wide"), split_axis=0, concat_axis=0, tiled=True)
        )
    weight = jnp.sum(jnp.where(match.transpose(1, 0, 2), gates[:, None, :], 0.0), axis=-1)
    weight_hi = weight.astype(jnp.bfloat16)
    weight_lo = (weight - weight_hi.astype(jnp.float32)).astype(jnp.bfloat16)
    routed = jnp.zeros((rows, D), jnp.float32)
    bounds = ((0, cut), (cut, CAP))
    stacked = jnp.concatenate([weight_hi, weight_lo], axis=0).reshape(
        2 * rows, EXPERTS * SPLIT, CAP
    )
    for (lo_slot, hi_slot), part in zip(bounds, parts):
        both = jnp.dot(
            stacked[:, :, lo_slot:hi_slot].reshape(2 * rows, -1),
            part.reshape(-1, D),
            preferred_element_type=jnp.float32,
        )
        routed = routed + (both[:rows] + both[rows:])
    return ((residual + routed).astype(jnp.bfloat16), suffix_cache)


def solution(mesh):
    return jax.shard_map(
        on_device,
        mesh=mesh,
        in_specs=(
            P(("req", "wide"), None),
            P(("req", "wide"), None),
            P(),
            P(),
            P(),
            P(),
            P(),
            P(),
            P(),
            P(("req", "wide"), None, None),
            P(("req", "wide"), None, None),
            P(("req", "wide"), None, None),
            P("req", None, None),
            P("req", None, None),
            P(),
            P("req", "wide"),
            P(("req", "wide"), None),
        ),
        out_specs=(P(("req", "wide"), None), P(("req", "wide"), None)),
        check_vma=False,
    )
```

```python
import functools
import math

import jax
import jax.numpy as jnp
from jax import lax
from jax.experimental import pallas as pl
from jax.experimental.pallas import tpu as pltpu
from jax.sharding import PartitionSpec as P

D = 2048
HEADS = 16
NOPE = 128
ROPE = 64
LAT = 512
EXPERTS = 64
TOPK = 6
SPLIT = 2
PAGE = 128
CAP = 14
MOST_LEN = 1024


EPS = 1e-06
NEG = -1e30


def rotary(values, positions):
    half = values.shape[-1] // 2
    freqs = 10000.0 ** (-2.0 * jnp.arange(half, dtype=jnp.float32) / values.shape[-1])
    angles = positions.astype(jnp.float32)[:, None] * freqs[None, :]
    shape = (positions.shape[0],) + (1,) * (values.ndim - 2) + (half,)
    cosine = jnp.cos(angles).reshape(shape)
    sine = jnp.sin(angles).reshape(shape)
    first = values[..., :half]
    second = values[..., half:]
    return jnp.concatenate(
        [first * cosine - second * sine, second * cosine + first * sine], axis=-1
    )


def rms_scale(values, gain):
    return values * lax.rsqrt(jnp.mean(values * values, axis=-1, keepdims=True) + EPS) * gain


def offsets(segments):
    length = segments.shape[0]
    index = jnp.arange(length, dtype=jnp.int32)
    fresh = jnp.concatenate([jnp.ones((1,), dtype=bool), segments[1:] != segments[:-1]])
    starts = lax.cummax(jnp.where(fresh, index, 0), axis=0)
    return index - starts


def page_positions(page_table, slots):
    logical = jnp.sum(
        jnp.where(
            page_table[None, :] == slots[:, None],
            jnp.arange(page_table.shape[0], dtype=jnp.int32)[None, :],
            0,
        ),
        axis=1,
    )
    return (logical[:, None] * PAGE + jnp.arange(PAGE, dtype=jnp.int32)[None, :]).reshape(-1)


def attend_kernel(
    base_ref, ql_ref, qr_ref, kp_ref, kl_ref, kr_ref, lo_ref, hi_ref, out_ref, *, window, scale
):
    base = pl.multiple_of(base_ref[0], 128)
    lat = out_ref.shape[1]
    ql = ql_ref[...]
    qr = qr_ref[...]
    kp_lat = kp_ref[:, :lat]
    kp_rot = kp_ref[:, lat:]
    k_lat = kl_ref[pl.ds(base, window), :lat]
    k_rot = kr_ref[...]
    dims = (((1,), (1,)), ((), ()))
    s_p = (
        lax.dot_general(ql, kp_lat, dims, preferred_element_type=jnp.float32)
        + lax.dot_general(qr, kp_rot, dims, preferred_element_type=jnp.float32)
    ) * scale
    s_s = (
        lax.dot_general(ql, k_lat, dims, preferred_element_type=jnp.float32)
        + lax.dot_general(qr, k_rot, dims, preferred_element_type=jnp.float32)
    ) * scale
    copies = ql_ref.shape[0] // lo_ref.shape[0]
    lo = jnp.concatenate([lo_ref[...]] * copies, axis=0)
    hi = jnp.concatenate([hi_ref[...]] * copies, axis=0)
    kidx = base + lax.broadcasted_iota(jnp.int32, (1, window), 1)
    allowed = (kidx >= lo) & (kidx <= hi)
    s_s = jnp.where(allowed, s_s, NEG)
    top = jnp.maximum(jnp.max(s_p, axis=1, keepdims=True), jnp.max(s_s, axis=1, keepdims=True))
    w_p = jnp.exp(s_p - top)
    w_s = jnp.exp(s_s - top)
    total = jnp.sum(w_p, axis=1, keepdims=True) + jnp.sum(w_s, axis=1, keepdims=True)
    accum = jnp.dot(w_p.astype(jnp.bfloat16), kp_lat, preferred_element_type=jnp.float32) + jnp.dot(
        w_s.astype(jnp.bfloat16), k_lat, preferred_element_type=jnp.float32
    )
    out_ref[...] = (accum / total).astype(out_ref.dtype)


def attend(base, q_lat, q_rot, kp, k_lat, k_rot, lo, hi, window, block=512):
    rows = q_lat.shape[0]
    return pl.pallas_call(
        functools.partial(attend_kernel, window=window, scale=1.0 / math.sqrt(NOPE + ROPE)),
        grid_spec=pltpu.PrefetchScalarGridSpec(
            num_scalar_prefetch=1,
            grid=(rows // block,),
            in_specs=[
                pl.BlockSpec((block, LAT), lambda i, b: (i, 0)),
                pl.BlockSpec((block, ROPE), lambda i, b: (i, 0)),
                pl.BlockSpec(kp.shape, lambda i, b: (0, 0)),
                pl.BlockSpec(k_lat.shape, lambda i, b: (0, 0)),
                pl.BlockSpec(k_rot.shape, lambda i, b: (0, 0)),
                pl.BlockSpec(lo.shape, lambda i, b: (0, 0)),
                pl.BlockSpec(hi.shape, lambda i, b: (0, 0)),
            ],
            out_specs=pl.BlockSpec((block, LAT), lambda i, b: (i, 0)),
        ),
        out_shape=jax.ShapeDtypeStruct((rows, LAT), jnp.bfloat16),
    )(base, q_lat, q_rot, kp, k_lat, k_rot, lo, hi)


def expert_rows(received, gate_pieces, up_pieces, down_pieces):
    owned = gate_pieces.shape[0]
    grid = received.reshape(-1, owned, received.shape[1], received.shape[2])
    gate = jnp.einsum("spkd,pdf->spkf", grid, gate_pieces, preferred_element_type=jnp.float32)
    upper = jnp.einsum("spkd,pdf->spkf", grid, up_pieces, preferred_element_type=jnp.float32)
    active = (jax.nn.silu(gate) * upper).astype(jnp.bfloat16)
    output = jnp.einsum(
        "spkf,pfd->spkd", active, down_pieces, preferred_element_type=jnp.float32
    ).astype(jnp.bfloat16)
    return output.reshape(received.shape)


def on_device(
    hidden_in,
    queries,
    latent_weight,
    latent_gain,
    key_up,
    value_up,
    out_weight,
    ffn_gain,
    router_weight,
    gate_pieces,
    up_pieces,
    down_pieces,
    prefix_latent,
    prefix_rope,
    page_table,
    segment_ids,
    expert_ids,
):
    rows = hidden_in.shape[0]
    n_wide = lax.axis_size("wide")
    wide_at = lax.axis_index("wide")
    my_start = wide_at * rows
    prefix_len = prefix_latent.shape[0] * lax.axis_size("req") * PAGE
    slots = lax.axis_index("req") * prefix_latent.shape[0] + jnp.arange(
        prefix_latent.shape[0], dtype=jnp.int32
    )
    key_pos = page_positions(page_table, slots)
    own_rot = rotary(prefix_rope.reshape(-1, ROPE).astype(jnp.float32), key_pos).astype(jnp.bfloat16)
    own_keys = jnp.concatenate([prefix_latent.reshape(-1, LAT), own_rot], axis=1)
    page_keys = lax.all_gather(own_keys, "req", axis=0, tiled=True)
    raw = jnp.dot(hidden_in, latent_weight, preferred_element_type=jnp.float32)
    latent = rms_scale(raw[:, :LAT], latent_gain).astype(jnp.bfloat16)
    key_rope = raw[:, LAT:].astype(jnp.bfloat16)
    suffix_cache = jnp.concatenate([latent, key_rope], axis=1)
    tag = jnp.broadcast_to(segment_ids.reshape(rows, 1).astype(jnp.bfloat16), (rows, ROPE))
    group = lax.all_gather(
        jnp.concatenate([suffix_cache, tag], axis=1), "wide", axis=0, tiled=True
    )
    split_q = queries.reshape(rows, HEADS, NOPE + ROPE)
    q_lat = jnp.einsum(
        "thn,lhn->htl",
        split_q[..., :NOPE],
        key_up.reshape(LAT, HEADS, NOPE),
        preferred_element_type=jnp.float32,
    ).astype(jnp.bfloat16)
    hits = expert_ids[..., None] == jnp.arange(EXPERTS, dtype=jnp.int32)
    flat_hits = hits.reshape(rows * TOPK, EXPERTS).astype(jnp.int32)
    slot = jnp.sum((jnp.cumsum(flat_hits, axis=0) - flat_hits) * flat_hits, axis=-1).reshape(
        rows, TOPK
    )
    column = jnp.arange(EXPERTS * SPLIT * CAP, dtype=jnp.int32)
    first = expert_ids * (SPLIT * CAP) + slot
    match = jnp.zeros((EXPERTS * SPLIT * CAP, rows, TOPK), dtype=bool)
    for half in range(SPLIT):
        match = match | ((first + half * CAP)[None, :, :] == column[:, None, None])
    selector = jnp.any(match, axis=-1).astype(jnp.bfloat16).reshape(EXPERTS * SPLIT, CAP, rows)
    group, q_lat, selector = lax.optimization_barrier((group, q_lat, selector))
    group_seg = group[:, LAT + ROPE].astype(jnp.int32)
    group_pos = prefix_len + offsets(group_seg)
    index_q = my_start + jnp.arange(rows, dtype=jnp.int32)
    position = lax.dynamic_slice_in_dim(group_pos, my_start, rows, 0)
    q_rot = (
        rotary(split_q[..., NOPE:].astype(jnp.float32), position)
        .astype(jnp.bfloat16)
        .transpose(1, 0, 2)
    )
    reach = -(-(MOST_LEN - 1) // rows) + 1
    blocks = min(n_wide, reach)
    base = (jnp.maximum(wide_at - (blocks - 1), 0) * rows).astype(jnp.int32).reshape(1)
    window_rope = lax.dynamic_slice_in_dim(group[:, LAT : LAT + ROPE], base[0], blocks * rows, 0)
    window_pos = lax.dynamic_slice_in_dim(group_pos, base[0], blocks * rows, 0)
    group_rot = rotary(window_rope.astype(jnp.float32), window_pos).astype(jnp.bfloat16)
    lo = (index_q - (position - prefix_len))[:, None]
    hi = index_q[:, None]
    mixed = attend(
        base,
        q_lat.reshape(rows * HEADS, LAT),
        q_rot.reshape(rows * HEADS, ROPE),
        page_keys,
        group,
        group_rot,
        lo,
        hi,
        blocks * rows,
    ).reshape(
        HEADS, rows, LAT
    )
    head_out = (
        jnp.einsum(
            "htl,lhn->thn",
            mixed,
            value_up.reshape(LAT, HEADS, NOPE),
            preferred_element_type=jnp.float32,
        )
        .astype(jnp.bfloat16)
        .reshape(rows, HEADS * NOPE)
    )
    residual = hidden_in.astype(jnp.float32) + jnp.dot(
        head_out, out_weight, preferred_element_type=jnp.float32
    )
    normed = rms_scale(residual, ffn_gain).astype(jnp.bfloat16)
    logits = jnp.dot(normed, router_weight, preferred_element_type=jnp.float32)
    chosen = jnp.sum(jnp.where(hits, logits[:, None, :], 0.0), axis=-1)
    gates = jax.nn.softmax(chosen, axis=-1)
    cut = CAP // 2
    parts = []
    for lo_slot, hi_slot in ((0, cut), (cut, CAP)):
        outgoing = (
            jnp.dot(
                selector[:, lo_slot:hi_slot].reshape(-1, rows),
                normed,
                preferred_element_type=jnp.float32,
            )
            .astype(jnp.bfloat16)
            .reshape(EXPERTS * SPLIT, hi_slot - lo_slot, D)
        )
        sent = lax.all_to_all(outgoing, ("req", "wide"), split_axis=0, concat_axis=0, tiled=True)
        worked = expert_rows(sent, gate_pieces, up_pieces, down_pieces)
        parts.append(
            lax.all_to_all(worked, ("req", "wide"), split_axis=0, concat_axis=0, tiled=True)
        )
    weight = jnp.sum(jnp.where(match.transpose(1, 0, 2), gates[:, None, :], 0.0), axis=-1)
    weight_hi = weight.astype(jnp.bfloat16)
    weight_lo = (weight - weight_hi.astype(jnp.float32)).astype(jnp.bfloat16)
    routed = jnp.zeros((rows, D), jnp.float32)
    bounds = ((0, cut), (cut, CAP))
    stacked = jnp.concatenate([weight_hi, weight_lo], axis=0).reshape(
        2 * rows, EXPERTS * SPLIT, CAP
    )
    for (lo_slot, hi_slot), part in zip(bounds, parts):
        both = jnp.dot(
            stacked[:, :, lo_slot:hi_slot].reshape(2 * rows, -1),
            part.reshape(-1, D),
            preferred_element_type=jnp.float32,
        )
        routed = routed + (both[:rows] + both[rows:])
    return ((residual + routed).astype(jnp.bfloat16), suffix_cache)


def solution(mesh):
    return jax.shard_map(
        on_device,
        mesh=mesh,
        in_specs=(
            P(("req", "wide"), None),
            P(("req", "wide"), None),
            P(),
            P(),
            P(),
            P(),
            P(),
            P(),
            P(),
            P(("req", "wide"), None, None),
            P(("req", "wide"), None, None),
            P(("req", "wide"), None, None),
            P("req", None, None),
            P("req", None, None),
            P(),
            P("req", "wide"),
            P(("req", "wide"), None),
        ),
        out_specs=(P(("req", "wide"), None), P(("req", "wide"), None)),
        check_vma=False,
    )
```

```python
import functools
import math

import jax
import jax.numpy as jnp
from jax import lax
from jax.experimental import pallas as pl
from jax.experimental.pallas import tpu as pltpu
from jax.sharding import PartitionSpec as P

D = 2048
HEADS = 16
NOPE = 128
ROPE = 64
LAT = 512
EXPERTS = 64
TOPK = 6
SPLIT = 2
PAGE = 128
CAP = 14
MOST_LEN = 1024


EPS = 1e-06
NEG = -1e30


def rotary(values, positions):
    half = values.shape[-1] // 2
    freqs = 10000.0 ** (-2.0 * jnp.arange(half, dtype=jnp.float32) / values.shape[-1])
    angles = positions.astype(jnp.float32)[:, None] * freqs[None, :]
    shape = (positions.shape[0],) + (1,) * (values.ndim - 2) + (half,)
    cosine = jnp.cos(angles).reshape(shape)
    sine = jnp.sin(angles).reshape(shape)
    first = values[..., :half]
    second = values[..., half:]
    return jnp.concatenate(
        [first * cosine - second * sine, second * cosine + first * sine], axis=-1
    )


def rms_scale(values, gain):
    return values * lax.rsqrt(jnp.mean(values * values, axis=-1, keepdims=True) + EPS) * gain


def offsets(segments):
    length = segments.shape[0]
    index = jnp.arange(length, dtype=jnp.int32)
    fresh = jnp.concatenate([jnp.ones((1,), dtype=bool), segments[1:] != segments[:-1]])
    starts = lax.cummax(jnp.where(fresh, index, 0), axis=0)
    return index - starts


def page_positions(page_table, slots):
    logical = jnp.sum(
        jnp.where(
            page_table[None, :] == slots[:, None],
            jnp.arange(page_table.shape[0], dtype=jnp.int32)[None, :],
            0,
        ),
        axis=1,
    )
    return (logical[:, None] * PAGE + jnp.arange(PAGE, dtype=jnp.int32)[None, :]).reshape(-1)


def attend_kernel(
    base_ref, ql_ref, qr_ref, kp_ref, kl_ref, kr_ref, lo_ref, hi_ref, out_ref, *, window, scale
):
    base = pl.multiple_of(base_ref[0], 128)
    lat = out_ref.shape[1]
    ql = ql_ref[...]
    qr = qr_ref[...]
    kp_lat = kp_ref[:, :lat]
    kp_rot = kp_ref[:, lat:]
    k_lat = kl_ref[pl.ds(base, window), :lat]
    k_rot = kr_ref[...]
    dims = (((1,), (1,)), ((), ()))
    s_p = (
        lax.dot_general(ql, kp_lat, dims, preferred_element_type=jnp.float32)
        + lax.dot_general(qr, kp_rot, dims, preferred_element_type=jnp.float32)
    ) * scale
    s_s = (
        lax.dot_general(ql, k_lat, dims, preferred_element_type=jnp.float32)
        + lax.dot_general(qr, k_rot, dims, preferred_element_type=jnp.float32)
    ) * scale
    copies = ql_ref.shape[0] // lo_ref.shape[0]
    lo = jnp.concatenate([lo_ref[...]] * copies, axis=0)
    hi = jnp.concatenate([hi_ref[...]] * copies, axis=0)
    kidx = base + lax.broadcasted_iota(jnp.int32, (1, window), 1)
    allowed = (kidx >= lo) & (kidx <= hi)
    s_s = jnp.where(allowed, s_s, NEG)
    top = jnp.maximum(jnp.max(s_p, axis=1, keepdims=True), jnp.max(s_s, axis=1, keepdims=True))
    w_p = jnp.exp(s_p - top)
    w_s = jnp.exp(s_s - top)
    total = jnp.sum(w_p, axis=1, keepdims=True) + jnp.sum(w_s, axis=1, keepdims=True)
    accum = jnp.dot(w_p.astype(jnp.bfloat16), kp_lat, preferred_element_type=jnp.float32) + jnp.dot(
        w_s.astype(jnp.bfloat16), k_lat, preferred_element_type=jnp.float32
    )
    out_ref[...] = (accum / total).astype(out_ref.dtype)


def attend(base, q_lat, q_rot, kp, k_lat, k_rot, lo, hi, window, block=512):
    rows = q_lat.shape[0]
    return pl.pallas_call(
        functools.partial(attend_kernel, window=window, scale=1.0 / math.sqrt(NOPE + ROPE)),
        grid_spec=pltpu.PrefetchScalarGridSpec(
            num_scalar_prefetch=1,
            grid=(rows // block,),
            in_specs=[
                pl.BlockSpec((block, LAT), lambda i, b: (i, 0)),
                pl.BlockSpec((block, ROPE), lambda i, b: (i, 0)),
                pl.BlockSpec(kp.shape, lambda i, b: (0, 0)),
                pl.BlockSpec(k_lat.shape, lambda i, b: (0, 0)),
                pl.BlockSpec(k_rot.shape, lambda i, b: (0, 0)),
                pl.BlockSpec(lo.shape, lambda i, b: (0, 0)),
                pl.BlockSpec(hi.shape, lambda i, b: (0, 0)),
            ],
            out_specs=pl.BlockSpec((block, LAT), lambda i, b: (i, 0)),
        ),
        out_shape=jax.ShapeDtypeStruct((rows, LAT), jnp.bfloat16),
    )(base, q_lat, q_rot, kp, k_lat, k_rot, lo, hi)


def combine_kernel(w_ref, r_ref, o_ref):
    half = o_ref.shape[0]
    total = jnp.zeros((2 * half, o_ref.shape[1]), jnp.float32)
    for at in range(w_ref.shape[0]):
        total = total + jnp.dot(w_ref[at], r_ref[:, at, :], preferred_element_type=jnp.float32)
    o_ref[...] = total[:half] + total[half:]


def combine(weights, part):
    rows = weights.shape[1] // 2
    return pl.pallas_call(
        combine_kernel,
        out_shape=jax.ShapeDtypeStruct((rows, part.shape[2]), jnp.float32),
    )(weights, part)


def expert_rows(received, gate_pieces, up_pieces, down_pieces):
    owned = gate_pieces.shape[0]
    grid = received.reshape(-1, owned, received.shape[1], received.shape[2])
    gate = jnp.einsum("spkd,pdf->spkf", grid, gate_pieces, preferred_element_type=jnp.float32)
    upper = jnp.einsum("spkd,pdf->spkf", grid, up_pieces, preferred_element_type=jnp.float32)
    active = (jax.nn.silu(gate) * upper).astype(jnp.bfloat16)
    output = jnp.einsum(
        "spkf,pfd->spkd", active, down_pieces, preferred_element_type=jnp.float32
    ).astype(jnp.bfloat16)
    return output.reshape(received.shape)


def on_device(
    hidden_in,
    queries,
    latent_weight,
    latent_gain,
    key_up,
    value_up,
    out_weight,
    ffn_gain,
    router_weight,
    gate_pieces,
    up_pieces,
    down_pieces,
    prefix_latent,
    prefix_rope,
    page_table,
    segment_ids,
    expert_ids,
):
    rows = hidden_in.shape[0]
    n_wide = lax.axis_size("wide")
    wide_at = lax.axis_index("wide")
    my_start = wide_at * rows
    prefix_len = prefix_latent.shape[0] * lax.axis_size("req") * PAGE
    slots = lax.axis_index("req") * prefix_latent.shape[0] + jnp.arange(
        prefix_latent.shape[0], dtype=jnp.int32
    )
    key_pos = page_positions(page_table, slots)
    own_rot = rotary(prefix_rope.reshape(-1, ROPE).astype(jnp.float32), key_pos).astype(jnp.bfloat16)
    own_keys = jnp.concatenate([prefix_latent.reshape(-1, LAT), own_rot], axis=1)
    page_keys = lax.all_gather(own_keys, "req", axis=0, tiled=True)
    raw = jnp.dot(hidden_in, latent_weight, preferred_element_type=jnp.float32)
    latent = rms_scale(raw[:, :LAT], latent_gain).astype(jnp.bfloat16)
    key_rope = raw[:, LAT:].astype(jnp.bfloat16)
    suffix_cache = jnp.concatenate([latent, key_rope], axis=1)
    tag = jnp.broadcast_to(segment_ids.reshape(rows, 1).astype(jnp.bfloat16), (rows, ROPE))
    group = lax.all_gather(
        jnp.concatenate([suffix_cache, tag], axis=1), "wide", axis=0, tiled=True
    )
    split_q = queries.reshape(rows, HEADS, NOPE + ROPE)
    q_lat = jnp.einsum(
        "thn,lhn->htl",
        split_q[..., :NOPE],
        key_up.reshape(LAT, HEADS, NOPE),
        preferred_element_type=jnp.float32,
    ).astype(jnp.bfloat16)
    hits = expert_ids[..., None] == jnp.arange(EXPERTS, dtype=jnp.int32)
    flat_hits = hits.reshape(rows * TOPK, EXPERTS).astype(jnp.int32)
    slot = jnp.sum((jnp.cumsum(flat_hits, axis=0) - flat_hits) * flat_hits, axis=-1).reshape(
        rows, TOPK
    )
    column = jnp.arange(EXPERTS * SPLIT * CAP, dtype=jnp.int32)
    first = expert_ids * (SPLIT * CAP) + slot
    match = jnp.zeros((EXPERTS * SPLIT * CAP, rows, TOPK), dtype=bool)
    for half in range(SPLIT):
        match = match | ((first + half * CAP)[None, :, :] == column[:, None, None])
    selector = jnp.any(match, axis=-1).astype(jnp.bfloat16).reshape(EXPERTS * SPLIT, CAP, rows)
    group, q_lat, selector = lax.optimization_barrier((group, q_lat, selector))
    group_seg = group[:, LAT + ROPE].astype(jnp.int32)
    group_pos = prefix_len + offsets(group_seg)
    index_q = my_start + jnp.arange(rows, dtype=jnp.int32)
    position = lax.dynamic_slice_in_dim(group_pos, my_start, rows, 0)
    q_rot = (
        rotary(split_q[..., NOPE:].astype(jnp.float32), position)
        .astype(jnp.bfloat16)
        .transpose(1, 0, 2)
    )
    reach = -(-(MOST_LEN - 1) // rows) + 1
    blocks = min(n_wide, reach)
    base = (jnp.maximum(wide_at - (blocks - 1), 0) * rows).astype(jnp.int32).reshape(1)
    window_rope = lax.dynamic_slice_in_dim(group[:, LAT : LAT + ROPE], base[0], blocks * rows, 0)
    window_pos = lax.dynamic_slice_in_dim(group_pos, base[0], blocks * rows, 0)
    group_rot = rotary(window_rope.astype(jnp.float32), window_pos).astype(jnp.bfloat16)
    lo = (index_q - (position - prefix_len))[:, None]
    hi = index_q[:, None]
    mixed = attend(
        base,
        q_lat.reshape(rows * HEADS, LAT),
        q_rot.reshape(rows * HEADS, ROPE),
        page_keys,
        group,
        group_rot,
        lo,
        hi,
        blocks * rows,
    ).reshape(
        HEADS, rows, LAT
    )
    head_out = (
        jnp.einsum(
            "htl,lhn->thn",
            mixed,
            value_up.reshape(LAT, HEADS, NOPE),
            preferred_element_type=jnp.float32,
        )
        .astype(jnp.bfloat16)
        .reshape(rows, HEADS * NOPE)
    )
    residual = hidden_in.astype(jnp.float32) + jnp.dot(
        head_out, out_weight, preferred_element_type=jnp.float32
    )
    normed = rms_scale(residual, ffn_gain).astype(jnp.bfloat16)
    logits = jnp.dot(normed, router_weight, preferred_element_type=jnp.float32)
    chosen = jnp.sum(jnp.where(hits, logits[:, None, :], 0.0), axis=-1)
    gates = jax.nn.softmax(chosen, axis=-1)
    cut = CAP // 2
    parts = []
    for lo_slot, hi_slot in ((0, cut), (cut, CAP)):
        outgoing = (
            jnp.dot(
                selector[:, lo_slot:hi_slot].reshape(-1, rows),
                normed,
                preferred_element_type=jnp.float32,
            )
            .astype(jnp.bfloat16)
            .reshape(EXPERTS * SPLIT, hi_slot - lo_slot, D)
        )
        sent = lax.all_to_all(outgoing, ("req", "wide"), split_axis=0, concat_axis=0, tiled=True)
        worked = expert_rows(sent, gate_pieces, up_pieces, down_pieces)
        parts.append(
            lax.all_to_all(worked, ("req", "wide"), split_axis=0, concat_axis=0, tiled=True)
        )
    weight = jnp.sum(jnp.where(match.transpose(1, 0, 2), gates[:, None, :], 0.0), axis=-1)
    weight_hi = weight.astype(jnp.bfloat16)
    weight_lo = (weight - weight_hi.astype(jnp.float32)).astype(jnp.bfloat16)
    routed = jnp.zeros((rows, D), jnp.float32)
    bounds = ((0, cut), (cut, CAP))
    stacked = jnp.concatenate([weight_hi, weight_lo], axis=0).reshape(
        2 * rows, EXPERTS * SPLIT, CAP
    )
    for (lo_slot, hi_slot), part in zip(bounds, parts):
        routed = routed + combine(stacked[:, :, lo_slot:hi_slot].transpose(2, 0, 1), part)
    return ((residual + routed).astype(jnp.bfloat16), suffix_cache)


def solution(mesh):
    return jax.shard_map(
        on_device,
        mesh=mesh,
        in_specs=(
            P(("req", "wide"), None),
            P(("req", "wide"), None),
            P(),
            P(),
            P(),
            P(),
            P(),
            P(),
            P(),
            P(("req", "wide"), None, None),
            P(("req", "wide"), None, None),
            P(("req", "wide"), None, None),
            P("req", None, None),
            P("req", None, None),
            P(),
            P("req", "wide"),
            P(("req", "wide"), None),
        ),
        out_specs=(P(("req", "wide"), None), P(("req", "wide"), None)),
        check_vma=False,
    )
```

```python
import functools
import math

import jax
import jax.numpy as jnp
from jax import lax
from jax.experimental import pallas as pl
from jax.experimental.pallas import tpu as pltpu
from jax.sharding import PartitionSpec as P

D = 2048
HEADS = 16
NOPE = 128
ROPE = 64
LAT = 512
EXPERTS = 64
TOPK = 6
SPLIT = 2
PAGE = 128
CAP = 14
MOST_LEN = 1024


EPS = 1e-06
NEG = -1e30


def rotary(values, positions):
    half = values.shape[-1] // 2
    freqs = 10000.0 ** (-2.0 * jnp.arange(half, dtype=jnp.float32) / values.shape[-1])
    angles = positions.astype(jnp.float32)[:, None] * freqs[None, :]
    shape = (positions.shape[0],) + (1,) * (values.ndim - 2) + (half,)
    cosine = jnp.cos(angles).reshape(shape)
    sine = jnp.sin(angles).reshape(shape)
    first = values[..., :half]
    second = values[..., half:]
    return jnp.concatenate(
        [first * cosine - second * sine, second * cosine + first * sine], axis=-1
    )


def rms_scale(values, gain):
    return values * lax.rsqrt(jnp.mean(values * values, axis=-1, keepdims=True) + EPS) * gain


def offsets(segments):
    length = segments.shape[0]
    index = jnp.arange(length, dtype=jnp.int32)
    fresh = jnp.concatenate([jnp.ones((1,), dtype=bool), segments[1:] != segments[:-1]])
    starts = lax.cummax(jnp.where(fresh, index, 0), axis=0)
    return index - starts


def page_positions(page_table, slots):
    logical = jnp.sum(
        jnp.where(
            page_table[None, :] == slots[:, None],
            jnp.arange(page_table.shape[0], dtype=jnp.int32)[None, :],
            0,
        ),
        axis=1,
    )
    return (logical[:, None] * PAGE + jnp.arange(PAGE, dtype=jnp.int32)[None, :]).reshape(-1)


def attend_kernel(
    base_ref, ql_ref, qr_ref, kp_ref, kl_ref, kr_ref, lo_ref, hi_ref, out_ref, *, window, scale
):
    base = pl.multiple_of(base_ref[0], 128)
    lat = out_ref.shape[1]
    ql = ql_ref[...]
    qr = qr_ref[...]
    kp_lat = kp_ref[:, :lat]
    kp_rot = kp_ref[:, lat:]
    k_lat = kl_ref[pl.ds(base, window), :lat]
    k_rot = kr_ref[...]
    dims = (((1,), (1,)), ((), ()))
    s_p = (
        lax.dot_general(ql, kp_lat, dims, preferred_element_type=jnp.float32)
        + lax.dot_general(qr, kp_rot, dims, preferred_element_type=jnp.float32)
    ) * scale
    s_s = (
        lax.dot_general(ql, k_lat, dims, preferred_element_type=jnp.float32)
        + lax.dot_general(qr, k_rot, dims, preferred_element_type=jnp.float32)
    ) * scale
    copies = ql_ref.shape[0] // lo_ref.shape[0]
    lo = jnp.concatenate([lo_ref[...]] * copies, axis=0)
    hi = jnp.concatenate([hi_ref[...]] * copies, axis=0)
    kidx = base + lax.broadcasted_iota(jnp.int32, (1, window), 1)
    allowed = (kidx >= lo) & (kidx <= hi)
    s_s = jnp.where(allowed, s_s, NEG)
    top = jnp.maximum(jnp.max(s_p, axis=1, keepdims=True), jnp.max(s_s, axis=1, keepdims=True))
    w_p = jnp.exp(s_p - top)
    w_s = jnp.exp(s_s - top)
    total = jnp.sum(w_p, axis=1, keepdims=True) + jnp.sum(w_s, axis=1, keepdims=True)
    accum = jnp.dot(w_p.astype(jnp.bfloat16), kp_lat, preferred_element_type=jnp.float32) + jnp.dot(
        w_s.astype(jnp.bfloat16), k_lat, preferred_element_type=jnp.float32
    )
    out_ref[...] = (accum / total).astype(out_ref.dtype)


def attend(base, q_lat, q_rot, kp, k_lat, k_rot, lo, hi, window, block=1024):
    rows = q_lat.shape[0]
    return pl.pallas_call(
        functools.partial(attend_kernel, window=window, scale=1.0 / math.sqrt(NOPE + ROPE)),
        grid_spec=pltpu.PrefetchScalarGridSpec(
            num_scalar_prefetch=1,
            grid=(rows // block,),
            in_specs=[
                pl.BlockSpec((block, LAT), lambda i, b: (i, 0)),
                pl.BlockSpec((block, ROPE), lambda i, b: (i, 0)),
                pl.BlockSpec(kp.shape, lambda i, b: (0, 0)),
                pl.BlockSpec(k_lat.shape, lambda i, b: (0, 0)),
                pl.BlockSpec(k_rot.shape, lambda i, b: (0, 0)),
                pl.BlockSpec(lo.shape, lambda i, b: (0, 0)),
                pl.BlockSpec(hi.shape, lambda i, b: (0, 0)),
            ],
            out_specs=pl.BlockSpec((block, LAT), lambda i, b: (i, 0)),
        ),
        out_shape=jax.ShapeDtypeStruct((rows, LAT), jnp.bfloat16),
    )(base, q_lat, q_rot, kp, k_lat, k_rot, lo, hi)


def expert_rows(received, gate_pieces, up_pieces, down_pieces):
    owned = gate_pieces.shape[0]
    grid = received.reshape(-1, owned, received.shape[1], received.shape[2])
    gate = jnp.einsum("spkd,pdf->spkf", grid, gate_pieces, preferred_element_type=jnp.float32)
    upper = jnp.einsum("spkd,pdf->spkf", grid, up_pieces, preferred_element_type=jnp.float32)
    active = (jax.nn.silu(gate) * upper).astype(jnp.bfloat16)
    output = jnp.einsum(
        "spkf,pfd->spkd", active, down_pieces, preferred_element_type=jnp.float32
    ).astype(jnp.bfloat16)
    return output.reshape(received.shape)


def on_device(
    hidden_in,
    queries,
    latent_weight,
    latent_gain,
    key_up,
    value_up,
    out_weight,
    ffn_gain,
    router_weight,
    gate_pieces,
    up_pieces,
    down_pieces,
    prefix_latent,
    prefix_rope,
    page_table,
    segment_ids,
    expert_ids,
):
    rows = hidden_in.shape[0]
    n_wide = lax.axis_size("wide")
    wide_at = lax.axis_index("wide")
    my_start = wide_at * rows
    prefix_len = prefix_latent.shape[0] * lax.axis_size("req") * PAGE
    slots = lax.axis_index("req") * prefix_latent.shape[0] + jnp.arange(
        prefix_latent.shape[0], dtype=jnp.int32
    )
    key_pos = page_positions(page_table, slots)
    own_rot = rotary(prefix_rope.reshape(-1, ROPE).astype(jnp.float32), key_pos).astype(jnp.bfloat16)
    own_keys = jnp.concatenate([prefix_latent.reshape(-1, LAT), own_rot], axis=1)
    page_keys = lax.all_gather(own_keys, "req", axis=0, tiled=True)
    raw = jnp.dot(hidden_in, latent_weight, preferred_element_type=jnp.float32)
    latent = rms_scale(raw[:, :LAT], latent_gain).astype(jnp.bfloat16)
    key_rope = raw[:, LAT:].astype(jnp.bfloat16)
    suffix_cache = jnp.concatenate([latent, key_rope], axis=1)
    tag = jnp.broadcast_to(segment_ids.reshape(rows, 1).astype(jnp.bfloat16), (rows, ROPE))
    group = lax.all_gather(
        jnp.concatenate([suffix_cache, tag], axis=1), "wide", axis=0, tiled=True
    )
    split_q = queries.reshape(rows, HEADS, NOPE + ROPE)
    q_lat = jnp.einsum(
        "thn,lhn->htl",
        split_q[..., :NOPE],
        key_up.reshape(LAT, HEADS, NOPE),
        preferred_element_type=jnp.float32,
    ).astype(jnp.bfloat16)
    hits = expert_ids[..., None] == jnp.arange(EXPERTS, dtype=jnp.int32)
    flat_hits = hits.reshape(rows * TOPK, EXPERTS).astype(jnp.int32)
    slot = jnp.sum((jnp.cumsum(flat_hits, axis=0) - flat_hits) * flat_hits, axis=-1).reshape(
        rows, TOPK
    )
    column = jnp.arange(EXPERTS * SPLIT * CAP, dtype=jnp.int32)
    first = expert_ids * (SPLIT * CAP) + slot
    match = jnp.zeros((EXPERTS * SPLIT * CAP, rows, TOPK), dtype=bool)
    for half in range(SPLIT):
        match = match | ((first + half * CAP)[None, :, :] == column[:, None, None])
    selector = jnp.any(match, axis=-1).astype(jnp.bfloat16).reshape(EXPERTS * SPLIT, CAP, rows)
    group, q_lat, selector = lax.optimization_barrier((group, q_lat, selector))
    group_seg = group[:, LAT + ROPE].astype(jnp.int32)
    group_pos = prefix_len + offsets(group_seg)
    index_q = my_start + jnp.arange(rows, dtype=jnp.int32)
    position = lax.dynamic_slice_in_dim(group_pos, my_start, rows, 0)
    q_rot = (
        rotary(split_q[..., NOPE:].astype(jnp.float32), position)
        .astype(jnp.bfloat16)
        .transpose(1, 0, 2)
    )
    reach = -(-(MOST_LEN - 1) // rows) + 1
    blocks = min(n_wide, reach)
    base = (jnp.maximum(wide_at - (blocks - 1), 0) * rows).astype(jnp.int32).reshape(1)
    window_rope = lax.dynamic_slice_in_dim(group[:, LAT : LAT + ROPE], base[0], blocks * rows, 0)
    window_pos = lax.dynamic_slice_in_dim(group_pos, base[0], blocks * rows, 0)
    group_rot = rotary(window_rope.astype(jnp.float32), window_pos).astype(jnp.bfloat16)
    lo = (index_q - (position - prefix_len))[:, None]
    hi = index_q[:, None]
    mixed = attend(
        base,
        q_lat.reshape(rows * HEADS, LAT),
        q_rot.reshape(rows * HEADS, ROPE),
        page_keys,
        group,
        group_rot,
        lo,
        hi,
        blocks * rows,
    ).reshape(
        HEADS, rows, LAT
    )
    head_out = (
        jnp.einsum(
            "htl,lhn->thn",
            mixed,
            value_up.reshape(LAT, HEADS, NOPE),
            preferred_element_type=jnp.float32,
        )
        .astype(jnp.bfloat16)
        .reshape(rows, HEADS * NOPE)
    )
    residual = hidden_in.astype(jnp.float32) + jnp.dot(
        head_out, out_weight, preferred_element_type=jnp.float32
    )
    normed = rms_scale(residual, ffn_gain).astype(jnp.bfloat16)
    logits = jnp.dot(normed, router_weight, preferred_element_type=jnp.float32)
    chosen = jnp.sum(jnp.where(hits, logits[:, None, :], 0.0), axis=-1)
    gates = jax.nn.softmax(chosen, axis=-1)
    cut = CAP // 2
    parts = []
    for lo_slot, hi_slot in ((0, cut), (cut, CAP)):
        outgoing = (
            jnp.dot(
                selector[:, lo_slot:hi_slot].reshape(-1, rows),
                normed,
                preferred_element_type=jnp.float32,
            )
            .astype(jnp.bfloat16)
            .reshape(EXPERTS * SPLIT, hi_slot - lo_slot, D)
        )
        sent = lax.all_to_all(outgoing, ("req", "wide"), split_axis=0, concat_axis=0, tiled=True)
        worked = expert_rows(sent, gate_pieces, up_pieces, down_pieces)
        parts.append(
            lax.all_to_all(worked, ("req", "wide"), split_axis=0, concat_axis=0, tiled=True)
        )
    weight = jnp.sum(jnp.where(match.transpose(1, 0, 2), gates[:, None, :], 0.0), axis=-1)
    weight_hi = weight.astype(jnp.bfloat16)
    weight_lo = (weight - weight_hi.astype(jnp.float32)).astype(jnp.bfloat16)
    routed = jnp.zeros((rows, D), jnp.float32)
    bounds = ((0, cut), (cut, CAP))
    stacked = jnp.concatenate([weight_hi, weight_lo], axis=0).reshape(
        2 * rows, EXPERTS * SPLIT, CAP
    )
    for (lo_slot, hi_slot), part in zip(bounds, parts):
        both = jnp.dot(
            stacked[:, :, lo_slot:hi_slot].reshape(2 * rows, -1),
            part.reshape(-1, D),
            preferred_element_type=jnp.float32,
        )
        routed = routed + (both[:rows] + both[rows:])
    return ((residual + routed).astype(jnp.bfloat16), suffix_cache)


def solution(mesh):
    return jax.shard_map(
        on_device,
        mesh=mesh,
        in_specs=(
            P(("req", "wide"), None),
            P(("req", "wide"), None),
            P(),
            P(),
            P(),
            P(),
            P(),
            P(),
            P(),
            P(("req", "wide"), None, None),
            P(("req", "wide"), None, None),
            P(("req", "wide"), None, None),
            P("req", None, None),
            P("req", None, None),
            P(),
            P("req", "wide"),
            P(("req", "wide"), None),
        ),
        out_specs=(P(("req", "wide"), None), P(("req", "wide"), None)),
        check_vma=False,
    )
```

```python
import functools
import math

import jax
import jax.numpy as jnp
from jax import lax
from jax.experimental import pallas as pl
from jax.experimental.pallas import tpu as pltpu
from jax.sharding import PartitionSpec as P

D = 2048
HEADS = 16
NOPE = 128
ROPE = 64
LAT = 512
EXPERTS = 64
TOPK = 6
SPLIT = 2
PAGE = 128
CAP = 14
MOST_LEN = 1024


EPS = 1e-06
NEG = -1e30


def rotary(values, positions):
    half = values.shape[-1] // 2
    freqs = 10000.0 ** (-2.0 * jnp.arange(half, dtype=jnp.float32) / values.shape[-1])
    angles = positions.astype(jnp.float32)[:, None] * freqs[None, :]
    shape = (positions.shape[0],) + (1,) * (values.ndim - 2) + (half,)
    cosine = jnp.cos(angles).reshape(shape)
    sine = jnp.sin(angles).reshape(shape)
    first = values[..., :half]
    second = values[..., half:]
    return jnp.concatenate(
        [first * cosine - second * sine, second * cosine + first * sine], axis=-1
    )


def rms_scale(values, gain):
    return values * lax.rsqrt(jnp.mean(values * values, axis=-1, keepdims=True) + EPS) * gain


def offsets(segments):
    length = segments.shape[0]
    index = jnp.arange(length, dtype=jnp.int32)
    fresh = jnp.concatenate([jnp.ones((1,), dtype=bool), segments[1:] != segments[:-1]])
    starts = lax.cummax(jnp.where(fresh, index, 0), axis=0)
    return index - starts


def page_positions(page_table, slots):
    logical = jnp.sum(
        jnp.where(
            page_table[None, :] == slots[:, None],
            jnp.arange(page_table.shape[0], dtype=jnp.int32)[None, :],
            0,
        ),
        axis=1,
    )
    return (logical[:, None] * PAGE + jnp.arange(PAGE, dtype=jnp.int32)[None, :]).reshape(-1)


def attend_kernel(
    base_ref, ql_ref, qr_ref, kp_ref, kl_ref, kr_ref, lo_ref, hi_ref, out_ref, *, window, scale
):
    base = pl.multiple_of(base_ref[0], 128)
    lat = out_ref.shape[1]
    ql = ql_ref[...]
    qr = qr_ref[...]
    kp_lat = kp_ref[:, :lat]
    kp_rot = kp_ref[:, lat:]
    k_lat = kl_ref[pl.ds(base, window), :lat]
    k_rot = kr_ref[...]
    dims = (((1,), (1,)), ((), ()))
    s_p = (
        lax.dot_general(ql, kp_lat, dims, preferred_element_type=jnp.float32)
        + lax.dot_general(qr, kp_rot, dims, preferred_element_type=jnp.float32)
    ) * scale
    s_s = (
        lax.dot_general(ql, k_lat, dims, preferred_element_type=jnp.float32)
        + lax.dot_general(qr, k_rot, dims, preferred_element_type=jnp.float32)
    ) * scale
    copies = ql_ref.shape[0] // lo_ref.shape[0]
    lo = jnp.concatenate([lo_ref[...]] * copies, axis=0)
    hi = jnp.concatenate([hi_ref[...]] * copies, axis=0)
    kidx = base + lax.broadcasted_iota(jnp.int32, (1, window), 1)
    allowed = (kidx >= lo) & (kidx <= hi)
    s_s = jnp.where(allowed, s_s, NEG)
    top = jnp.maximum(jnp.max(s_p, axis=1, keepdims=True), jnp.max(s_s, axis=1, keepdims=True))
    w_p = jnp.exp(s_p - top)
    w_s = jnp.exp(s_s - top)
    total = jnp.sum(w_p, axis=1, keepdims=True) + jnp.sum(w_s, axis=1, keepdims=True)
    accum = jnp.dot(w_p.astype(jnp.bfloat16), kp_lat, preferred_element_type=jnp.float32) + jnp.dot(
        w_s.astype(jnp.bfloat16), k_lat, preferred_element_type=jnp.float32
    )
    out_ref[...] = (accum / total).astype(out_ref.dtype)


def attend(base, q_lat, q_rot, kp, k_lat, k_rot, lo, hi, window, block=512):
    rows = q_lat.shape[0]
    return pl.pallas_call(
        functools.partial(attend_kernel, window=window, scale=1.0 / math.sqrt(NOPE + ROPE)),
        grid_spec=pltpu.PrefetchScalarGridSpec(
            num_scalar_prefetch=1,
            grid=(rows // block,),
            in_specs=[
                pl.BlockSpec((block, LAT), lambda i, b: (i, 0)),
                pl.BlockSpec((block, ROPE), lambda i, b: (i, 0)),
                pl.BlockSpec(kp.shape, lambda i, b: (0, 0)),
                pl.BlockSpec(k_lat.shape, lambda i, b: (0, 0)),
                pl.BlockSpec(k_rot.shape, lambda i, b: (0, 0)),
                pl.BlockSpec(lo.shape, lambda i, b: (0, 0)),
                pl.BlockSpec(hi.shape, lambda i, b: (0, 0)),
            ],
            out_specs=pl.BlockSpec((block, LAT), lambda i, b: (i, 0)),
        ),
        out_shape=jax.ShapeDtypeStruct((rows, LAT), jnp.bfloat16),
    )(base, q_lat, q_rot, kp, k_lat, k_rot, lo, hi)


def expert_rows(received, gate_pieces, up_pieces, down_pieces):
    owned = gate_pieces.shape[0]
    grid = received.reshape(-1, owned, received.shape[1], received.shape[2])
    gate = jnp.einsum("spkd,pdf->spkf", grid, gate_pieces, preferred_element_type=jnp.float32)
    upper = jnp.einsum("spkd,pdf->spkf", grid, up_pieces, preferred_element_type=jnp.float32)
    active = (jax.nn.silu(gate) * upper).astype(jnp.bfloat16)
    output = jnp.einsum(
        "spkf,pfd->spkd", active, down_pieces, preferred_element_type=jnp.float32
    ).astype(jnp.bfloat16)
    return output.reshape(received.shape)


def on_device(
    hidden_in,
    queries,
    latent_weight,
    latent_gain,
    key_up,
    value_up,
    out_weight,
    ffn_gain,
    router_weight,
    gate_pieces,
    up_pieces,
    down_pieces,
    prefix_latent,
    prefix_rope,
    page_table,
    segment_ids,
    expert_ids,
):
    rows = hidden_in.shape[0]
    n_wide = lax.axis_size("wide")
    wide_at = lax.axis_index("wide")
    my_start = wide_at * rows
    prefix_len = prefix_latent.shape[0] * lax.axis_size("req") * PAGE
    slots = lax.axis_index("req") * prefix_latent.shape[0] + jnp.arange(
        prefix_latent.shape[0], dtype=jnp.int32
    )
    key_pos = page_positions(page_table, slots)
    own_rot = rotary(prefix_rope.reshape(-1, ROPE).astype(jnp.float32), key_pos).astype(jnp.bfloat16)
    own_keys = jnp.concatenate([prefix_latent.reshape(-1, LAT), own_rot], axis=1)
    page_keys = lax.all_gather(own_keys, "req", axis=0, tiled=True)
    raw = jnp.dot(hidden_in, latent_weight, preferred_element_type=jnp.float32)
    latent = rms_scale(raw[:, :LAT], latent_gain).astype(jnp.bfloat16)
    key_rope = raw[:, LAT:].astype(jnp.bfloat16)
    suffix_cache = jnp.concatenate([latent, key_rope], axis=1)
    tag = jnp.broadcast_to(segment_ids.reshape(rows, 1).astype(jnp.bfloat16), (rows, ROPE))
    group = lax.all_gather(
        jnp.concatenate([suffix_cache, tag], axis=1), "wide", axis=0, tiled=True
    )
    split_q = queries.reshape(rows, HEADS, NOPE + ROPE)
    q_lat = jnp.einsum(
        "thn,lhn->htl",
        split_q[..., :NOPE],
        key_up.reshape(LAT, HEADS, NOPE),
        preferred_element_type=jnp.float32,
    ).astype(jnp.bfloat16)
    hits = expert_ids[..., None] == jnp.arange(EXPERTS, dtype=jnp.int32)
    flat_hits = hits.reshape(rows * TOPK, EXPERTS).astype(jnp.int32)
    slot = jnp.sum((jnp.cumsum(flat_hits, axis=0) - flat_hits) * flat_hits, axis=-1).reshape(
        rows, TOPK
    )
    column = jnp.arange(EXPERTS * SPLIT * CAP, dtype=jnp.int32)
    first = expert_ids * (SPLIT * CAP) + slot
    match = jnp.zeros((EXPERTS * SPLIT * CAP, rows, TOPK), dtype=bool)
    for half in range(SPLIT):
        match = match | ((first + half * CAP)[None, :, :] == column[:, None, None])
    selector = jnp.any(match, axis=-1).astype(jnp.bfloat16).reshape(EXPERTS * SPLIT, CAP, rows)
    value_heads = value_up.reshape(LAT, HEADS, NOPE).transpose(1, 0, 2)
    group, q_lat, selector, value_heads = lax.optimization_barrier(
        (group, q_lat, selector, value_heads)
    )
    group_seg = group[:, LAT + ROPE].astype(jnp.int32)
    group_pos = prefix_len + offsets(group_seg)
    index_q = my_start + jnp.arange(rows, dtype=jnp.int32)
    position = lax.dynamic_slice_in_dim(group_pos, my_start, rows, 0)
    q_rot = (
        rotary(split_q[..., NOPE:].astype(jnp.float32), position)
        .astype(jnp.bfloat16)
        .transpose(1, 0, 2)
    )
    reach = -(-(MOST_LEN - 1) // rows) + 1
    blocks = min(n_wide, reach)
    base = (jnp.maximum(wide_at - (blocks - 1), 0) * rows).astype(jnp.int32).reshape(1)
    window_rope = lax.dynamic_slice_in_dim(group[:, LAT : LAT + ROPE], base[0], blocks * rows, 0)
    window_pos = lax.dynamic_slice_in_dim(group_pos, base[0], blocks * rows, 0)
    group_rot = rotary(window_rope.astype(jnp.float32), window_pos).astype(jnp.bfloat16)
    lo = (index_q - (position - prefix_len))[:, None]
    hi = index_q[:, None]
    mixed = attend(
        base,
        q_lat.reshape(rows * HEADS, LAT),
        q_rot.reshape(rows * HEADS, ROPE),
        page_keys,
        group,
        group_rot,
        lo,
        hi,
        blocks * rows,
    ).reshape(
        HEADS, rows, LAT
    )
    head_out = (
        jnp.einsum(
            "htl,hln->thn",
            mixed,
            value_heads,
            preferred_element_type=jnp.float32,
        )
        .astype(jnp.bfloat16)
        .reshape(rows, HEADS * NOPE)
    )
    residual = hidden_in.astype(jnp.float32) + jnp.dot(
        head_out, out_weight, preferred_element_type=jnp.float32
    )
    normed = rms_scale(residual, ffn_gain).astype(jnp.bfloat16)
    logits = jnp.dot(normed, router_weight, preferred_element_type=jnp.float32)
    chosen = jnp.sum(jnp.where(hits, logits[:, None, :], 0.0), axis=-1)
    gates = jax.nn.softmax(chosen, axis=-1)
    cut = CAP // 2
    parts = []
    for lo_slot, hi_slot in ((0, cut), (cut, CAP)):
        outgoing = (
            jnp.dot(
                selector[:, lo_slot:hi_slot].reshape(-1, rows),
                normed,
                preferred_element_type=jnp.float32,
            )
            .astype(jnp.bfloat16)
            .reshape(EXPERTS * SPLIT, hi_slot - lo_slot, D)
        )
        sent = lax.all_to_all(outgoing, ("req", "wide"), split_axis=0, concat_axis=0, tiled=True)
        worked = expert_rows(sent, gate_pieces, up_pieces, down_pieces)
        parts.append(
            lax.all_to_all(worked, ("req", "wide"), split_axis=0, concat_axis=0, tiled=True)
        )
    weight = jnp.sum(jnp.where(match.transpose(1, 0, 2), gates[:, None, :], 0.0), axis=-1)
    weight_hi = weight.astype(jnp.bfloat16)
    weight_lo = (weight - weight_hi.astype(jnp.float32)).astype(jnp.bfloat16)
    routed = jnp.zeros((rows, D), jnp.float32)
    bounds = ((0, cut), (cut, CAP))
    stacked = jnp.concatenate([weight_hi, weight_lo], axis=0).reshape(
        2 * rows, EXPERTS * SPLIT, CAP
    )
    for (lo_slot, hi_slot), part in zip(bounds, parts):
        both = jnp.dot(
            stacked[:, :, lo_slot:hi_slot].reshape(2 * rows, -1),
            part.reshape(-1, D),
            preferred_element_type=jnp.float32,
        )
        routed = routed + (both[:rows] + both[rows:])
    return ((residual + routed).astype(jnp.bfloat16), suffix_cache)


def solution(mesh):
    return jax.shard_map(
        on_device,
        mesh=mesh,
        in_specs=(
            P(("req", "wide"), None),
            P(("req", "wide"), None),
            P(),
            P(),
            P(),
            P(),
            P(),
            P(),
            P(),
            P(("req", "wide"), None, None),
            P(("req", "wide"), None, None),
            P(("req", "wide"), None, None),
            P("req", None, None),
            P("req", None, None),
            P(),
            P("req", "wide"),
            P(("req", "wide"), None),
        ),
        out_specs=(P(("req", "wide"), None), P(("req", "wide"), None)),
        check_vma=False,
    )
```
